32 devices in a mesh: dp: 8 (over z, core), mp: 4 (over y, x).
Axes of the slice: x: 2, y: 2, z: 4, core: 2. Of those that a mesh axis runs over, the one named last changes fastest.
Arguments:
- tokens: bfloat16 [16384, 1280], P(('dp', 'mp')), may hold values from -6 to 6
- cotangent: bfloat16 [16384, 1280], P(('dp', 'mp')), may hold values from -6 to 6
- lengths: int32 [16], replicated, may hold values from 256 to 1024, as said below
- dealing: int32 [16], replicated, may hold values from 0 to 15, as said below
- gain_one: bfloat16 [1280], P('mp'), may hold values from 0.5 to 1.5
- gain_two: bfloat16 [1280], P('mp'), may hold values from 0.5 to 1.5
- attention_in: bfloat16 [1280, 3, 1280], P('mp'), may hold values from -0.15625 to 0.15625
- query_scale: float32 [80], replicated, may hold values from 0 to 1.5
- attention_out: bfloat16 [1280, 1280], P('mp'), may hold values from -1.25 to 1.25
- hidden_in: bfloat16 [1280, 1280], P('mp'), may hold values from -0.15625 to 0.15625
- hidden_out: bfloat16 [1280, 1280], P('mp'), may hold values from -0.3125 to 0.3125
Outputs:
- layer_out: bfloat16 [16384, 1280], P(('dp', 'mp'))
- tokens_grad: float32 [16384, 1280], P(('dp', 'mp'))
- series_cache: bfloat16 [2, 16384, 1280], P(None, 'dp', 'mp')
- gain_one_grad: float32 [1280], P('mp')
- gain_two_grad: float32 [1280], P('mp')
- attention_in_grad: float32 [1280, 3, 1280], P('mp')
- query_scale_grad: float32 [80], replicated
- attention_out_grad: float32 [1280, 1280], P('mp')
- hidden_in_grad: float32 [1280, 1280], P('mp')
- hidden_out_grad: float32 [1280, 1280], P('mp')
The draws below stay inside these ranges and needn't reach their ends.
Inputs may be any that keep to these rules, and one draw needn't show every extreme that they name: `lengths`: series s belongs to group s // 2; every group has a series of exactly 1024 tokens. A permutation of the 16 places: series s goes to group dealing[s] // 2 at place dealing[s] % 2. The series of one group go to one group at most 1 at a time, and in every draw some group sends exactly 1 series to some group.
All inputs are finite; a program needn't handle non-finite values.
Results may differ from the reference program's by a relative error of at most 0.02.
Values may be sent and summed in bfloat16 or wider, within the bound.
No kernel may reach another device: no remote copies, remote signals or barrier semaphores. Data moves between devices by JAX's collectives and lax.ppermute only.
A program may use at most 256 MiB of HBM per device.

```python
import math
import jax
import jax.numpy as jnp
from jax import lax

D = 1280
NH = 16
HD = 80
FF = 1280
LMAX = 1024
LMIN = 256
BLK = 128
GROUP_ROWS = 2048
SER_GRP = 2
NSER = 16
TOKENS = 16384


def draw_lengths(key, part):
    groups = NSER // SER_GRP
    first_key, second_key = jax.random.split(jax.random.fold_in(key, 17))
    spans = jax.random.randint(first_key, (groups, SER_GRP), LMIN, LMAX + 1, dtype=jnp.int32)
    longest = jax.random.randint(second_key, (groups, 1), 0, SER_GRP, dtype=jnp.int32)
    places = jnp.arange(SER_GRP, dtype=jnp.int32)[None, :]
    return jnp.where(places == longest, LMAX, spans).reshape(NSER).astype(jnp.int32)


def draw_dealing(key, part):
    groups = NSER // SER_GRP
    first_key, second_key, third_key = jax.random.split(jax.random.fold_in(key, 29), 3)
    shuffle = jax.random.permutation(first_key, groups).astype(jnp.int32)
    shifts = jax.random.permutation(second_key, groups).astype(jnp.int32)
    turns = jax.random.randint(third_key, (groups,), 0, SER_GRP, dtype=jnp.int32)
    source = jnp.arange(groups, dtype=jnp.int32)[:, None]
    places = jnp.arange(SER_GRP, dtype=jnp.int32)[None, :]
    target = (shuffle[source] + shifts[places % groups]) % groups
    seat = (places + turns[target]) % SER_GRP
    return (target * SER_GRP + seat).reshape(NSER).astype(jnp.int32)


def block_scale(stream_key, shape, cuts, smallest, high):
    loudness = 1.0
    for dim, shards_of in cuts:
        heights = jax.random.uniform(jax.random.fold_in(jax.random.fold_in(stream_key, 6), dim), (shards_of,), jnp.float32, smallest / len(cuts), high / len(cuts))
        loudness = loudness * jnp.repeat(jnp.exp(heights), shape[dim] // shards_of).reshape((-1,) + (1,) * (len(shape) - 1 - dim))
    return loudness


def centred(key, extent, width, most, pieces=(), kind=jnp.bfloat16):
    entries = jax.random.normal(key, extent, jnp.float32) * width
    if len(pieces) > 0:
        entries = block_scale(key, extent, pieces, -0.22, 0.18) * entries
    return jnp.clip(entries, min=-most, max=most).astype(kind)


def setup_inputs(seed: int = 0) -> dict:
    key_list = jax.random.split(jax.random.key(seed), 12)
    return {
        "tokens": centred(key_list[0], (TOKENS, D), 1.0, 6.0, ((0, 32),)),
        "cotangent": centred(key_list[1], (TOKENS, D), 1.0, 6.0, ((0, 32),)),
        "lengths": draw_lengths(jax.random.fold_in(key_list[11], 71), 0),
        "dealing": draw_dealing(jax.random.fold_in(key_list[11], 71), 0),
        "gain_one": jnp.clip(1.0 + 0.1 * jax.random.normal(key_list[4], (D,), jnp.float32), 0.5, 1.5).astype(jnp.bfloat16),
        "gain_two": jnp.clip(1.0 + 0.1 * jax.random.normal(key_list[5], (D,), jnp.float32), 0.5, 1.5).astype(jnp.bfloat16),
        "attention_in": centred(key_list[6], (D, 3, D), D ** -0.5, 0.15625, ((0, 4),)),
        "query_scale": jnp.clip(jax.random.uniform(key_list[7], (HD,), jnp.float32, 0.0, 1.5), 0.0, 1.5),
        "attention_out": centred(key_list[8], (D, D), (D // 64) ** -0.5, 1.25, ((0, 4),)),
        "hidden_in": centred(key_list[9], (FF, D), D ** -0.5, 0.15625, ((0, 4),)),
        "hidden_out": centred(key_list[10], (FF, D), (FF // 4) ** -0.5, 0.3125, ((0, 4),)),
    }


epsilon = 1e-06
scale_base = 1.442695041
masked_score = -1e+30
highest = lax.Precision.HIGHEST

@jax.custom_vjp
def low(v):
    return lax.optimization_barrier(v.astype(jnp.bfloat16)).astype(jnp.float32)

@jax.custom_vjp
def low_back(v):
    return v

def low_keep(v):
    return (low(v), None)

def low_pass(kept, grad):
    return (grad,)

def back_keep(v):
    return (v, None)

def back_low(kept, grad):
    return (low(grad),)
low.defvjp(low_keep, low_pass)
low_back.defvjp(back_keep, back_low)

def rms_scale(operand):
    return lax.rsqrt(lax.optimization_barrier(jnp.mean(operand * operand, axis=-1, keepdims=True)) + epsilon)

def packing(span_len):
    blocks = (span_len + BLK - 1) // BLK
    block_ends = (BLK * jnp.cumsum(blocks, axis=1)).astype(jnp.int32)
    starts = (block_ends - BLK * blocks).astype(jnp.int32)
    in_group = jnp.arange(GROUP_ROWS, dtype=jnp.int32)
    series_at = lax.optimization_barrier(jnp.sum((block_ends[:, None, :] <= in_group[None, :, None]).astype(jnp.int32), axis=2)).astype(jnp.int32)
    capped = jnp.minimum(series_at, SER_GRP - 1).astype(jnp.int32)
    offset = (in_group[None, :] - jnp.take_along_axis(starts, capped, axis=1)).astype(jnp.int32)
    live_row = (series_at < SER_GRP) & (offset < jnp.take_along_axis(span_len, capped, axis=1))
    return (starts, capped, offset, live_row)

def one_series(item):
    block, span_count = item
    positions = jnp.arange(LMAX, dtype=jnp.int32)
    queries = block[0].reshape(LMAX, NH, HD)
    keys = block[1].reshape(LMAX, NH, HD)
    values = block[2].reshape(LMAX, NH, HD)
    allowed = (positions[None, :] <= positions[:, None]) & (positions[None, :] < span_count)
    scores = low_back(jnp.einsum('qhd,khd->hqk', queries, keys, precision=highest))
    scores = jnp.where(allowed[None], scores, masked_score)
    row_max = lax.optimization_barrier(jnp.max(scores, axis=-1, keepdims=True))
    exponent = jnp.exp(scores - row_max)
    soft_weights = exponent / lax.optimization_barrier(jnp.sum(exponent, axis=-1, keepdims=True))
    mixed = jnp.einsum('hqk,khd->qhd', low(soft_weights), values, precision=highest)
    return mixed.reshape(LMAX, D)

def reference(tokens, cotangent, lengths, dealing, gain_one, gain_two, attention_in, query_scale, attention_out, hidden_in, hidden_out):
    groups = NSER // SER_GRP
    span_len = lengths.reshape(groups, SER_GRP)
    starts, capped, offset, live_row = packing(span_len)
    group_ids = jnp.arange(groups, dtype=jnp.int32)
    series_of_row = (group_ids[:, None] * SER_GRP + capped).reshape(-1)
    live_tokens = live_row.reshape(-1)
    back_index = jnp.clip(series_of_row * LMAX + offset.reshape(-1), 0, NSER * LMAX - 1).astype(jnp.int32)
    first_row = (group_ids[:, None] * GROUP_ROWS + starts).reshape(-1).astype(jnp.int32)
    positions = jnp.arange(LMAX, dtype=jnp.int32)
    series_rows = jnp.clip(first_row[:, None] + positions[None, :], 0, TOKENS - 1).reshape(-1).astype(jnp.int32)
    series_live = (positions[None, :] < lengths[:, None]).reshape(-1).astype(jnp.float32)
    keep_mask = live_tokens.astype(jnp.float32)[:, None]

    def forward(inputs, gains_one, gains_two, qkv_weight, scale_param, out_weight, in_weight, down_weight):
        normed_one = low(inputs * rms_scale(inputs) * gains_one)
        projected = jnp.einsum('rd,ucd->cru', normed_one, qkv_weight, precision=highest)
        query_raw = low_back(projected[0])
        dim_scale = scale_base / math.sqrt(HD) * jax.nn.softplus(scale_param)
        queries = low_back(low((query_raw.reshape(-1, NH, HD) * dim_scale).reshape(-1, D)))
        keys = low_back(low(projected[1]))
        values = low_back(low(projected[2]))
        stacked = jnp.stack([queries, keys, values])
        per_series = jnp.take(stacked, series_rows, axis=1) * series_live[None, :, None]
        per_series = jnp.transpose(per_series.reshape(3, NSER, LMAX, D), (1, 0, 2, 3))
        mixed = lax.map(jax.checkpoint(one_series), (per_series, lengths))
        attended = jnp.take(mixed.reshape(NSER * LMAX, D), back_index, axis=0) * keep_mask
        attended = low_back(low(attended))
        branch = low_back(jnp.dot(attended, out_weight, precision=highest))
        first_sum = inputs + branch
        normed_two = low(first_sum * rms_scale(first_sum) * gains_two)
        preact = low_back(jnp.einsum('rd,fd->rf', normed_two, in_weight, precision=highest))
        hidden = low(jax.nn.silu(preact))
        feed = low_back(jnp.dot(hidden, down_weight, precision=highest))
        return ((first_sum + feed) * keep_mask, (keys, values))
    primals = (tokens.astype(jnp.float32), gain_one.astype(jnp.float32), gain_two.astype(jnp.float32), attention_in.astype(jnp.float32), query_scale.astype(jnp.float32), attention_out.astype(jnp.float32), hidden_in.astype(jnp.float32), hidden_out.astype(jnp.float32))
    layer, pullback, kept = jax.vjp(forward, *primals, has_aux=True)
    grads = pullback(cotangent.astype(jnp.float32))
    keys, values = kept
    inverse = jnp.argsort(dealing).astype(jnp.int32)
    dealt_len = jnp.take(lengths, inverse).reshape(groups, SER_GRP)
    dealt_starts, dealt_capped, dealt_offset, dealt_live = packing(dealt_len)
    dealt_series = jnp.take_along_axis(inverse.reshape(groups, SER_GRP), dealt_capped, axis=1).reshape(-1)
    source_rows = jnp.clip(jnp.take(first_row, dealt_series) + dealt_offset.reshape(-1), 0, TOKENS - 1).astype(jnp.int32)
    dealt_mask = dealt_live.reshape(-1).astype(jnp.float32)[:, None]
    cache = jnp.stack([jnp.take(keys, source_rows, axis=0) * dealt_mask, jnp.take(values, source_rows, axis=0) * dealt_mask]).astype(jnp.bfloat16)
    return (layer.astype(jnp.bfloat16), grads[0], cache, grads[1], grads[2], grads[3], grads[4], grads[5], grads[6], grads[7])
```

```python
import math

import jax
import jax.numpy as jnp
from jax import lax
from jax.sharding import PartitionSpec as P

D = 1280
NH = 16
HD = 80
LMAX = 1024
BLK = 128
QBLK = 512


epsilon = 1e-06
scale_base = 1.442695041
masked_score = -1e30


def lookup(values_table, positions):
    entries = jnp.arange(values_table.shape[0], dtype=jnp.int32)
    picked = jnp.where(positions[:, None] == entries[None, :], values_table[None, :], 0)
    return jnp.sum(picked, axis=1)


def packing(span_len, group_rows):
    blocks = (span_len + BLK - 1) // BLK
    block_ends = BLK * jnp.cumsum(blocks)
    starts = block_ends - BLK * blocks
    in_group = jnp.arange(group_rows, dtype=jnp.int32)
    series_at = jnp.sum((block_ends[None, :] <= in_group[:, None]).astype(jnp.int32), axis=1)
    capped = jnp.minimum(series_at, span_len.shape[0] - 1)
    offset = in_group - lookup(starts, capped)
    live_row = (series_at < span_len.shape[0]) & (offset < lookup(span_len, capped))
    return (starts, series_at, capped, offset, live_row)


def slot_table(slot_of, starts, span_len, slot_count):
    entries = jnp.arange(slot_count, dtype=jnp.int32)
    matched = slot_of[None, :] == entries[:, None]
    slot_first = jnp.sum(jnp.where(matched, starts[None, :], 0), axis=1)
    slot_length = jnp.sum(jnp.where(matched, span_len[None, :], 0), axis=1)
    return (slot_first, slot_length)


def series_maps(lengths, dealing, series_grp, group_rows, my_group):
    groups = lengths.shape[0] // series_grp
    capacity = (series_grp + groups - 1) // groups
    places = jnp.arange(series_grp, dtype=jnp.int32)
    target = dealing.reshape(groups, series_grp) // series_grp
    earlier = (target[:, :, None] == target[:, None, :]) & (
        places[None, None, :] < places[None, :, None]
    )
    rank_of = jnp.sum(earlier.astype(jnp.int32), axis=2)
    slot_of = (target * capacity + rank_of).reshape(-1)
    rank_flat = rank_of.reshape(-1)
    src_len = lax.dynamic_slice_in_dim(lengths, my_group * series_grp, series_grp)
    src_slot = lax.dynamic_slice_in_dim(slot_of, my_group * series_grp, series_grp)
    src_starts, src_at, src_capped, src_offset, src_live = packing(src_len, group_rows)
    dealt_places = jnp.arange(lengths.shape[0], dtype=jnp.int32)
    owner = jnp.sum(
        jnp.where(dealing[None, :] == dealt_places[:, None], dealt_places[None, :], 0), axis=1
    )
    my_series = lax.dynamic_slice_in_dim(owner, my_group * series_grp, series_grp)
    dst_len = lookup(lengths, my_series)
    dst_slot = my_series // series_grp * capacity + lookup(rank_flat, my_series)
    dst_starts, dst_at, dst_capped, dst_offset, dst_live = packing(dst_len, group_rows)
    slot_count = groups * capacity
    send_first, send_len = slot_table(src_slot, src_starts, src_len, slot_count)
    back_first, back_len = slot_table(dst_slot, dst_starts, dst_len, slot_count)
    src_index = lookup(src_slot, src_capped) * LMAX + src_offset
    dst_index = lookup(dst_slot, dst_capped) * LMAX + dst_offset
    key_live = jnp.where(dst_at < series_grp, dst_live, True)
    return (
        send_first,
        send_len,
        back_first,
        back_len,
        src_index,
        src_live,
        dst_index,
        dst_live,
        dst_at,
        key_live,
    )


def fill_slots(values, slot_first, slot_length):
    positions = jnp.arange(LMAX, dtype=jnp.int32)
    row_index = jnp.clip(slot_first[:, None] + positions[None, :], 0, values.shape[1] - 1).reshape(
        -1
    )
    inside = (positions[None, :] < slot_length[:, None]).reshape(-1)
    picked = jnp.take(values, row_index, axis=1)
    picked = jnp.where(inside[None, :, None], picked, jnp.zeros((), values.dtype))
    return picked.reshape(values.shape[0], slot_first.shape[0], LMAX, values.shape[2])


def place_rows(slots_in, row_index, live_row):
    flattened = slots_in.reshape(slots_in.shape[0], -1, slots_in.shape[3])
    picked = jnp.take(flattened, jnp.clip(row_index, 0, flattened.shape[1] - 1), axis=1)
    return jnp.where(live_row[None, :, None], picked, jnp.zeros((), flattened.dtype))


def unit_terms(unit_sides, other_sides):
    qkv_grad, att_rows, preact_grad, hidden = unit_sides
    normed_one, branch_grad, normed_two, feed_grad = other_sides
    qkv_part = jnp.einsum("cru,rd->ucd", qkv_grad, normed_one, preferred_element_type=jnp.float32)
    out_part = jnp.einsum("ru,rd->ud", att_rows, branch_grad, preferred_element_type=jnp.float32)
    in_part = jnp.einsum("ru,rd->ud", preact_grad, normed_two, preferred_element_type=jnp.float32)
    down_part = jnp.einsum("ru,rd->ud", hidden, feed_grad, preferred_element_type=jnp.float32)
    return jnp.concatenate(
        [qkv_part, out_part[:, None], in_part[:, None], down_part[:, None]], axis=1
    )


def per_device(
    tokens,
    cotangent,
    lengths,
    dealing,
    gain_one,
    gain_two,
    attention_in,
    query_scale,
    attention_out,
    hidden_in,
    hidden_out,
):
    gains_one, gains_two, out_all, in_all, down_all = (
        lax.all_gather(gain_one, "mp", axis=0, tiled=True),
        lax.all_gather(gain_two, "mp", axis=0, tiled=True),
        lax.all_gather(attention_out, "mp", axis=0, tiled=True),
        lax.all_gather(hidden_in, "mp", axis=0, tiled=True),
        lax.all_gather(hidden_out, "mp", axis=0, tiled=True),
    )
    row_count = tokens.shape[0]
    mp_count = lax.axis_size("mp")
    my_group = lax.axis_index("dp")
    my_part = lax.axis_index("mp")
    group_rows = row_count * mp_count
    series_grp = group_rows // LMAX
    heads_here = NH // mp_count
    width_here = heads_here * HD
    (
        send_first,
        send_len,
        back_first,
        back_len,
        src_index,
        src_live,
        dst_index,
        dst_live,
        dst_at,
        dst_key_live,
    ) = series_maps(lengths, dealing, series_grp, group_rows, my_group)
    src_len = lax.dynamic_slice_in_dim(lengths, my_group * series_grp, series_grp)
    _, segment, _, _, _ = packing(src_len, group_rows)
    key_live = jnp.where(segment < series_grp, src_live, True)
    group_live = src_live.astype(jnp.float32)[:, None]
    live_mine = lax.dynamic_slice_in_dim(src_live, my_part * row_count, row_count).astype(
        jnp.float32
    )[:, None]
    inputs = tokens.astype(jnp.float32)
    inv_one = lax.rsqrt(jnp.mean(inputs * inputs, axis=1, keepdims=True) + epsilon)
    gain_first = gains_one.astype(jnp.float32)
    normed_one = (inputs * inv_one * gain_first).astype(jnp.bfloat16)
    normed_group = lax.all_gather(normed_one, "mp", axis=0, tiled=True)
    projected = jnp.einsum(
        "rd,ucd->cru", normed_group, attention_in, preferred_element_type=jnp.float32
    )
    dim_scale = scale_base / math.sqrt(HD) * jax.nn.softplus(query_scale)
    query_raw = projected[0].reshape(group_rows, heads_here, HD)
    queries = (query_raw * dim_scale).astype(jnp.bfloat16)
    keys_group = projected[1].astype(jnp.bfloat16)
    values_group = projected[2].astype(jnp.bfloat16)
    kv_group = jnp.stack([keys_group, values_group])
    incoming = lax.all_to_all(
        fill_slots(kv_group, send_first, send_len), "dp", split_axis=1, concat_axis=1, tiled=True
    )
    cache = place_rows(incoming, dst_index, dst_live)
    margin = LMAX - BLK
    window = margin + QBLK
    keys_pad = jnp.pad(keys_group, ((margin, 0), (0, 0))).reshape(
        group_rows + margin, heads_here, HD
    )
    values_pad = jnp.pad(values_group, ((margin, 0), (0, 0))).reshape(
        group_rows + margin, heads_here, HD
    )
    segment_pad = jnp.concatenate([jnp.full((margin,), -1, jnp.int32), segment])
    live_pad = jnp.concatenate([jnp.zeros((margin,), jnp.bool_), key_live])
    block_starts = jnp.arange(group_rows // QBLK, dtype=jnp.int32) * QBLK
    query_pos = jnp.arange(QBLK, dtype=jnp.int32)
    key_pos = jnp.arange(window, dtype=jnp.int32) - margin

    def block_scores(block_start):
        query_block = lax.dynamic_slice_in_dim(queries, block_start, QBLK, 0)
        key_window = lax.dynamic_slice_in_dim(keys_pad, block_start, window, 0)
        value_window = lax.dynamic_slice_in_dim(values_pad, block_start, window, 0)
        seg_query = lax.dynamic_slice_in_dim(segment, block_start, QBLK, 0)
        seg_key = lax.dynamic_slice_in_dim(segment_pad, block_start, window, 0)
        live_key = lax.dynamic_slice_in_dim(live_pad, block_start, window, 0)
        allowed = (
            (seg_query[:, None] == seg_key[None, :])
            & (key_pos[None, :] <= query_pos[:, None])
            & live_key[None, :]
        )
        scores = jnp.einsum(
            "qhd,khd->hqk", query_block, key_window, preferred_element_type=jnp.float32
        )
        return (
            query_block,
            key_window,
            value_window,
            jnp.where(allowed[None], scores, masked_score),
        )

    def forward_block(carry, block_start):
        query_block, key_window, value_window, scores = block_scores(block_start)
        row_max = jnp.max(scores, axis=2, keepdims=True)
        exponent = jnp.exp(scores - row_max)
        row_total = jnp.sum(exponent, axis=2, keepdims=True)
        soft_weights = (exponent / row_total).astype(jnp.bfloat16)
        mixed = jnp.einsum(
            "hqk,khd->qhd", soft_weights, value_window, preferred_element_type=jnp.float32
        )
        log_total = (row_max + jnp.log(row_total))[:, :, 0]
        return (carry, (mixed.astype(jnp.bfloat16).reshape(QBLK, width_here), log_total))

    _, (mixed_blocks, log_totals) = lax.scan(forward_block, jnp.int32(0), block_starts)
    att_group = jnp.where(
        src_live[:, None], mixed_blocks.reshape(group_rows, width_here), jnp.zeros((), jnp.bfloat16)
    )
    att_rows = lax.all_to_all(att_group, "mp", split_axis=0, concat_axis=1, tiled=True)
    branch = jnp.dot(att_rows, out_all, preferred_element_type=jnp.float32)
    first_sum = inputs + branch
    inv_two = lax.rsqrt(jnp.mean(first_sum * first_sum, axis=1, keepdims=True) + epsilon)
    gain_second = gains_two.astype(jnp.float32)
    normed_two = (first_sum * inv_two * gain_second).astype(jnp.bfloat16)
    preact = jnp.einsum("rd,fd->rf", normed_two, in_all, preferred_element_type=jnp.float32)
    hidden = jax.nn.silu(preact).astype(jnp.bfloat16)
    feed = jnp.dot(hidden, down_all, preferred_element_type=jnp.float32)
    layer_out = ((first_sum + feed) * live_mine).astype(jnp.bfloat16)
    out_grad = cotangent.astype(jnp.float32) * live_mine
    feed_grad = out_grad.astype(jnp.bfloat16)
    hidden_grad = jnp.einsum("rd,fd->rf", feed_grad, down_all, preferred_element_type=jnp.float32)
    gate_sig = jax.nn.sigmoid(preact)
    preact_grad = (hidden_grad * gate_sig * (1.0 + preact * (1.0 - gate_sig))).astype(jnp.bfloat16)
    normed_two_grad = jnp.dot(preact_grad, in_all, preferred_element_type=jnp.float32)
    scaled_two = gain_second * normed_two_grad
    first_grad = (
        out_grad
        + inv_two * scaled_two
        - first_sum * inv_two**3 * jnp.mean(scaled_two * first_sum, axis=1, keepdims=True)
    )
    branch_grad = first_grad.astype(jnp.bfloat16)
    att_rows_grad = jnp.einsum(
        "rd,ud->ru", branch_grad, out_all, preferred_element_type=jnp.float32
    ).astype(jnp.bfloat16)
    grad_group = lax.all_to_all(att_rows_grad, "mp", split_axis=1, concat_axis=0, tiled=True)
    grad_dealt = jnp.where(src_live[:, None], grad_group, jnp.zeros((), jnp.bfloat16)).reshape(
        group_rows, heads_here, HD
    )

    def backward_block(carry, item):
        block_start, log_total = item
        key_grads, value_grads = carry
        query_block, key_window, value_window, scores = block_scores(block_start)
        probs_full = jnp.exp(scores - log_total[:, :, None])
        grad_block = lax.dynamic_slice_in_dim(grad_dealt, block_start, QBLK, 0)
        weight_grad = jnp.einsum(
            "qhd,khd->hqk", grad_block, value_window, preferred_element_type=jnp.float32
        )
        row_dot = jnp.sum(probs_full * weight_grad, axis=2, keepdims=True)
        score_grad = (probs_full * (weight_grad - row_dot)).astype(jnp.bfloat16)
        query_grad = jnp.einsum(
            "hqk,khd->qhd", score_grad, key_window, preferred_element_type=jnp.float32
        )
        key_part = jnp.einsum(
            "hqk,qhd->khd", score_grad, query_block, preferred_element_type=jnp.float32
        )
        value_part = jnp.einsum(
            "hqk,qhd->khd",
            probs_full.astype(jnp.bfloat16),
            grad_block,
            preferred_element_type=jnp.float32,
        )
        key_grads = lax.dynamic_update_slice_in_dim(
            key_grads,
            lax.dynamic_slice_in_dim(key_grads, block_start, window, 0) + key_part,
            block_start,
            0,
        )
        value_grads = lax.dynamic_update_slice_in_dim(
            value_grads,
            lax.dynamic_slice_in_dim(value_grads, block_start, window, 0) + value_part,
            block_start,
            0,
        )
        return ((key_grads, value_grads), query_grad.reshape(QBLK, heads_here, HD))

    empty = jnp.zeros((group_rows + margin, heads_here, HD), jnp.float32)
    (key_grads, value_grads), query_blocks = lax.scan(
        backward_block, (empty, empty), (block_starts, log_totals)
    )
    query_scaled_grad = query_blocks.reshape(group_rows, heads_here, HD).astype(jnp.bfloat16)
    query_scaled_grad = jnp.where(
        src_live[:, None, None], query_scaled_grad, jnp.zeros((), jnp.bfloat16)
    ).astype(jnp.float32)
    scale_part = (
        jnp.sum(query_scaled_grad * query_raw, axis=(0, 1))
        * (scale_base / math.sqrt(HD))
        * jax.nn.sigmoid(query_scale)
    )
    query_grad_group = (query_scaled_grad * dim_scale).reshape(group_rows, width_here)
    key_grad_group = key_grads[margin:].reshape(group_rows, width_here).astype(jnp.bfloat16)
    value_grad_group = value_grads[margin:].reshape(group_rows, width_here).astype(jnp.bfloat16)
    proj_grad = jnp.stack(
        [
            query_grad_group.astype(jnp.bfloat16),
            jnp.where(src_live[:, None], key_grad_group, jnp.zeros((), jnp.bfloat16)),
            jnp.where(src_live[:, None], value_grad_group, jnp.zeros((), jnp.bfloat16)),
        ]
    )
    qkv_part = jnp.einsum(
        "cru,rd->ucd", proj_grad, normed_group, preferred_element_type=jnp.float32
    )
    normed_one_part = jnp.einsum(
        "cru,ucd->rd", proj_grad, attention_in, preferred_element_type=jnp.float32
    )
    normed_one_grad = lax.psum_scatter(
        normed_one_part.astype(jnp.bfloat16), "mp", scatter_dimension=0, tiled=True
    ).astype(jnp.float32)
    scaled_one = gain_first * normed_one_grad
    tokens_grad = (
        first_grad
        + inv_one * scaled_one
        - inputs * inv_one**3 * jnp.mean(scaled_one * inputs, axis=1, keepdims=True)
    )
    gain_one_part = jnp.sum(normed_one_grad * inputs * inv_one, axis=0)
    gain_two_part = jnp.sum(normed_two_grad * first_sum * inv_two, axis=0)
    gain_one_sum, gain_two_sum, query_scale_grad = lax.psum(
        (gain_one_part, gain_two_part, scale_part), ("dp", "mp")
    )
    shard_width = D // mp_count
    gain_one_grad = lax.dynamic_slice_in_dim(gain_one_sum, my_part * shard_width, shard_width)
    gain_two_grad = lax.dynamic_slice_in_dim(gain_two_sum, my_part * shard_width, shard_width)
    out_part = jnp.einsum("ru,rd->ud", att_rows, branch_grad, preferred_element_type=jnp.float32)
    in_part = jnp.einsum("ru,rd->ud", preact_grad, normed_two, preferred_element_type=jnp.float32)
    down_part = jnp.einsum("ru,rd->ud", hidden, feed_grad, preferred_element_type=jnp.float32)
    row_terms = jnp.stack([out_part, in_part, down_part], axis=1)
    shares = lax.psum_scatter(
        row_terms.astype(jnp.bfloat16), "mp", scatter_dimension=0, tiled=True
    )
    totals = lax.psum(
        jnp.concatenate([qkv_part.astype(jnp.bfloat16), shares], axis=1), "dp"
    ).astype(jnp.float32)
    return (
        layer_out,
        tokens_grad,
        cache,
        gain_one_grad,
        gain_two_grad,
        totals[:, 0:3],
        query_scale_grad,
        totals[:, 3],
        totals[:, 4],
        totals[:, 5],
    )


def solution(mesh):
    placed = (
        P(("dp", "mp"), None),
        P(("dp", "mp"), None),
        P(),
        P(),
        P("mp"),
        P("mp"),
        P("mp", None, None),
        P(),
        P("mp", None),
        P("mp", None),
        P("mp", None),
    )
    return jax.shard_map(
        per_device,
        mesh=mesh,
        in_specs=placed,
        out_specs=(
            P(("dp", "mp"), None),
            P(("dp", "mp"), None),
            P(None, "dp", "mp"),
            P("mp"),
            P("mp"),
            P("mp", None, None),
            P(),
            P("mp", None),
            P("mp", None),
            P("mp", None),
        ),
        check_vma=False,
    )
```

```python
import math

import jax
import jax.numpy as jnp
from jax import lax
from jax.experimental import pallas as pl
from jax.experimental.pallas import tpu as pltpu
from jax.sharding import PartitionSpec as P

D = 1280
NH = 16
HD = 80
LMAX = 1024
BLK = 128
TQ = 128


epsilon = 1e-06
scale_base = 1.442695041
masked_score = -1e30


def lookup(values_table, positions):
    entries = jnp.arange(values_table.shape[0], dtype=jnp.int32)
    picked = jnp.where(positions[:, None] == entries[None, :], values_table[None, :], 0)
    return jnp.sum(picked, axis=1)


def packing(span_len, group_rows):
    blocks = (span_len + BLK - 1) // BLK
    block_ends = BLK * jnp.cumsum(blocks)
    starts = block_ends - BLK * blocks
    in_group = jnp.arange(group_rows, dtype=jnp.int32)
    series_at = jnp.sum((block_ends[None, :] <= in_group[:, None]).astype(jnp.int32), axis=1)
    capped = jnp.minimum(series_at, span_len.shape[0] - 1)
    offset = in_group - lookup(starts, capped)
    live_row = (series_at < span_len.shape[0]) & (offset < lookup(span_len, capped))
    return (starts, series_at, capped, offset, live_row)


def slot_table(slot_of, starts, span_len, slot_count):
    entries = jnp.arange(slot_count, dtype=jnp.int32)
    matched = slot_of[None, :] == entries[:, None]
    slot_first = jnp.sum(jnp.where(matched, starts[None, :], 0), axis=1)
    slot_length = jnp.sum(jnp.where(matched, span_len[None, :], 0), axis=1)
    return (slot_first, slot_length)


def series_maps(lengths, dealing, series_grp, group_rows, my_group):
    groups = lengths.shape[0] // series_grp
    capacity = (series_grp + groups - 1) // groups
    places = jnp.arange(series_grp, dtype=jnp.int32)
    target = dealing.reshape(groups, series_grp) // series_grp
    earlier = (target[:, :, None] == target[:, None, :]) & (
        places[None, None, :] < places[None, :, None]
    )
    rank_of = jnp.sum(earlier.astype(jnp.int32), axis=2)
    slot_of = (target * capacity + rank_of).reshape(-1)
    rank_flat = rank_of.reshape(-1)
    src_len = lax.dynamic_slice_in_dim(lengths, my_group * series_grp, series_grp)
    src_slot = lax.dynamic_slice_in_dim(slot_of, my_group * series_grp, series_grp)
    src_starts, src_at, src_capped, src_offset, src_live = packing(src_len, group_rows)
    dealt_places = jnp.arange(lengths.shape[0], dtype=jnp.int32)
    owner = jnp.sum(
        jnp.where(dealing[None, :] == dealt_places[:, None], dealt_places[None, :], 0), axis=1
    )
    my_series = lax.dynamic_slice_in_dim(owner, my_group * series_grp, series_grp)
    dst_len = lookup(lengths, my_series)
    dst_slot = my_series // series_grp * capacity + lookup(rank_flat, my_series)
    dst_starts, dst_at, dst_capped, dst_offset, dst_live = packing(dst_len, group_rows)
    slot_count = groups * capacity
    send_first, send_len = slot_table(src_slot, src_starts, src_len, slot_count)
    back_first, back_len = slot_table(dst_slot, dst_starts, dst_len, slot_count)
    src_index = lookup(src_slot, src_capped) * LMAX + src_offset
    dst_index = lookup(dst_slot, dst_capped) * LMAX + dst_offset
    key_live = jnp.where(dst_at < series_grp, dst_live, True)
    return (
        send_first,
        send_len,
        back_first,
        back_len,
        src_index,
        src_live,
        dst_index,
        dst_live,
        dst_at,
        key_live,
    )


def fill_slots(values, slot_first, slot_length):
    padded = jnp.pad(values, ((0, 0), (0, LMAX), (0, 0)))
    positions = jnp.arange(LMAX, dtype=jnp.int32)[None, :, None]
    slots = []
    for g in range(slot_first.shape[0]):
        window = lax.dynamic_slice_in_dim(padded, slot_first[g], LMAX, axis=1)
        slots.append(jnp.where(positions < slot_length[g], window, jnp.zeros((), values.dtype)))
    return jnp.stack(slots, axis=1)


def place_slots(incoming, place_slot, place_start, place_len, out_rows):
    positions = jnp.arange(LMAX, dtype=jnp.int32)[None, :, None]
    placed = jnp.zeros((incoming.shape[0], out_rows + LMAX, incoming.shape[3]), incoming.dtype)
    for q in range(place_slot.shape[0]):
        window = lax.dynamic_index_in_dim(incoming, place_slot[q], axis=1, keepdims=False)
        window = jnp.where(positions < place_len[q], window, jnp.zeros((), incoming.dtype))
        placed = lax.dynamic_update_slice_in_dim(placed, window, place_start[q], axis=1)
    return placed[:, :out_rows]


def dealt_places(lengths, dealing, series_grp, my_group):
    groups = lengths.shape[0] // series_grp
    dealt_places = jnp.arange(lengths.shape[0], dtype=jnp.int32)
    owner = jnp.sum(
        jnp.where(dealing[None, :] == dealt_places[:, None], dealt_places[None, :], 0), axis=1
    )
    my_series = lax.dynamic_slice_in_dim(owner, my_group * series_grp, series_grp)
    place_len = lookup(lengths, my_series)
    blocks = (place_len + BLK - 1) // BLK
    place_start = BLK * jnp.cumsum(blocks) - BLK * blocks
    return my_series // series_grp, place_start, place_len


def block_bounds(src_len, group_rows):
    starts, series_at, capped, offset, live_row = packing(src_len, group_rows)
    first_rows = jnp.arange(group_rows // TQ, dtype=jnp.int32) * TQ
    seg = series_at[first_rows]
    inside = seg < src_len.shape[0]
    seg_c = jnp.minimum(seg, src_len.shape[0] - 1)
    block_start = jnp.where(inside, lookup(starts, seg_c), 0)
    block_end = jnp.where(inside, block_start + lookup(src_len, seg_c), 0)
    return block_start.astype(jnp.int32), block_end.astype(jnp.int32), live_row


def _window(i, rows):
    qs = i * TQ
    ws = jnp.minimum(jnp.maximum(qs - (LMAX - TQ), 0), rows - LMAX)
    return qs, pl.multiple_of(ws, TQ)


def _allowed(qs, ws, s0, e0):
    a = qs + lax.broadcasted_iota(jnp.int32, (TQ, LMAX), 0)
    b = ws + lax.broadcasted_iota(jnp.int32, (TQ, LMAX), 1)
    return (b >= s0) & (b <= a) & (b < e0)


def attn_fwd_kernel(starts_ref, ends_ref, q_ref, k_ref, v_ref, o_ref, lse_ref):
    i = pl.program_id(0)
    heads, rows = k_ref.shape[0], k_ref.shape[1]
    qs, ws = _window(i, rows)
    s0 = starts_ref[i]
    e0 = ends_ref[i]

    @pl.when(s0 < e0)
    def _():
        allowed = _allowed(qs, ws, s0, e0)
        for h in range(heads):
            q = q_ref[h]
            k = k_ref[h, pl.ds(ws, LMAX), :]
            v = v_ref[h, pl.ds(ws, LMAX), :]
            s = lax.dot_general(q, k, (((1,), (1,)), ((), ())), preferred_element_type=jnp.float32)
            s = jnp.where(allowed, s, masked_score)
            m = jnp.max(s, axis=1, keepdims=True)
            p = jnp.exp(s - m)
            l = jnp.sum(p, axis=1, keepdims=True)
            probs = (p / l).astype(jnp.bfloat16)
            o = jnp.dot(probs, v, preferred_element_type=jnp.float32)
            o_ref[h] = o.astype(o_ref.dtype)
            lse_ref[h] = m + jnp.log(l)

    @pl.when(s0 >= e0)
    def _():
        o_ref[...] = jnp.zeros(o_ref.shape, o_ref.dtype)
        lse_ref[...] = jnp.zeros(lse_ref.shape, lse_ref.dtype)


def attn_bwd_kernel(starts_ref, ends_ref, q_ref, k_ref, v_ref, do_ref, lse_ref,
                    dq_ref, dk_ref, dv_ref, dk_acc, dv_acc):
    i = pl.program_id(0)
    heads, rows = k_ref.shape[0], k_ref.shape[1]
    qs, ws = _window(i, rows)
    s0 = starts_ref[i]
    e0 = ends_ref[i]

    @pl.when(i == 0)
    def _():
        dk_acc[...] = jnp.zeros(dk_acc.shape, dk_acc.dtype)
        dv_acc[...] = jnp.zeros(dv_acc.shape, dv_acc.dtype)

    @pl.when(s0 < e0)
    def _():
        allowed = _allowed(qs, ws, s0, e0)
        for h in range(heads):
            q = q_ref[h]
            k = k_ref[h, pl.ds(ws, LMAX), :]
            v = v_ref[h, pl.ds(ws, LMAX), :]
            do = do_ref[h]
            s = lax.dot_general(q, k, (((1,), (1,)), ((), ())), preferred_element_type=jnp.float32)
            s = jnp.where(allowed, s, masked_score)
            probs = jnp.exp(s - lse_ref[h])
            dp = lax.dot_general(do, v, (((1,), (1,)), ((), ())), preferred_element_type=jnp.float32)
            row_dot = jnp.sum(probs * dp, axis=1, keepdims=True)
            ds = (probs * (dp - row_dot)).astype(jnp.bfloat16)
            dq = jnp.dot(ds, k, preferred_element_type=jnp.float32)
            dq_ref[h] = dq.astype(dq_ref.dtype)
            dk_acc[h, pl.ds(ws, LMAX), :] += jnp.dot(ds.T, q, preferred_element_type=jnp.float32)
            dv_acc[h, pl.ds(ws, LMAX), :] += jnp.dot(
                probs.astype(jnp.bfloat16).T, do, preferred_element_type=jnp.float32
            )

    @pl.when(s0 >= e0)
    def _():
        dq_ref[...] = jnp.zeros(dq_ref.shape, dq_ref.dtype)

    @pl.when(i == pl.num_programs(0) - 1)
    def _():
        dk_ref[...] = dk_acc[...].astype(dk_ref.dtype)
        dv_ref[...] = dv_acc[...].astype(dv_ref.dtype)


def attention_forward(q, k, v, starts, ends):
    heads, rows, width = q.shape
    blocks = rows // TQ
    whole = pl.BlockSpec((heads, rows, width), lambda i, s, e: (0, 0, 0))
    part = pl.BlockSpec((heads, TQ, width), lambda i, s, e: (0, i, 0))
    flops = 4 * heads * rows * LMAX * width
    return pl.pallas_call(
        attn_fwd_kernel,
        grid_spec=pltpu.PrefetchScalarGridSpec(
            num_scalar_prefetch=2,
            grid=(blocks,),
            in_specs=[part, whole, whole],
            out_specs=[part, pl.BlockSpec((heads, TQ, 1), lambda i, s, e: (0, i, 0))],
        ),
        out_shape=[
            jax.ShapeDtypeStruct((heads, rows, width), jnp.bfloat16),
            jax.ShapeDtypeStruct((heads, rows, 1), jnp.float32),
        ],
        compiler_params=pltpu.CompilerParams(
            dimension_semantics=("arbitrary",), vmem_limit_bytes=48 * 1024 * 1024
        ),
        cost_estimate=pl.CostEstimate(
            flops=flops, transcendentals=heads * rows * LMAX, bytes_accessed=4 * q.size * 2
        ),
    )(starts, ends, q, k, v)


def attention_backward(q, k, v, do, lse, starts, ends):
    heads, rows, width = q.shape
    blocks = rows // TQ
    whole = pl.BlockSpec((heads, rows, width), lambda i, s, e: (0, 0, 0))
    part = pl.BlockSpec((heads, TQ, width), lambda i, s, e: (0, i, 0))
    flops = 10 * heads * rows * LMAX * width
    return pl.pallas_call(
        attn_bwd_kernel,
        grid_spec=pltpu.PrefetchScalarGridSpec(
            num_scalar_prefetch=2,
            grid=(blocks,),
            in_specs=[part, whole, whole, part, pl.BlockSpec((heads, TQ, 1), lambda i, s, e: (0, i, 0))],
            out_specs=[part, whole, whole],
            scratch_shapes=[
                pltpu.VMEM((heads, rows, width), jnp.float32),
                pltpu.VMEM((heads, rows, width), jnp.float32),
            ],
        ),
        out_shape=[jax.ShapeDtypeStruct((heads, rows, width), jnp.bfloat16)] * 3,
        compiler_params=pltpu.CompilerParams(
            dimension_semantics=("arbitrary",), vmem_limit_bytes=48 * 1024 * 1024
        ),
        cost_estimate=pl.CostEstimate(
            flops=flops, transcendentals=heads * rows * LMAX, bytes_accessed=7 * q.size * 2
        ),
    )(starts, ends, q, k, v, do, lse)


def per_device(
    tokens,
    cotangent,
    lengths,
    dealing,
    gain_one,
    gain_two,
    attention_in,
    query_scale,
    attention_out,
    hidden_in,
    hidden_out,
):
    out_all, in_all, down_all = (
        lax.all_gather(attention_out, "mp", axis=0, tiled=True),
        lax.all_gather(hidden_in, "mp", axis=0, tiled=True),
        lax.all_gather(hidden_out, "mp", axis=0, tiled=True),
    )
    row_count = tokens.shape[0]
    mp_count = lax.axis_size("mp")
    my_group = lax.axis_index("dp")
    my_part = lax.axis_index("mp")
    group_rows = row_count * mp_count
    series_grp = group_rows // LMAX
    heads_here = NH // mp_count
    width_here = heads_here * HD
    shard_width = D // mp_count
    maps = series_maps(lengths, dealing, series_grp, group_rows, my_group)
    send_first, send_len = maps[0], maps[1]
    place_slot, place_start, place_len = dealt_places(lengths, dealing, series_grp, my_group)
    src_len = lax.dynamic_slice_in_dim(lengths, my_group * series_grp, series_grp)
    block_start, block_end, src_live = block_bounds(src_len, group_rows)
    live_mine = lax.dynamic_slice_in_dim(src_live, my_part * row_count, row_count).astype(
        jnp.float32
    )[:, None]
    gain_rows = jnp.zeros((8, D), jnp.bfloat16)
    gain_rows = gain_rows.at[0, :shard_width].set(gain_one).at[0, shard_width : 2 * shard_width].set(gain_two)
    packed = lax.all_gather(jnp.concatenate([tokens, gain_rows]), "mp", axis=0, tiled=False)
    gain_first = packed[:, row_count, :shard_width].reshape(D).astype(jnp.float32)
    gain_second = packed[:, row_count, shard_width : 2 * shard_width].reshape(D).astype(jnp.float32)
    inputs_group = packed[:, :row_count].reshape(group_rows, D).astype(jnp.float32)
    inv_group = lax.rsqrt(jnp.mean(inputs_group * inputs_group, axis=1, keepdims=True) + epsilon)
    normed_group = (inputs_group * inv_group * gain_first).astype(jnp.bfloat16)
    inputs = tokens.astype(jnp.float32)
    inv_one = lax.rsqrt(jnp.mean(inputs * inputs, axis=1, keepdims=True) + epsilon)
    projected = jnp.einsum(
        "rd,ucd->cru", normed_group, attention_in, preferred_element_type=jnp.float32
    )
    dim_scale = scale_base / math.sqrt(HD) * jax.nn.softplus(query_scale)
    query_raw = projected[0].reshape(group_rows, heads_here, HD).transpose(1, 0, 2)
    queries = (query_raw * dim_scale).astype(jnp.bfloat16)
    keys_group = projected[1].astype(jnp.bfloat16)
    values_group = projected[2].astype(jnp.bfloat16)
    kv_group = jnp.stack([keys_group, values_group])
    incoming = lax.all_to_all(
        fill_slots(kv_group, send_first, send_len), "dp", split_axis=1, concat_axis=1, tiled=True
    )
    cache = place_slots(incoming, place_slot, place_start, place_len, group_rows)
    keys = keys_group.reshape(group_rows, heads_here, HD).transpose(1, 0, 2)
    values = values_group.reshape(group_rows, heads_here, HD).transpose(1, 0, 2)
    mixed, log_total = attention_forward(queries, keys, values, block_start, block_end)
    att_group = jnp.where(
        src_live[:, None],
        mixed.transpose(1, 0, 2).reshape(group_rows, width_here),
        jnp.zeros((), jnp.bfloat16),
    )
    att_rows = lax.all_to_all(att_group, "mp", split_axis=0, concat_axis=1, tiled=True)
    branch = jnp.dot(att_rows, out_all, preferred_element_type=jnp.float32)
    first_sum = inputs + branch
    inv_two = lax.rsqrt(jnp.mean(first_sum * first_sum, axis=1, keepdims=True) + epsilon)
    normed_two = (first_sum * inv_two * gain_second).astype(jnp.bfloat16)
    preact = jnp.einsum("rd,fd->rf", normed_two, in_all, preferred_element_type=jnp.float32)
    hidden = jax.nn.silu(preact).astype(jnp.bfloat16)
    feed = jnp.dot(hidden, down_all, preferred_element_type=jnp.float32)
    layer_out = ((first_sum + feed) * live_mine).astype(jnp.bfloat16)
    out_grad = cotangent.astype(jnp.float32) * live_mine
    feed_grad = out_grad.astype(jnp.bfloat16)
    hidden_grad = jnp.einsum("rd,fd->rf", feed_grad, down_all, preferred_element_type=jnp.float32)
    gate_sig = jax.nn.sigmoid(preact)
    preact_grad = (hidden_grad * gate_sig * (1.0 + preact * (1.0 - gate_sig))).astype(jnp.bfloat16)
    normed_two_grad = jnp.dot(preact_grad, in_all, preferred_element_type=jnp.float32)
    scaled_two = gain_second * normed_two_grad
    first_grad = (
        out_grad
        + inv_two * scaled_two
        - first_sum * inv_two**3 * jnp.mean(scaled_two * first_sum, axis=1, keepdims=True)
    )
    branch_grad = first_grad.astype(jnp.bfloat16)
    att_rows_grad = jnp.einsum(
        "rd,ud->ru", branch_grad, out_all, preferred_element_type=jnp.float32
    ).astype(jnp.bfloat16)
    grad_group = lax.all_to_all(att_rows_grad, "mp", split_axis=1, concat_axis=0, tiled=True)
    grad_heads = (
        jnp.where(src_live[:, None], grad_group, jnp.zeros((), jnp.bfloat16))
        .reshape(group_rows, heads_here, HD)
        .transpose(1, 0, 2)
    )
    query_scaled_grad, key_grad, value_grad = attention_backward(
        queries, keys, values, grad_heads, log_total, block_start, block_end
    )
    live_heads = src_live[None, :, None]
    query_scaled_grad = jnp.where(live_heads, query_scaled_grad, jnp.zeros((), jnp.bfloat16)).astype(
        jnp.float32
    )
    scale_part = (
        jnp.sum(query_scaled_grad * query_raw, axis=(0, 1))
        * (scale_base / math.sqrt(HD))
        * jax.nn.sigmoid(query_scale)
    )
    query_grad = (query_scaled_grad * dim_scale).astype(jnp.bfloat16)
    proj_grad = jnp.stack(
        [
            query_grad,
            jnp.where(live_heads, key_grad, jnp.zeros((), jnp.bfloat16)),
            jnp.where(live_heads, value_grad, jnp.zeros((), jnp.bfloat16)),
        ]
    )
    weight_heads = attention_in.reshape(heads_here, HD, 3, D)
    qkv_part = jnp.einsum(
        "chre,rd->hecd", proj_grad, normed_group, preferred_element_type=jnp.float32
    ).reshape(width_here, 3, D)
    normed_one_part = jnp.einsum(
        "chre,hecd->rd", proj_grad, weight_heads, preferred_element_type=jnp.float32
    )
    normed_one_grad = lax.psum_scatter(
        normed_one_part.astype(jnp.bfloat16), "mp", scatter_dimension=0, tiled=True
    ).astype(jnp.float32)
    scaled_one = gain_first * normed_one_grad
    tokens_grad = (
        first_grad
        + inv_one * scaled_one
        - inputs * inv_one**3 * jnp.mean(scaled_one * inputs, axis=1, keepdims=True)
    )
    gain_one_part = jnp.sum(normed_one_grad * inputs * inv_one, axis=0)
    gain_two_part = jnp.sum(normed_two_grad * first_sum * inv_two, axis=0)
    small = jnp.concatenate(
        [
            gain_one_part.reshape(mp_count, shard_width),
            gain_two_part.reshape(mp_count, shard_width),
            jnp.broadcast_to(scale_part, (mp_count, HD)),
        ],
        axis=1,
    )
    small = lax.psum(lax.psum_scatter(small, "mp", scatter_dimension=0, tiled=True), "dp")
    gain_one_grad = small[0, :shard_width]
    gain_two_grad = small[0, shard_width : 2 * shard_width]
    query_scale_grad = small[0, 2 * shard_width :]
    out_part = jnp.einsum("ru,rd->ud", att_rows, branch_grad, preferred_element_type=jnp.float32)
    in_part = jnp.einsum("ru,rd->ud", preact_grad, normed_two, preferred_element_type=jnp.float32)
    down_part = jnp.einsum("ru,rd->ud", hidden, feed_grad, preferred_element_type=jnp.float32)
    row_terms = jnp.stack([out_part, in_part, down_part], axis=1)
    shares = lax.psum_scatter(
        row_terms.astype(jnp.bfloat16), "mp", scatter_dimension=0, tiled=True
    )
    totals = lax.psum(
        jnp.concatenate([qkv_part.astype(jnp.bfloat16), shares], axis=1), "dp"
    ).astype(jnp.float32)
    return (
        layer_out,
        tokens_grad,
        cache,
        gain_one_grad,
        gain_two_grad,
        totals[:, 0:3],
        query_scale_grad,
        totals[:, 3],
        totals[:, 4],
        totals[:, 5],
    )


def solution(mesh):
    placed = (
        P(("dp", "mp"), None),
        P(("dp", "mp"), None),
        P(),
        P(),
        P("mp"),
        P("mp"),
        P("mp", None, None),
        P(),
        P("mp", None),
        P("mp", None),
        P("mp", None),
    )
    return jax.shard_map(
        per_device,
        mesh=mesh,
        in_specs=placed,
        out_specs=(
            P(("dp", "mp"), None),
            P(("dp", "mp"), None),
            P(None, "dp", "mp"),
            P("mp"),
            P("mp"),
            P("mp", None, None),
            P(),
            P("mp", None),
            P("mp", None),
            P("mp", None),
        ),
        check_vma=False,
    )
```

```python
import math

import jax
import jax.numpy as jnp
from jax import lax
from jax.experimental import pallas as pl
from jax.experimental.pallas import tpu as pltpu
from jax.sharding import PartitionSpec as P


D = 1280
NH = 16
HD = 80
LMAX = 1024
BLK = 128
TQ = 128


epsilon = 1e-06
scale_base = 1.442695041
masked_score = -1e30


def lookup(values_table, positions):
    entries = jnp.arange(values_table.shape[0], dtype=jnp.int32)
    picked = jnp.where(positions[:, None] == entries[None, :], values_table[None, :], 0)
    return jnp.sum(picked, axis=1)


def packing(span_len, group_rows):
    blocks = (span_len + BLK - 1) // BLK
    block_ends = BLK * jnp.cumsum(blocks)
    starts = block_ends - BLK * blocks
    in_group = jnp.arange(group_rows, dtype=jnp.int32)
    series_at = jnp.sum((block_ends[None, :] <= in_group[:, None]).astype(jnp.int32), axis=1)
    capped = jnp.minimum(series_at, span_len.shape[0] - 1)
    offset = in_group - lookup(starts, capped)
    live_row = (series_at < span_len.shape[0]) & (offset < lookup(span_len, capped))
    return (starts, series_at, capped, offset, live_row)


def slot_table(slot_of, starts, span_len, slot_count):
    entries = jnp.arange(slot_count, dtype=jnp.int32)
    matched = slot_of[None, :] == entries[:, None]
    slot_first = jnp.sum(jnp.where(matched, starts[None, :], 0), axis=1)
    slot_length = jnp.sum(jnp.where(matched, span_len[None, :], 0), axis=1)
    return (slot_first, slot_length)


def series_maps(lengths, dealing, series_grp, group_rows, my_group):
    groups = lengths.shape[0] // series_grp
    capacity = (series_grp + groups - 1) // groups
    places = jnp.arange(series_grp, dtype=jnp.int32)
    target = dealing.reshape(groups, series_grp) // series_grp
    earlier = (target[:, :, None] == target[:, None, :]) & (
        places[None, None, :] < places[None, :, None]
    )
    rank_of = jnp.sum(earlier.astype(jnp.int32), axis=2)
    slot_of = (target * capacity + rank_of).reshape(-1)
    rank_flat = rank_of.reshape(-1)
    src_len = lax.dynamic_slice_in_dim(lengths, my_group * series_grp, series_grp)
    src_slot = lax.dynamic_slice_in_dim(slot_of, my_group * series_grp, series_grp)
    src_starts, _, src_capped, src_offset, src_live = packing(src_len, group_rows)
    dealt_places = jnp.arange(lengths.shape[0], dtype=jnp.int32)
    owner = jnp.sum(
        jnp.where(dealing[None, :] == dealt_places[:, None], dealt_places[None, :], 0), axis=1
    )
    my_series = lax.dynamic_slice_in_dim(owner, my_group * series_grp, series_grp)
    dst_len = lookup(lengths, my_series)
    dst_slot = my_series // series_grp * capacity + lookup(rank_flat, my_series)
    dst_starts, dst_at, dst_capped, dst_offset, dst_live = packing(dst_len, group_rows)
    slot_count = groups * capacity
    send_first, send_len = slot_table(src_slot, src_starts, src_len, slot_count)
    back_first, back_len = slot_table(dst_slot, dst_starts, dst_len, slot_count)
    src_index = lookup(src_slot, src_capped) * LMAX + src_offset
    dst_index = lookup(dst_slot, dst_capped) * LMAX + dst_offset
    key_live = jnp.where(dst_at < series_grp, dst_live, True)
    return (
        send_first,
        send_len,
        back_first,
        back_len,
        src_index,
        src_live,
        dst_index,
        dst_live,
        dst_at,
        key_live,
    )


def send_windows(values, slot_first, slot_length, my_group, groups):
    padded = jnp.pad(values, ((0, 0), (0, LMAX), (0, 0)))
    positions = jnp.arange(LMAX, dtype=jnp.int32)[None, :, None]
    windows = []
    for shift in range(groups):
        target = (my_group + shift) % groups
        window = lax.dynamic_slice_in_dim(padded, slot_first[target], LMAX, axis=1)
        windows.append(
            jnp.where(positions < slot_length[target], window, jnp.zeros((), values.dtype))
        )
    return windows


def place_slots(received, place_shift, place_start, place_len, out_rows):
    stacked = jnp.stack(received)
    rows = jnp.arange(out_rows, dtype=jnp.int32)[None, :, None]
    placed = jnp.zeros((stacked.shape[1], out_rows, stacked.shape[3]), stacked.dtype)
    for q in range(place_shift.shape[0]):
        window = lax.dynamic_index_in_dim(stacked, place_shift[q], axis=0, keepdims=False)
        padded = jnp.pad(window, ((0, 0), (out_rows, out_rows - LMAX), (0, 0)))
        shifted = lax.dynamic_slice_in_dim(padded, out_rows - place_start[q], out_rows, axis=1)
        inside = (rows >= place_start[q]) & (rows < place_start[q] + place_len[q])
        placed = jnp.where(inside, shifted, placed)
    return placed


def dealt_places(lengths, dealing, series_grp, my_group):
    dealt_places = jnp.arange(lengths.shape[0], dtype=jnp.int32)
    owner = jnp.sum(
        jnp.where(dealing[None, :] == dealt_places[:, None], dealt_places[None, :], 0), axis=1
    )
    my_series = lax.dynamic_slice_in_dim(owner, my_group * series_grp, series_grp)
    place_len = lookup(lengths, my_series)
    blocks = (place_len + BLK - 1) // BLK
    place_start = BLK * jnp.cumsum(blocks) - BLK * blocks
    return my_series // series_grp, place_start, place_len


def block_bounds(src_len, group_rows):
    starts, series_at, _, _, live_row = packing(src_len, group_rows)
    first_rows = jnp.arange(group_rows // TQ, dtype=jnp.int32) * TQ
    seg = series_at[first_rows]
    inside = seg < src_len.shape[0]
    seg_c = jnp.minimum(seg, src_len.shape[0] - 1)
    block_start = jnp.where(inside, lookup(starts, seg_c), 0)
    block_end = jnp.where(inside, block_start + lookup(src_len, seg_c), 0)
    return block_start.astype(jnp.int32), block_end.astype(jnp.int32), live_row


def _window(i, rows):
    qs = i * TQ
    ws = jnp.minimum(jnp.maximum(qs - (LMAX - TQ), 0), rows - LMAX)
    return qs, pl.multiple_of(ws, TQ)


def _allowed(qs, ws, s0, e0):
    a = qs + lax.broadcasted_iota(jnp.int32, (TQ, LMAX), 0)
    b = ws + lax.broadcasted_iota(jnp.int32, (TQ, LMAX), 1)
    return (b >= s0) & (b <= a) & (b < e0)


def attn_fwd_kernel(starts_ref, ends_ref, q_ref, k_ref, v_ref, o_ref, lse_ref):
    i = pl.program_id(0)
    heads, rows = k_ref.shape[0], k_ref.shape[1]
    qs, ws = _window(i, rows)
    s0 = starts_ref[i]
    e0 = ends_ref[i]

    @pl.when(s0 < e0)
    def _():
        allowed = _allowed(qs, ws, s0, e0)
        for h in range(heads):
            q = q_ref[h]
            k = k_ref[h, pl.ds(ws, LMAX), :]
            v = v_ref[h, pl.ds(ws, LMAX), :]
            s = lax.dot_general(q, k, (((1,), (1,)), ((), ())), preferred_element_type=jnp.float32)
            s = jnp.where(allowed, s, masked_score)
            m = jnp.max(s, axis=1, keepdims=True)
            p = jnp.exp(s - m)
            l = jnp.sum(p, axis=1, keepdims=True)
            probs = (p / l).astype(jnp.bfloat16)
            o = jnp.dot(probs, v, preferred_element_type=jnp.float32)
            o_ref[h] = o.astype(o_ref.dtype)
            lse_ref[h] = m + jnp.log(l)

    @pl.when(s0 >= e0)
    def _():
        o_ref[...] = jnp.zeros(o_ref.shape, o_ref.dtype)
        lse_ref[...] = jnp.zeros(lse_ref.shape, lse_ref.dtype)


def attn_bwd_kernel(starts_ref, ends_ref, q_ref, k_ref, v_ref, do_ref, lse_ref,
                    dq_ref, dk_ref, dv_ref, dk_acc, dv_acc):
    i = pl.program_id(0)
    heads, rows = k_ref.shape[0], k_ref.shape[1]
    qs, ws = _window(i, rows)
    s0 = starts_ref[i]
    e0 = ends_ref[i]

    @pl.when(i == 0)
    def _():
        dk_acc[...] = jnp.zeros(dk_acc.shape, dk_acc.dtype)
        dv_acc[...] = jnp.zeros(dv_acc.shape, dv_acc.dtype)

    @pl.when(s0 < e0)
    def _():
        allowed = _allowed(qs, ws, s0, e0)
        for h in range(heads):
            q = q_ref[h]
            k = k_ref[h, pl.ds(ws, LMAX), :]
            v = v_ref[h, pl.ds(ws, LMAX), :]
            do = do_ref[h]
            s = lax.dot_general(q, k, (((1,), (1,)), ((), ())), preferred_element_type=jnp.float32)
            s = jnp.where(allowed, s, masked_score)
            probs = jnp.exp(s - lse_ref[h])
            dp = lax.dot_general(do, v, (((1,), (1,)), ((), ())), preferred_element_type=jnp.float32)
            row_dot = jnp.sum(probs * dp, axis=1, keepdims=True)
            ds = (probs * (dp - row_dot)).astype(jnp.bfloat16)
            dq = jnp.dot(ds, k, preferred_element_type=jnp.float32)
            dq_ref[h] = dq.astype(dq_ref.dtype)
            dk_acc[h, pl.ds(ws, LMAX), :] += jnp.dot(ds.T, q, preferred_element_type=jnp.float32)
            dv_acc[h, pl.ds(ws, LMAX), :] += jnp.dot(
                probs.astype(jnp.bfloat16).T, do, preferred_element_type=jnp.float32
            )

    @pl.when(s0 >= e0)
    def _():
        dq_ref[...] = jnp.zeros(dq_ref.shape, dq_ref.dtype)

    @pl.when(i == pl.num_programs(0) - 1)
    def _():
        dk_ref[...] = dk_acc[...].astype(dk_ref.dtype)
        dv_ref[...] = dv_acc[...].astype(dv_ref.dtype)


def attention_forward(q, k, v, starts, ends):
    heads, rows, width = q.shape
    blocks = rows // TQ
    whole = pl.BlockSpec((heads, rows, width), lambda i, s, e: (0, 0, 0))
    part = pl.BlockSpec((heads, TQ, width), lambda i, s, e: (0, i, 0))
    flops = 4 * heads * rows * LMAX * width
    return pl.pallas_call(
        attn_fwd_kernel,
        grid_spec=pltpu.PrefetchScalarGridSpec(
            num_scalar_prefetch=2,
            grid=(blocks,),
            in_specs=[part, whole, whole],
            out_specs=[part, pl.BlockSpec((heads, TQ, 1), lambda i, s, e: (0, i, 0))],
        ),
        out_shape=[
            jax.ShapeDtypeStruct((heads, rows, width), jnp.bfloat16),
            jax.ShapeDtypeStruct((heads, rows, 1), jnp.float32),
        ],
        compiler_params=pltpu.CompilerParams(
            dimension_semantics=("arbitrary",), vmem_limit_bytes=48 * 1024 * 1024
        ),
        cost_estimate=pl.CostEstimate(
            flops=flops, transcendentals=heads * rows * LMAX, bytes_accessed=4 * q.size * 2
        ),
    )(starts, ends, q, k, v)


def attention_backward(q, k, v, do, lse, starts, ends):
    heads, rows, width = q.shape
    blocks = rows // TQ
    whole = pl.BlockSpec((heads, rows, width), lambda i, s, e: (0, 0, 0))
    part = pl.BlockSpec((heads, TQ, width), lambda i, s, e: (0, i, 0))
    flops = 10 * heads * rows * LMAX * width
    return pl.pallas_call(
        attn_bwd_kernel,
        grid_spec=pltpu.PrefetchScalarGridSpec(
            num_scalar_prefetch=2,
            grid=(blocks,),
            in_specs=[part, whole, whole, part, pl.BlockSpec((heads, TQ, 1), lambda i, s, e: (0, i, 0))],
            out_specs=[part, whole, whole],
            scratch_shapes=[
                pltpu.VMEM((heads, rows, width), jnp.float32),
                pltpu.VMEM((heads, rows, width), jnp.float32),
            ],
        ),
        out_shape=[jax.ShapeDtypeStruct((heads, rows, width), jnp.bfloat16)] * 3,
        compiler_params=pltpu.CompilerParams(
            dimension_semantics=("arbitrary",), vmem_limit_bytes=48 * 1024 * 1024
        ),
        cost_estimate=pl.CostEstimate(
            flops=flops, transcendentals=heads * rows * LMAX, bytes_accessed=7 * q.size * 2
        ),
    )(starts, ends, q, k, v, do, lse)


def per_device(
    tokens,
    cotangent,
    lengths,
    dealing,
    gain_one,
    gain_two,
    attention_in,
    query_scale,
    attention_out,
    hidden_in,
    hidden_out,
):
    out_all, in_all, down_all = (
        lax.all_gather(attention_out, "mp", axis=0, tiled=True),
        lax.all_gather(hidden_in, "mp", axis=0, tiled=True),
        lax.all_gather(hidden_out, "mp", axis=0, tiled=True),
    )
    row_count = tokens.shape[0]
    mp_count = lax.axis_size("mp")
    my_group = lax.axis_index("dp")
    my_part = lax.axis_index("mp")
    group_rows = row_count * mp_count
    series_grp = group_rows // LMAX
    heads_here = NH // mp_count
    width_here = heads_here * HD
    shard_width = D // mp_count
    maps = series_maps(lengths, dealing, series_grp, group_rows, my_group)
    send_first, send_len = maps[0], maps[1]
    place_slot, place_start, place_len = dealt_places(lengths, dealing, series_grp, my_group)
    src_len = lax.dynamic_slice_in_dim(lengths, my_group * series_grp, series_grp)
    block_start, block_end, src_live = block_bounds(src_len, group_rows)
    live_mine = lax.dynamic_slice_in_dim(src_live, my_part * row_count, row_count).astype(
        jnp.float32
    )[:, None]
    gain_rows = jnp.zeros((8, D), jnp.bfloat16)
    gain_rows = gain_rows.at[0, :shard_width].set(gain_one).at[0, shard_width : 2 * shard_width].set(gain_two)
    packed = lax.all_gather(jnp.concatenate([tokens, gain_rows]), "mp", axis=0, tiled=False)
    gain_first = packed[:, row_count, :shard_width].reshape(D).astype(jnp.float32)
    gain_second = packed[:, row_count, shard_width : 2 * shard_width].reshape(D).astype(jnp.float32)
    inputs_group = packed[:, :row_count].reshape(group_rows, D).astype(jnp.float32)
    inv_group = lax.rsqrt(jnp.mean(inputs_group * inputs_group, axis=1, keepdims=True) + epsilon)
    normed_group = (inputs_group * inv_group * gain_first).astype(jnp.bfloat16)
    inputs = tokens.astype(jnp.float32)
    inv_one = lax.rsqrt(jnp.mean(inputs * inputs, axis=1, keepdims=True) + epsilon)
    projected = jnp.einsum(
        "rd,ucd->cru", normed_group, attention_in, preferred_element_type=jnp.float32
    )
    dim_scale = scale_base / math.sqrt(HD) * jax.nn.softplus(query_scale)
    query_raw = projected[0].reshape(group_rows, heads_here, HD).transpose(1, 0, 2)
    queries = (query_raw * dim_scale).astype(jnp.bfloat16)
    keys_group = projected[1].astype(jnp.bfloat16)
    values_group = projected[2].astype(jnp.bfloat16)
    kv_group = jnp.stack([keys_group, values_group])
    groups = lax.axis_size("dp")
    windows = send_windows(kv_group, send_first, send_len, my_group, groups)
    received = [windows[0]] + [
        lax.ppermute(
            windows[shift], "dp", [(r, (r + shift) % groups) for r in range(groups)]
        )
        for shift in range(1, groups)
    ]
    place_shift = (my_group - place_slot) % groups
    cache = place_slots(received, place_shift, place_start, place_len, group_rows)
    keys = keys_group.reshape(group_rows, heads_here, HD).transpose(1, 0, 2)
    values = values_group.reshape(group_rows, heads_here, HD).transpose(1, 0, 2)
    mixed, log_total = attention_forward(queries, keys, values, block_start, block_end)
    att_group = jnp.where(
        src_live[:, None],
        mixed.transpose(1, 0, 2).reshape(group_rows, width_here),
        jnp.zeros((), jnp.bfloat16),
    )
    att_rows = lax.all_to_all(att_group, "mp", split_axis=0, concat_axis=1, tiled=True)
    branch = jnp.dot(att_rows, out_all, preferred_element_type=jnp.float32)
    first_sum = inputs + branch
    inv_two = lax.rsqrt(jnp.mean(first_sum * first_sum, axis=1, keepdims=True) + epsilon)
    normed_two = (first_sum * inv_two * gain_second).astype(jnp.bfloat16)
    preact = jnp.einsum("rd,fd->rf", normed_two, in_all, preferred_element_type=jnp.float32)
    hidden = jax.nn.silu(preact).astype(jnp.bfloat16)
    feed = jnp.dot(hidden, down_all, preferred_element_type=jnp.float32)
    layer_out = ((first_sum + feed) * live_mine).astype(jnp.bfloat16)
    out_grad = cotangent.astype(jnp.float32) * live_mine
    feed_grad = out_grad.astype(jnp.bfloat16)
    hidden_grad = jnp.einsum("rd,fd->rf", feed_grad, down_all, preferred_element_type=jnp.float32)
    gate_sig = jax.nn.sigmoid(preact)
    preact_grad = (hidden_grad * gate_sig * (1.0 + preact * (1.0 - gate_sig))).astype(jnp.bfloat16)
    normed_two_grad = jnp.dot(preact_grad, in_all, preferred_element_type=jnp.float32)
    scaled_two = gain_second * normed_two_grad
    first_grad = (
        out_grad
        + inv_two * scaled_two
        - first_sum * inv_two**3 * jnp.mean(scaled_two * first_sum, axis=1, keepdims=True)
    )
    branch_grad = first_grad.astype(jnp.bfloat16)
    att_rows_grad = jnp.einsum(
        "rd,ud->ru", branch_grad, out_all, preferred_element_type=jnp.float32
    ).astype(jnp.bfloat16)
    grad_group = lax.all_to_all(att_rows_grad, "mp", split_axis=1, concat_axis=0, tiled=True)
    grad_heads = (
        jnp.where(src_live[:, None], grad_group, jnp.zeros((), jnp.bfloat16))
        .reshape(group_rows, heads_here, HD)
        .transpose(1, 0, 2)
    )
    query_scaled_grad, key_grad, value_grad = attention_backward(
        queries, keys, values, grad_heads, log_total, block_start, block_end
    )
    live_heads = src_live[None, :, None]
    query_scaled_grad = jnp.where(live_heads, query_scaled_grad, jnp.zeros((), jnp.bfloat16)).astype(
        jnp.float32
    )
    scale_part = (
        jnp.sum(query_scaled_grad * query_raw, axis=(0, 1))
        * (scale_base / math.sqrt(HD))
        * jax.nn.sigmoid(query_scale)
    )
    query_grad = (query_scaled_grad * dim_scale).astype(jnp.bfloat16)
    proj_grad = jnp.stack(
        [
            query_grad,
            jnp.where(live_heads, key_grad, jnp.zeros((), jnp.bfloat16)),
            jnp.where(live_heads, value_grad, jnp.zeros((), jnp.bfloat16)),
        ]
    )
    weight_heads = attention_in.reshape(heads_here, HD, 3, D)
    qkv_part = jnp.einsum(
        "chre,rd->hecd", proj_grad, normed_group, preferred_element_type=jnp.float32
    ).reshape(width_here, 3, D)
    normed_one_part = jnp.einsum(
        "chre,hecd->rd", proj_grad, weight_heads, preferred_element_type=jnp.float32
    )
    normed_one_grad = lax.psum_scatter(
        normed_one_part.astype(jnp.bfloat16), "mp", scatter_dimension=0, tiled=True
    ).astype(jnp.float32)
    scaled_one = gain_first * normed_one_grad
    tokens_grad = (
        first_grad
        + inv_one * scaled_one
        - inputs * inv_one**3 * jnp.mean(scaled_one * inputs, axis=1, keepdims=True)
    )
    gain_one_part = jnp.sum(normed_one_part * inputs_group * inv_group, axis=0)
    gain_two_part = jnp.sum(normed_two_grad * first_sum * inv_two, axis=0)
    small = jnp.concatenate(
        [
            gain_one_part.reshape(mp_count, shard_width),
            gain_two_part.reshape(mp_count, shard_width),
            jnp.broadcast_to(scale_part, (mp_count, HD)),
        ],
        axis=1,
    )
    small = lax.psum(lax.psum_scatter(small, "mp", scatter_dimension=0, tiled=True), "dp")
    gain_one_grad = small[0, :shard_width]
    gain_two_grad = small[0, shard_width : 2 * shard_width]
    query_scale_grad = small[0, 2 * shard_width :]
    out_part = jnp.einsum("ru,rd->ud", att_rows, branch_grad, preferred_element_type=jnp.float32)
    in_part = jnp.einsum("ru,rd->ud", preact_grad, normed_two, preferred_element_type=jnp.float32)
    down_part = jnp.einsum("ru,rd->ud", hidden, feed_grad, preferred_element_type=jnp.float32)
    row_terms = jnp.stack([out_part, in_part, down_part], axis=1)
    shares = lax.psum_scatter(
        row_terms.astype(jnp.bfloat16), "mp", scatter_dimension=0, tiled=True
    )
    totals = lax.psum(
        jnp.concatenate([qkv_part.astype(jnp.bfloat16), shares], axis=1), "dp"
    ).astype(jnp.float32)
    return (
        layer_out,
        tokens_grad,
        cache,
        gain_one_grad,
        gain_two_grad,
        totals[:, 0:3],
        query_scale_grad,
        totals[:, 3],
        totals[:, 4],
        totals[:, 5],
    )


def solution(mesh):
    placed = (
        P(("dp", "mp"), None),
        P(("dp", "mp"), None),
        P(),
        P(),
        P("mp"),
        P("mp"),
        P("mp", None, None),
        P(),
        P("mp", None),
        P("mp", None),
        P("mp", None),
    )
    return jax.shard_map(
        per_device,
        mesh=mesh,
        in_specs=placed,
        out_specs=(
            P(("dp", "mp"), None),
            P(("dp", "mp"), None),
            P(None, "dp", "mp"),
            P("mp"),
            P("mp"),
            P("mp", None, None),
            P(),
            P("mp", None),
            P("mp", None),
            P("mp", None),
        ),
        check_vma=False,
    )
```

```python
import math

import jax
import jax.numpy as jnp
from jax import lax
from jax.experimental import pallas as pl
from jax.experimental.pallas import tpu as pltpu
from jax.sharding import PartitionSpec as P


D = 1280
NH = 16
HD = 80
LMAX = 1024
BLK = 128
TQ = 128


epsilon = 1e-06
scale_base = 1.442695041
masked_score = -1e30


def lookup(values_table, positions):
    entries = jnp.arange(values_table.shape[0], dtype=jnp.int32)
    picked = jnp.where(positions[:, None] == entries[None, :], values_table[None, :], 0)
    return jnp.sum(picked, axis=1)


def packing(span_len, group_rows):
    blocks = (span_len + BLK - 1) // BLK
    block_ends = BLK * jnp.cumsum(blocks)
    starts = block_ends - BLK * blocks
    in_group = jnp.arange(group_rows, dtype=jnp.int32)
    series_at = jnp.sum((block_ends[None, :] <= in_group[:, None]).astype(jnp.int32), axis=1)
    capped = jnp.minimum(series_at, span_len.shape[0] - 1)
    offset = in_group - lookup(starts, capped)
    live_row = (series_at < span_len.shape[0]) & (offset < lookup(span_len, capped))
    return (starts, series_at, capped, offset, live_row)


def slot_table(slot_of, starts, span_len, slot_count):
    entries = jnp.arange(slot_count, dtype=jnp.int32)
    matched = slot_of[None, :] == entries[:, None]
    slot_first = jnp.sum(jnp.where(matched, starts[None, :], 0), axis=1)
    slot_length = jnp.sum(jnp.where(matched, span_len[None, :], 0), axis=1)
    return (slot_first, slot_length)


def series_maps(lengths, dealing, series_grp, group_rows, my_group):
    groups = lengths.shape[0] // series_grp
    capacity = (series_grp + groups - 1) // groups
    places = jnp.arange(series_grp, dtype=jnp.int32)
    target = dealing.reshape(groups, series_grp) // series_grp
    earlier = (target[:, :, None] == target[:, None, :]) & (
        places[None, None, :] < places[None, :, None]
    )
    rank_of = jnp.sum(earlier.astype(jnp.int32), axis=2)
    slot_of = (target * capacity + rank_of).reshape(-1)
    rank_flat = rank_of.reshape(-1)
    src_len = lax.dynamic_slice_in_dim(lengths, my_group * series_grp, series_grp)
    src_slot = lax.dynamic_slice_in_dim(slot_of, my_group * series_grp, series_grp)
    src_starts, _, src_capped, src_offset, src_live = packing(src_len, group_rows)
    dealt_places = jnp.arange(lengths.shape[0], dtype=jnp.int32)
    owner = jnp.sum(
        jnp.where(dealing[None, :] == dealt_places[:, None], dealt_places[None, :], 0), axis=1
    )
    my_series = lax.dynamic_slice_in_dim(owner, my_group * series_grp, series_grp)
    dst_len = lookup(lengths, my_series)
    dst_slot = my_series // series_grp * capacity + lookup(rank_flat, my_series)
    dst_starts, dst_at, dst_capped, dst_offset, dst_live = packing(dst_len, group_rows)
    slot_count = groups * capacity
    send_first, send_len = slot_table(src_slot, src_starts, src_len, slot_count)
    back_first, back_len = slot_table(dst_slot, dst_starts, dst_len, slot_count)
    src_index = lookup(src_slot, src_capped) * LMAX + src_offset
    dst_index = lookup(dst_slot, dst_capped) * LMAX + dst_offset
    key_live = jnp.where(dst_at < series_grp, dst_live, True)
    return (
        send_first,
        send_len,
        back_first,
        back_len,
        src_index,
        src_live,
        dst_index,
        dst_live,
        dst_at,
        key_live,
    )


def send_windows(values, slot_first, slot_length, my_group, groups):
    padded = jnp.pad(values, ((0, 0), (0, LMAX), (0, 0)))
    positions = jnp.arange(LMAX, dtype=jnp.int32)[None, :, None]
    windows = []
    for shift in range(groups):
        target = (my_group + shift) % groups
        window = lax.dynamic_slice_in_dim(padded, slot_first[target], LMAX, axis=1)
        windows.append(
            jnp.where(positions < slot_length[target], window, jnp.zeros((), values.dtype))
        )
    return windows


def place_slots(received, place_shift, place_start, place_len, out_rows):
    stacked = jnp.stack(received)
    rows = jnp.arange(out_rows, dtype=jnp.int32)[None, :, None]
    placed = jnp.zeros((stacked.shape[1], out_rows, stacked.shape[3]), stacked.dtype)
    for q in range(place_shift.shape[0]):
        window = lax.dynamic_index_in_dim(stacked, place_shift[q], axis=0, keepdims=False)
        padded = jnp.pad(window, ((0, 0), (out_rows, out_rows - LMAX), (0, 0)))
        shifted = lax.dynamic_slice_in_dim(padded, out_rows - place_start[q], out_rows, axis=1)
        inside = (rows >= place_start[q]) & (rows < place_start[q] + place_len[q])
        placed = jnp.where(inside, shifted, placed)
    return placed


def dealt_places(lengths, dealing, series_grp, my_group):
    dealt_places = jnp.arange(lengths.shape[0], dtype=jnp.int32)
    owner = jnp.sum(
        jnp.where(dealing[None, :] == dealt_places[:, None], dealt_places[None, :], 0), axis=1
    )
    my_series = lax.dynamic_slice_in_dim(owner, my_group * series_grp, series_grp)
    place_len = lookup(lengths, my_series)
    blocks = (place_len + BLK - 1) // BLK
    place_start = BLK * jnp.cumsum(blocks) - BLK * blocks
    return my_series // series_grp, place_start, place_len


def block_bounds(src_len, group_rows):
    starts, series_at, _, _, live_row = packing(src_len, group_rows)
    first_rows = jnp.arange(group_rows // TQ, dtype=jnp.int32) * TQ
    seg = series_at[first_rows]
    inside = seg < src_len.shape[0]
    seg_c = jnp.minimum(seg, src_len.shape[0] - 1)
    block_start = jnp.where(inside, lookup(starts, seg_c), 0)
    block_end = jnp.where(inside, block_start + lookup(src_len, seg_c), 0)
    return block_start.astype(jnp.int32), block_end.astype(jnp.int32), live_row


def _window(i, rows):
    qs = i * TQ
    ws = jnp.minimum(jnp.maximum(qs - (LMAX - TQ), 0), rows - LMAX)
    return qs, pl.multiple_of(ws, TQ)


def _allowed(qs, ws, s0, e0):
    a = qs + lax.broadcasted_iota(jnp.int32, (TQ, LMAX), 0)
    b = ws + lax.broadcasted_iota(jnp.int32, (TQ, LMAX), 1)
    return (b >= s0) & (b <= a) & (b < e0)


def attn_fwd_kernel(starts_ref, ends_ref, q_ref, k_ref, v_ref, o_ref, lse_ref):
    i = pl.program_id(0)
    heads, rows = k_ref.shape[0], k_ref.shape[1]
    qs, ws = _window(i, rows)
    s0 = starts_ref[i]
    e0 = ends_ref[i]

    @pl.when(s0 < e0)
    def _():
        allowed = _allowed(qs, ws, s0, e0)
        for h in range(heads):
            q = q_ref[h]
            k = k_ref[h, pl.ds(ws, LMAX), :]
            v = v_ref[h, pl.ds(ws, LMAX), :]
            s = lax.dot_general(q, k, (((1,), (1,)), ((), ())), preferred_element_type=jnp.float32)
            s = jnp.where(allowed, s, masked_score)
            m = jnp.max(s, axis=1, keepdims=True)
            p = jnp.exp(s - m)
            l = jnp.sum(p, axis=1, keepdims=True)
            probs = (p / l).astype(jnp.bfloat16)
            o = jnp.dot(probs, v, preferred_element_type=jnp.float32)
            o_ref[h] = o.astype(o_ref.dtype)
            lse_ref[h] = m + jnp.log(l)

    @pl.when(s0 >= e0)
    def _():
        o_ref[...] = jnp.zeros(o_ref.shape, o_ref.dtype)
        lse_ref[...] = jnp.zeros(lse_ref.shape, lse_ref.dtype)


def attn_bwd_kernel(starts_ref, ends_ref, q_ref, k_ref, v_ref, do_ref, lse_ref,
                    dq_ref, dk_ref, dv_ref, dk_acc, dv_acc):
    i = pl.program_id(0)
    heads, rows = k_ref.shape[0], k_ref.shape[1]
    qs, ws = _window(i, rows)
    s0 = starts_ref[i]
    e0 = ends_ref[i]

    @pl.when(i == 0)
    def _():
        dk_acc[...] = jnp.zeros(dk_acc.shape, dk_acc.dtype)
        dv_acc[...] = jnp.zeros(dv_acc.shape, dv_acc.dtype)

    @pl.when(s0 < e0)
    def _():
        allowed = _allowed(qs, ws, s0, e0)
        for h in range(heads):
            q = q_ref[h]
            k = k_ref[h, pl.ds(ws, LMAX), :]
            v = v_ref[h, pl.ds(ws, LMAX), :]
            do = do_ref[h]
            s = lax.dot_general(q, k, (((1,), (1,)), ((), ())), preferred_element_type=jnp.float32)
            s = jnp.where(allowed, s, masked_score)
            probs = jnp.exp(s - lse_ref[h])
            dp = lax.dot_general(do, v, (((1,), (1,)), ((), ())), preferred_element_type=jnp.float32)
            row_dot = jnp.sum(probs * dp, axis=1, keepdims=True)
            ds = (probs * (dp - row_dot)).astype(jnp.bfloat16)
            dq = jnp.dot(ds, k, preferred_element_type=jnp.float32)
            dq_ref[h] = dq.astype(dq_ref.dtype)
            dk_acc[h, pl.ds(ws, LMAX), :] += jnp.dot(ds.T, q, preferred_element_type=jnp.float32)
            dv_acc[h, pl.ds(ws, LMAX), :] += jnp.dot(
                probs.astype(jnp.bfloat16).T, do, preferred_element_type=jnp.float32
            )

    @pl.when(s0 >= e0)
    def _():
        dq_ref[...] = jnp.zeros(dq_ref.shape, dq_ref.dtype)

    @pl.when(i == pl.num_programs(0) - 1)
    def _():
        dk_ref[...] = dk_acc[...].astype(dk_ref.dtype)
        dv_ref[...] = dv_acc[...].astype(dv_ref.dtype)


def attention_forward(q, k, v, starts, ends):
    heads, rows, width = q.shape
    blocks = rows // TQ
    whole = pl.BlockSpec((heads, rows, width), lambda i, s, e: (0, 0, 0))
    part = pl.BlockSpec((heads, TQ, width), lambda i, s, e: (0, i, 0))
    flops = 4 * heads * rows * LMAX * width
    return pl.pallas_call(
        attn_fwd_kernel,
        grid_spec=pltpu.PrefetchScalarGridSpec(
            num_scalar_prefetch=2,
            grid=(blocks,),
            in_specs=[part, whole, whole],
            out_specs=[part, pl.BlockSpec((heads, TQ, 1), lambda i, s, e: (0, i, 0))],
        ),
        out_shape=[
            jax.ShapeDtypeStruct((heads, rows, width), jnp.bfloat16),
            jax.ShapeDtypeStruct((heads, rows, 1), jnp.float32),
        ],
        compiler_params=pltpu.CompilerParams(
            dimension_semantics=("arbitrary",), vmem_limit_bytes=48 * 1024 * 1024
        ),
        cost_estimate=pl.CostEstimate(
            flops=flops, transcendentals=heads * rows * LMAX, bytes_accessed=4 * q.size * 2
        ),
    )(starts, ends, q, k, v)


def attention_backward(q, k, v, do, lse, starts, ends):
    heads, rows, width = q.shape
    blocks = rows // TQ
    whole = pl.BlockSpec((heads, rows, width), lambda i, s, e: (0, 0, 0))
    part = pl.BlockSpec((heads, TQ, width), lambda i, s, e: (0, i, 0))
    flops = 10 * heads * rows * LMAX * width
    return pl.pallas_call(
        attn_bwd_kernel,
        grid_spec=pltpu.PrefetchScalarGridSpec(
            num_scalar_prefetch=2,
            grid=(blocks,),
            in_specs=[part, whole, whole, part, pl.BlockSpec((heads, TQ, 1), lambda i, s, e: (0, i, 0))],
            out_specs=[part, whole, whole],
            scratch_shapes=[
                pltpu.VMEM((heads, rows, width), jnp.float32),
                pltpu.VMEM((heads, rows, width), jnp.float32),
            ],
        ),
        out_shape=[jax.ShapeDtypeStruct((heads, rows, width), jnp.bfloat16)] * 3,
        compiler_params=pltpu.CompilerParams(
            dimension_semantics=("arbitrary",), vmem_limit_bytes=48 * 1024 * 1024
        ),
        cost_estimate=pl.CostEstimate(
            flops=flops, transcendentals=heads * rows * LMAX, bytes_accessed=7 * q.size * 2
        ),
    )(starts, ends, q, k, v, do, lse)


def per_device(
    tokens,
    cotangent,
    lengths,
    dealing,
    gain_one,
    gain_two,
    attention_in,
    query_scale,
    attention_out,
    hidden_in,
    hidden_out,
):
    out_all, in_all, down_all = (
        lax.all_gather(attention_out, "mp", axis=0, tiled=True),
        lax.all_gather(hidden_in, "mp", axis=0, tiled=True),
        lax.all_gather(hidden_out, "mp", axis=0, tiled=True),
    )
    row_count = tokens.shape[0]
    mp_count = lax.axis_size("mp")
    my_group = lax.axis_index("dp")
    my_part = lax.axis_index("mp")
    group_rows = row_count * mp_count
    series_grp = group_rows // LMAX
    heads_here = NH // mp_count
    width_here = heads_here * HD
    shard_width = D // mp_count
    maps = series_maps(lengths, dealing, series_grp, group_rows, my_group)
    send_first, send_len = maps[0], maps[1]
    place_slot, place_start, place_len = dealt_places(lengths, dealing, series_grp, my_group)
    src_len = lax.dynamic_slice_in_dim(lengths, my_group * series_grp, series_grp)
    block_start, block_end, src_live = block_bounds(src_len, group_rows)
    live_mine = lax.dynamic_slice_in_dim(src_live, my_part * row_count, row_count).astype(
        jnp.float32
    )[:, None]
    gain_rows = jnp.zeros((8, D), jnp.bfloat16)
    gain_rows = gain_rows.at[0, :shard_width].set(gain_one).at[0, shard_width : 2 * shard_width].set(gain_two)
    packed = lax.all_gather(jnp.concatenate([tokens, gain_rows]), "mp", axis=0, tiled=False)
    gain_first = packed[:, row_count, :shard_width].reshape(D).astype(jnp.float32)
    gain_second = packed[:, row_count, shard_width : 2 * shard_width].reshape(D).astype(jnp.float32)
    inputs_group = packed[:, :row_count].reshape(group_rows, D).astype(jnp.float32)
    inv_group = lax.rsqrt(jnp.mean(inputs_group * inputs_group, axis=1, keepdims=True) + epsilon)
    normed_group = (inputs_group * inv_group * gain_first).astype(jnp.bfloat16)
    inputs = tokens.astype(jnp.float32)
    inv_one = lax.rsqrt(jnp.mean(inputs * inputs, axis=1, keepdims=True) + epsilon)
    weight_heads = attention_in.reshape(heads_here, HD, 3, D)
    projected = jnp.einsum(
        "rd,hecd->chre", normed_group, weight_heads, preferred_element_type=jnp.float32
    )
    dim_scale = scale_base / math.sqrt(HD) * jax.nn.softplus(query_scale)
    query_raw = projected[0]
    queries = (query_raw * dim_scale).astype(jnp.bfloat16)
    keys = projected[1].astype(jnp.bfloat16)
    values = projected[2].astype(jnp.bfloat16)
    kv_rows = jnp.stack([keys, values]).transpose(0, 2, 1, 3).reshape(2, group_rows, width_here)
    groups = lax.axis_size("dp")
    windows = send_windows(kv_rows, send_first, send_len, my_group, groups)
    received = [windows[0]] + [
        lax.ppermute(
            windows[shift], "dp", [(r, (r + shift) % groups) for r in range(groups)]
        )
        for shift in range(1, groups)
    ]
    place_shift = (my_group - place_slot) % groups
    cache = place_slots(received, place_shift, place_start, place_len, group_rows)
    mixed, log_total = attention_forward(queries, keys, values, block_start, block_end)
    att_group = jnp.where(src_live[None, :, None], mixed, jnp.zeros((), jnp.bfloat16))
    att_heads = lax.all_to_all(att_group, "mp", split_axis=1, concat_axis=0, tiled=True)
    out_heads = out_all.reshape(NH, HD, D)
    branch = jnp.einsum("hie,hed->id", att_heads, out_heads, preferred_element_type=jnp.float32)
    first_sum = inputs + branch
    inv_two = lax.rsqrt(jnp.mean(first_sum * first_sum, axis=1, keepdims=True) + epsilon)
    normed_two = (first_sum * inv_two * gain_second).astype(jnp.bfloat16)
    preact = jnp.einsum("rd,fd->rf", normed_two, in_all, preferred_element_type=jnp.float32)
    hidden = jax.nn.silu(preact).astype(jnp.bfloat16)
    feed = jnp.dot(hidden, down_all, preferred_element_type=jnp.float32)
    layer_out = ((first_sum + feed) * live_mine).astype(jnp.bfloat16)
    out_grad = cotangent.astype(jnp.float32) * live_mine
    feed_grad = out_grad.astype(jnp.bfloat16)
    hidden_grad = jnp.einsum("rd,fd->rf", feed_grad, down_all, preferred_element_type=jnp.float32)
    gate_sig = jax.nn.sigmoid(preact)
    preact_grad = (hidden_grad * gate_sig * (1.0 + preact * (1.0 - gate_sig))).astype(jnp.bfloat16)
    normed_two_grad = jnp.dot(preact_grad, in_all, preferred_element_type=jnp.float32)
    scaled_two = gain_second * normed_two_grad
    first_grad = (
        out_grad
        + inv_two * scaled_two
        - first_sum * inv_two**3 * jnp.mean(scaled_two * first_sum, axis=1, keepdims=True)
    )
    branch_grad = first_grad.astype(jnp.bfloat16)
    att_heads_grad = jnp.einsum(
        "id,hed->hie", branch_grad, out_heads, preferred_element_type=jnp.float32
    ).astype(jnp.bfloat16)
    grad_group = lax.all_to_all(att_heads_grad, "mp", split_axis=0, concat_axis=1, tiled=True)
    grad_heads = jnp.where(src_live[None, :, None], grad_group, jnp.zeros((), jnp.bfloat16))
    query_scaled_grad, key_grad, value_grad = attention_backward(
        queries, keys, values, grad_heads, log_total, block_start, block_end
    )
    live_heads = src_live[None, :, None]
    query_scaled_grad = jnp.where(live_heads, query_scaled_grad, jnp.zeros((), jnp.bfloat16)).astype(
        jnp.float32
    )
    scale_part = (
        jnp.sum(query_scaled_grad * query_raw, axis=(0, 1))
        * (scale_base / math.sqrt(HD))
        * jax.nn.sigmoid(query_scale)
    )
    query_grad = (query_scaled_grad * dim_scale).astype(jnp.bfloat16)
    proj_grad = jnp.stack(
        [
            query_grad,
            jnp.where(live_heads, key_grad, jnp.zeros((), jnp.bfloat16)),
            jnp.where(live_heads, value_grad, jnp.zeros((), jnp.bfloat16)),
        ]
    )
    qkv_part = jnp.einsum(
        "chre,rd->hecd", proj_grad, normed_group, preferred_element_type=jnp.float32
    ).reshape(width_here, 3, D)
    normed_one_part = jnp.einsum(
        "chre,hecd->rd", proj_grad, weight_heads, preferred_element_type=jnp.float32
    )
    normed_one_grad = lax.psum_scatter(
        normed_one_part.astype(jnp.bfloat16), "mp", scatter_dimension=0, tiled=True
    ).astype(jnp.float32)
    scaled_one = gain_first * normed_one_grad
    tokens_grad = (
        first_grad
        + inv_one * scaled_one
        - inputs * inv_one**3 * jnp.mean(scaled_one * inputs, axis=1, keepdims=True)
    )
    gain_one_part = jnp.sum(normed_one_part * inputs_group * inv_group, axis=0)
    gain_two_part = jnp.sum(normed_two_grad * first_sum * inv_two, axis=0)
    small = jnp.concatenate(
        [
            gain_one_part.reshape(mp_count, shard_width),
            gain_two_part.reshape(mp_count, shard_width),
            jnp.broadcast_to(scale_part, (mp_count, HD)),
        ],
        axis=1,
    )
    small = lax.psum(lax.psum_scatter(small, "mp", scatter_dimension=0, tiled=True), "dp")
    gain_one_grad = small[0, :shard_width]
    gain_two_grad = small[0, shard_width : 2 * shard_width]
    query_scale_grad = small[0, 2 * shard_width :]
    out_part = jnp.einsum(
        "hie,id->hed", att_heads, branch_grad, preferred_element_type=jnp.float32
    ).reshape(D, D)
    in_part = jnp.einsum("ru,rd->ud", preact_grad, normed_two, preferred_element_type=jnp.float32)
    down_part = jnp.einsum("ru,rd->ud", hidden, feed_grad, preferred_element_type=jnp.float32)
    row_terms = jnp.stack([out_part, in_part, down_part], axis=1)
    shares = lax.psum_scatter(
        row_terms.astype(jnp.bfloat16), "mp", scatter_dimension=0, tiled=True
    )
    totals = lax.psum(
        jnp.concatenate([qkv_part.astype(jnp.bfloat16), shares], axis=1), "dp"
    ).astype(jnp.float32)
    return (
        layer_out,
        tokens_grad,
        cache,
        gain_one_grad,
        gain_two_grad,
        totals[:, 0:3],
        query_scale_grad,
        totals[:, 3],
        totals[:, 4],
        totals[:, 5],
    )


def solution(mesh):
    placed = (
        P(("dp", "mp"), None),
        P(("dp", "mp"), None),
        P(),
        P(),
        P("mp"),
        P("mp"),
        P("mp", None, None),
        P(),
        P("mp", None),
        P("mp", None),
        P("mp", None),
    )
    return jax.shard_map(
        per_device,
        mesh=mesh,
        in_specs=placed,
        out_specs=(
            P(("dp", "mp"), None),
            P(("dp", "mp"), None),
            P(None, "dp", "mp"),
            P("mp"),
            P("mp"),
            P("mp", None, None),
            P(),
            P("mp", None),
            P("mp", None),
            P("mp", None),
        ),
        check_vma=False,
    )
```

```python
import math

import jax
import jax.numpy as jnp
from jax import lax
from jax.experimental import pallas as pl
from jax.experimental.pallas import tpu as pltpu
from jax.sharding import PartitionSpec as P


D = 1280
NH = 16
HD = 80
LMAX = 1024
BLK = 128
TQ = 128


epsilon = 1e-06
scale_base = 1.442695041
masked_score = -1e30


def lookup(values_table, positions):
    entries = jnp.arange(values_table.shape[0], dtype=jnp.int32)
    picked = jnp.where(positions[:, None] == entries[None, :], values_table[None, :], 0)
    return jnp.sum(picked, axis=1)


def packing(span_len, group_rows):
    blocks = (span_len + BLK - 1) // BLK
    block_ends = BLK * jnp.cumsum(blocks)
    starts = block_ends - BLK * blocks
    in_group = jnp.arange(group_rows, dtype=jnp.int32)
    series_at = jnp.sum((block_ends[None, :] <= in_group[:, None]).astype(jnp.int32), axis=1)
    capped = jnp.minimum(series_at, span_len.shape[0] - 1)
    offset = in_group - lookup(starts, capped)
    live_row = (series_at < span_len.shape[0]) & (offset < lookup(span_len, capped))
    return (starts, series_at, capped, offset, live_row)


def slot_table(slot_of, starts, span_len, slot_count):
    entries = jnp.arange(slot_count, dtype=jnp.int32)
    matched = slot_of[None, :] == entries[:, None]
    slot_first = jnp.sum(jnp.where(matched, starts[None, :], 0), axis=1)
    slot_length = jnp.sum(jnp.where(matched, span_len[None, :], 0), axis=1)
    return (slot_first, slot_length)


def series_maps(lengths, dealing, series_grp, group_rows, my_group):
    groups = lengths.shape[0] // series_grp
    capacity = (series_grp + groups - 1) // groups
    places = jnp.arange(series_grp, dtype=jnp.int32)
    target = dealing.reshape(groups, series_grp) // series_grp
    earlier = (target[:, :, None] == target[:, None, :]) & (
        places[None, None, :] < places[None, :, None]
    )
    rank_of = jnp.sum(earlier.astype(jnp.int32), axis=2)
    slot_of = (target * capacity + rank_of).reshape(-1)
    rank_flat = rank_of.reshape(-1)
    src_len = lax.dynamic_slice_in_dim(lengths, my_group * series_grp, series_grp)
    src_slot = lax.dynamic_slice_in_dim(slot_of, my_group * series_grp, series_grp)
    src_starts, _, src_capped, src_offset, src_live = packing(src_len, group_rows)
    dealt_places = jnp.arange(lengths.shape[0], dtype=jnp.int32)
    owner = jnp.sum(
        jnp.where(dealing[None, :] == dealt_places[:, None], dealt_places[None, :], 0), axis=1
    )
    my_series = lax.dynamic_slice_in_dim(owner, my_group * series_grp, series_grp)
    dst_len = lookup(lengths, my_series)
    dst_slot = my_series // series_grp * capacity + lookup(rank_flat, my_series)
    dst_starts, dst_at, dst_capped, dst_offset, dst_live = packing(dst_len, group_rows)
    slot_count = groups * capacity
    send_first, send_len = slot_table(src_slot, src_starts, src_len, slot_count)
    back_first, back_len = slot_table(dst_slot, dst_starts, dst_len, slot_count)
    src_index = lookup(src_slot, src_capped) * LMAX + src_offset
    dst_index = lookup(dst_slot, dst_capped) * LMAX + dst_offset
    key_live = jnp.where(dst_at < series_grp, dst_live, True)
    return (
        send_first,
        send_len,
        back_first,
        back_len,
        src_index,
        src_live,
        dst_index,
        dst_live,
        dst_at,
        key_live,
    )


def send_windows(values, slot_first, slot_length, my_group, groups):
    padded = jnp.pad(values, ((0, 0), (0, LMAX), (0, 0)))
    positions = jnp.arange(LMAX, dtype=jnp.int32)[None, :, None]
    windows = []
    for shift in range(groups):
        target = (my_group + shift) % groups
        window = lax.dynamic_slice_in_dim(padded, slot_first[target], LMAX, axis=1)
        windows.append(
            jnp.where(positions < slot_length[target], window, jnp.zeros((), values.dtype))
        )
    return windows


def place_slots(received, place_shift, place_start, place_len, out_rows):
    stacked = jnp.stack(received)
    rows = jnp.arange(out_rows, dtype=jnp.int32)[None, :, None]
    placed = jnp.zeros((stacked.shape[1], out_rows, stacked.shape[3]), stacked.dtype)
    for q in range(place_shift.shape[0]):
        window = lax.dynamic_index_in_dim(stacked, place_shift[q], axis=0, keepdims=False)
        padded = jnp.pad(window, ((0, 0), (out_rows, out_rows - LMAX), (0, 0)))
        shifted = lax.dynamic_slice_in_dim(padded, out_rows - place_start[q], out_rows, axis=1)
        inside = (rows >= place_start[q]) & (rows < place_start[q] + place_len[q])
        placed = jnp.where(inside, shifted, placed)
    return placed


def dealt_places(lengths, dealing, series_grp, my_group):
    dealt_places = jnp.arange(lengths.shape[0], dtype=jnp.int32)
    owner = jnp.sum(
        jnp.where(dealing[None, :] == dealt_places[:, None], dealt_places[None, :], 0), axis=1
    )
    my_series = lax.dynamic_slice_in_dim(owner, my_group * series_grp, series_grp)
    place_len = lookup(lengths, my_series)
    blocks = (place_len + BLK - 1) // BLK
    place_start = BLK * jnp.cumsum(blocks) - BLK * blocks
    return my_series // series_grp, place_start, place_len


def block_bounds(src_len, group_rows):
    starts, series_at, _, _, live_row = packing(src_len, group_rows)
    first_rows = jnp.arange(group_rows // TQ, dtype=jnp.int32) * TQ
    seg = series_at[first_rows]
    inside = seg < src_len.shape[0]
    seg_c = jnp.minimum(seg, src_len.shape[0] - 1)
    block_start = jnp.where(inside, lookup(starts, seg_c), 0)
    block_end = jnp.where(inside, block_start + lookup(src_len, seg_c), 0)
    return block_start.astype(jnp.int32), block_end.astype(jnp.int32), live_row


def _window(i, rows):
    qs = i * TQ
    ws = jnp.minimum(jnp.maximum(qs - (LMAX - TQ), 0), rows - LMAX)
    return qs, pl.multiple_of(ws, TQ)


def _allowed(qs, ws, s0, e0):
    a = qs + lax.broadcasted_iota(jnp.int32, (TQ, LMAX), 0)
    b = ws + lax.broadcasted_iota(jnp.int32, (TQ, LMAX), 1)
    return (b >= s0) & (b <= a) & (b < e0)


def attn_fwd_kernel(starts_ref, ends_ref, q_ref, k_ref, v_ref, o_ref, lse_ref):
    i = pl.program_id(0)
    heads, rows = k_ref.shape[0], k_ref.shape[1]
    qs, ws = _window(i, rows)
    s0 = starts_ref[i]
    e0 = ends_ref[i]

    @pl.when(s0 < e0)
    def _():
        allowed = _allowed(qs, ws, s0, e0)
        for h in range(heads):
            q = q_ref[h]
            k = k_ref[h, pl.ds(ws, LMAX), :]
            v = v_ref[h, pl.ds(ws, LMAX), :]
            s = lax.dot_general(q, k, (((1,), (1,)), ((), ())), preferred_element_type=jnp.float32)
            s = jnp.where(allowed, s, masked_score)
            m = jnp.max(s, axis=1, keepdims=True)
            p = jnp.exp(s - m)
            l = jnp.sum(p, axis=1, keepdims=True)
            probs = (p / l).astype(jnp.bfloat16)
            o = jnp.dot(probs, v, preferred_element_type=jnp.float32)
            o_ref[h] = o.astype(o_ref.dtype)
            lse_ref[h] = m + jnp.log(l)

    @pl.when(s0 >= e0)
    def _():
        o_ref[...] = jnp.zeros(o_ref.shape, o_ref.dtype)
        lse_ref[...] = jnp.zeros(lse_ref.shape, lse_ref.dtype)


def attn_bwd_kernel(starts_ref, ends_ref, q_ref, k_ref, v_ref, do_ref, lse_ref,
                    dq_ref, dk_ref, dv_ref, dk_acc, dv_acc):
    i = pl.program_id(0)
    heads, rows = k_ref.shape[0], k_ref.shape[1]
    qs, ws = _window(i, rows)
    s0 = starts_ref[i]
    e0 = ends_ref[i]

    @pl.when(i == 0)
    def _():
        dk_acc[...] = jnp.zeros(dk_acc.shape, dk_acc.dtype)
        dv_acc[...] = jnp.zeros(dv_acc.shape, dv_acc.dtype)

    @pl.when(s0 < e0)
    def _():
        allowed = _allowed(qs, ws, s0, e0)
        for h in range(heads):
            q = q_ref[h]
            k = k_ref[h, pl.ds(ws, LMAX), :]
            v = v_ref[h, pl.ds(ws, LMAX), :]
            do = do_ref[h]
            s = lax.dot_general(q, k, (((1,), (1,)), ((), ())), preferred_element_type=jnp.float32)
            s = jnp.where(allowed, s, masked_score)
            probs = jnp.exp(s - lse_ref[h])
            dp = lax.dot_general(do, v, (((1,), (1,)), ((), ())), preferred_element_type=jnp.float32)
            row_dot = jnp.sum(probs * dp, axis=1, keepdims=True)
            ds = (probs * (dp - row_dot)).astype(jnp.bfloat16)
            dq = jnp.dot(ds, k, preferred_element_type=jnp.float32)
            dq_ref[h] = dq.astype(dq_ref.dtype)
            dk_acc[h, pl.ds(ws, LMAX), :] += jnp.dot(ds.T, q, preferred_element_type=jnp.float32)
            dv_acc[h, pl.ds(ws, LMAX), :] += jnp.dot(
                probs.astype(jnp.bfloat16).T, do, preferred_element_type=jnp.float32
            )

    @pl.when(s0 >= e0)
    def _():
        dq_ref[...] = jnp.zeros(dq_ref.shape, dq_ref.dtype)

    @pl.when(i == pl.num_programs(0) - 1)
    def _():
        dk_ref[...] = dk_acc[...].astype(dk_ref.dtype)
        dv_ref[...] = dv_acc[...].astype(dv_ref.dtype)


def attention_forward(q, k, v, starts, ends):
    heads, rows, width = q.shape
    blocks = rows // TQ
    whole = pl.BlockSpec((heads, rows, width), lambda i, s, e: (0, 0, 0))
    part = pl.BlockSpec((heads, TQ, width), lambda i, s, e: (0, i, 0))
    flops = 4 * heads * rows * LMAX * width
    return pl.pallas_call(
        attn_fwd_kernel,
        grid_spec=pltpu.PrefetchScalarGridSpec(
            num_scalar_prefetch=2,
            grid=(blocks,),
            in_specs=[part, whole, whole],
            out_specs=[part, pl.BlockSpec((heads, TQ, 1), lambda i, s, e: (0, i, 0))],
        ),
        out_shape=[
            jax.ShapeDtypeStruct((heads, rows, width), jnp.bfloat16),
            jax.ShapeDtypeStruct((heads, rows, 1), jnp.float32),
        ],
        compiler_params=pltpu.CompilerParams(
            dimension_semantics=("arbitrary",), vmem_limit_bytes=48 * 1024 * 1024
        ),
        cost_estimate=pl.CostEstimate(
            flops=flops, transcendentals=heads * rows * LMAX, bytes_accessed=4 * q.size * 2
        ),
    )(starts, ends, q, k, v)


def attention_backward(q, k, v, do, lse, starts, ends):
    heads, rows, width = q.shape
    blocks = rows // TQ
    whole = pl.BlockSpec((heads, rows, width), lambda i, s, e: (0, 0, 0))
    part = pl.BlockSpec((heads, TQ, width), lambda i, s, e: (0, i, 0))
    flops = 10 * heads * rows * LMAX * width
    return pl.pallas_call(
        attn_bwd_kernel,
        grid_spec=pltpu.PrefetchScalarGridSpec(
            num_scalar_prefetch=2,
            grid=(blocks,),
            in_specs=[part, whole, whole, part, pl.BlockSpec((heads, TQ, 1), lambda i, s, e: (0, i, 0))],
            out_specs=[part, whole, whole],
            scratch_shapes=[
                pltpu.VMEM((heads, rows, width), jnp.float32),
                pltpu.VMEM((heads, rows, width), jnp.float32),
            ],
        ),
        out_shape=[jax.ShapeDtypeStruct((heads, rows, width), jnp.bfloat16)] * 3,
        compiler_params=pltpu.CompilerParams(
            dimension_semantics=("arbitrary",), vmem_limit_bytes=48 * 1024 * 1024
        ),
        cost_estimate=pl.CostEstimate(
            flops=flops, transcendentals=heads * rows * LMAX, bytes_accessed=7 * q.size * 2
        ),
    )(starts, ends, q, k, v, do, lse)


def per_device(
    tokens,
    cotangent,
    lengths,
    dealing,
    gain_one,
    gain_two,
    attention_in,
    query_scale,
    attention_out,
    hidden_in,
    hidden_out,
):
    out_all, in_all, down_all = (
        lax.all_gather(attention_out, "mp", axis=0, tiled=True),
        lax.all_gather(hidden_in, "mp", axis=0, tiled=True),
        lax.all_gather(hidden_out, "mp", axis=0, tiled=True),
    )
    row_count = tokens.shape[0]
    mp_count = lax.axis_size("mp")
    my_group = lax.axis_index("dp")
    my_part = lax.axis_index("mp")
    group_rows = row_count * mp_count
    series_grp = group_rows // LMAX
    heads_here = NH // mp_count
    width_here = heads_here * HD
    shard_width = D // mp_count
    maps = series_maps(lengths, dealing, series_grp, group_rows, my_group)
    send_first, send_len = maps[0], maps[1]
    place_slot, place_start, place_len = dealt_places(lengths, dealing, series_grp, my_group)
    src_len = lax.dynamic_slice_in_dim(lengths, my_group * series_grp, series_grp)
    block_start, block_end, src_live = block_bounds(src_len, group_rows)
    live_mine = lax.dynamic_slice_in_dim(src_live, my_part * row_count, row_count).astype(
        jnp.float32
    )[:, None]
    gain_rows = jnp.zeros((8, D), jnp.bfloat16)
    gain_rows = gain_rows.at[0, :shard_width].set(gain_one).at[0, shard_width : 2 * shard_width].set(gain_two)
    packed = lax.all_gather(jnp.concatenate([tokens, gain_rows]), "mp", axis=0, tiled=False)
    gain_first = packed[:, row_count, :shard_width].reshape(D).astype(jnp.float32)
    gain_second = packed[:, row_count, shard_width : 2 * shard_width].reshape(D).astype(jnp.float32)
    inputs_group = packed[:, :row_count].reshape(group_rows, D).astype(jnp.float32)
    inv_group = lax.rsqrt(jnp.mean(inputs_group * inputs_group, axis=1, keepdims=True) + epsilon)
    normed_group = (inputs_group * inv_group * gain_first).astype(jnp.bfloat16)
    inputs = tokens.astype(jnp.float32)
    inv_one = lax.rsqrt(jnp.mean(inputs * inputs, axis=1, keepdims=True) + epsilon)
    weight_heads = attention_in.reshape(heads_here, HD, 3, D)
    projected = jnp.einsum(
        "rd,hecd->chre", normed_group, weight_heads, preferred_element_type=jnp.float32
    )
    dim_scale = scale_base / math.sqrt(HD) * jax.nn.softplus(query_scale)
    query_raw = projected[0]
    queries = (query_raw * dim_scale).astype(jnp.bfloat16)
    keys = projected[1].astype(jnp.bfloat16)
    values = projected[2].astype(jnp.bfloat16)
    mixed, log_total = attention_forward(queries, keys, values, block_start, block_end)
    kv_heads, mixed = lax.optimization_barrier((jnp.stack([keys, values]), mixed))
    kv_rows = kv_heads.transpose(0, 2, 1, 3).reshape(2, group_rows, width_here)
    groups = lax.axis_size("dp")
    windows = send_windows(kv_rows, send_first, send_len, my_group, groups)
    received = [windows[0]] + [
        lax.ppermute(
            windows[shift], "dp", [(r, (r + shift) % groups) for r in range(groups)]
        )
        for shift in range(1, groups)
    ]
    place_shift = (my_group - place_slot) % groups
    cache = place_slots(received, place_shift, place_start, place_len, group_rows)
    att_group = jnp.where(src_live[None, :, None], mixed, jnp.zeros((), jnp.bfloat16))
    att_heads = lax.all_to_all(att_group, "mp", split_axis=1, concat_axis=0, tiled=True)
    out_heads = out_all.reshape(NH, HD, D)
    branch = jnp.einsum("hie,hed->id", att_heads, out_heads, preferred_element_type=jnp.float32)
    first_sum = inputs + branch
    inv_two = lax.rsqrt(jnp.mean(first_sum * first_sum, axis=1, keepdims=True) + epsilon)
    normed_two = (first_sum * inv_two * gain_second).astype(jnp.bfloat16)
    preact = jnp.einsum("rd,fd->rf", normed_two, in_all, preferred_element_type=jnp.float32)
    hidden = jax.nn.silu(preact).astype(jnp.bfloat16)
    feed = jnp.dot(hidden, down_all, preferred_element_type=jnp.float32)
    layer_out = ((first_sum + feed) * live_mine).astype(jnp.bfloat16)
    out_grad = cotangent.astype(jnp.float32) * live_mine
    feed_grad = out_grad.astype(jnp.bfloat16)
    hidden_grad = jnp.einsum("rd,fd->rf", feed_grad, down_all, preferred_element_type=jnp.float32)
    gate_sig = jax.nn.sigmoid(preact)
    preact_grad = (hidden_grad * gate_sig * (1.0 + preact * (1.0 - gate_sig))).astype(jnp.bfloat16)
    normed_two_grad = jnp.dot(preact_grad, in_all, preferred_element_type=jnp.float32)
    scaled_two = gain_second * normed_two_grad
    first_grad = (
        out_grad
        + inv_two * scaled_two
        - first_sum * inv_two**3 * jnp.mean(scaled_two * first_sum, axis=1, keepdims=True)
    )
    branch_grad = first_grad.astype(jnp.bfloat16)
    att_heads_grad = jnp.einsum(
        "id,hed->hie", branch_grad, out_heads, preferred_element_type=jnp.float32
    ).astype(jnp.bfloat16)
    grad_group = lax.all_to_all(att_heads_grad, "mp", split_axis=0, concat_axis=1, tiled=True)
    grad_heads = jnp.where(src_live[None, :, None], grad_group, jnp.zeros((), jnp.bfloat16))
    query_scaled_grad, key_grad, value_grad = attention_backward(
        queries, keys, values, grad_heads, log_total, block_start, block_end
    )
    live_heads = src_live[None, :, None]
    query_scaled_grad = jnp.where(live_heads, query_scaled_grad, jnp.zeros((), jnp.bfloat16)).astype(
        jnp.float32
    )
    scale_part = (
        jnp.sum(query_scaled_grad * query_raw, axis=(0, 1))
        * (scale_base / math.sqrt(HD))
        * jax.nn.sigmoid(query_scale)
    )
    query_grad = (query_scaled_grad * dim_scale).astype(jnp.bfloat16)
    proj_grad = (
        query_grad,
        jnp.where(live_heads, key_grad, jnp.zeros((), jnp.bfloat16)),
        jnp.where(live_heads, value_grad, jnp.zeros((), jnp.bfloat16)),
    )
    qkv_part = jnp.stack(
        [
            jnp.einsum("hre,rd->hed", g, normed_group, preferred_element_type=jnp.float32)
            for g in proj_grad
        ],
        axis=2,
    ).reshape(width_here, 3, D)
    normed_one_part = sum(
        jnp.einsum("hre,hed->rd", g, weight_heads[:, :, c], preferred_element_type=jnp.float32)
        for c, g in enumerate(proj_grad)
    )
    normed_one_grad = lax.psum_scatter(
        normed_one_part.astype(jnp.bfloat16), "mp", scatter_dimension=0, tiled=True
    ).astype(jnp.float32)
    scaled_one = gain_first * normed_one_grad
    tokens_grad = (
        first_grad
        + inv_one * scaled_one
        - inputs * inv_one**3 * jnp.mean(scaled_one * inputs, axis=1, keepdims=True)
    )
    gain_one_part = jnp.sum(normed_one_part * inputs_group * inv_group, axis=0)
    gain_two_part = jnp.sum(normed_two_grad * first_sum * inv_two, axis=0)
    small = jnp.concatenate(
        [
            gain_one_part.reshape(mp_count, shard_width),
            gain_two_part.reshape(mp_count, shard_width),
            jnp.broadcast_to(scale_part, (mp_count, HD)),
        ],
        axis=1,
    )
    small = lax.psum(lax.psum_scatter(small, "mp", scatter_dimension=0, tiled=True), "dp")
    gain_one_grad = small[0, :shard_width]
    gain_two_grad = small[0, shard_width : 2 * shard_width]
    query_scale_grad = small[0, 2 * shard_width :]
    out_part = jnp.einsum(
        "hie,id->hed", att_heads, branch_grad, preferred_element_type=jnp.float32
    ).reshape(D, D)
    in_part = jnp.einsum("ru,rd->ud", preact_grad, normed_two, preferred_element_type=jnp.float32)
    down_part = jnp.einsum("ru,rd->ud", hidden, feed_grad, preferred_element_type=jnp.float32)
    row_terms = jnp.stack([out_part, in_part, down_part], axis=1)
    shares = lax.psum_scatter(
        row_terms.astype(jnp.bfloat16), "mp", scatter_dimension=0, tiled=True
    )
    totals = lax.psum(
        jnp.concatenate([qkv_part.astype(jnp.bfloat16), shares], axis=1), "dp"
    ).astype(jnp.float32)
    return (
        layer_out,
        tokens_grad,
        cache,
        gain_one_grad,
        gain_two_grad,
        totals[:, 0:3],
        query_scale_grad,
        totals[:, 3],
        totals[:, 4],
        totals[:, 5],
    )


def solution(mesh):
    placed = (
        P(("dp", "mp"), None),
        P(("dp", "mp"), None),
        P(),
        P(),
        P("mp"),
        P("mp"),
        P("mp", None, None),
        P(),
        P("mp", None),
        P("mp", None),
        P("mp", None),
    )
    return jax.shard_map(
        per_device,
        mesh=mesh,
        in_specs=placed,
        out_specs=(
            P(("dp", "mp"), None),
            P(("dp", "mp"), None),
            P(None, "dp", "mp"),
            P("mp"),
            P("mp"),
            P("mp", None, None),
            P(),
            P("mp", None),
            P("mp", None),
            P("mp", None),
        ),
        check_vma=False,
    )
```

```python
import math

import jax
import jax.numpy as jnp
from jax import lax
from jax.experimental import pallas as pl
from jax.experimental.pallas import tpu as pltpu
from jax.sharding import PartitionSpec as P


D = 1280
NH = 16
HD = 80
LMAX = 1024
BLK = 128
TQ = 128


epsilon = 1e-06
scale_base = 1.442695041
masked_score = -1e30


def lookup(values_table, positions):
    entries = jnp.arange(values_table.shape[0], dtype=jnp.int32)
    picked = jnp.where(positions[:, None] == entries[None, :], values_table[None, :], 0)
    return jnp.sum(picked, axis=1)


def packing(span_len, group_rows):
    blocks = (span_len + BLK - 1) // BLK
    block_ends = BLK * jnp.cumsum(blocks)
    starts = block_ends - BLK * blocks
    in_group = jnp.arange(group_rows, dtype=jnp.int32)
    series_at = jnp.sum((block_ends[None, :] <= in_group[:, None]).astype(jnp.int32), axis=1)
    capped = jnp.minimum(series_at, span_len.shape[0] - 1)
    offset = in_group - lookup(starts, capped)
    live_row = (series_at < span_len.shape[0]) & (offset < lookup(span_len, capped))
    return (starts, series_at, capped, offset, live_row)


def slot_table(slot_of, starts, span_len, slot_count):
    entries = jnp.arange(slot_count, dtype=jnp.int32)
    matched = slot_of[None, :] == entries[:, None]
    slot_first = jnp.sum(jnp.where(matched, starts[None, :], 0), axis=1)
    slot_length = jnp.sum(jnp.where(matched, span_len[None, :], 0), axis=1)
    return (slot_first, slot_length)


def series_maps(lengths, dealing, series_grp, group_rows, my_group):
    groups = lengths.shape[0] // series_grp
    capacity = (series_grp + groups - 1) // groups
    places = jnp.arange(series_grp, dtype=jnp.int32)
    target = dealing.reshape(groups, series_grp) // series_grp
    earlier = (target[:, :, None] == target[:, None, :]) & (
        places[None, None, :] < places[None, :, None]
    )
    rank_of = jnp.sum(earlier.astype(jnp.int32), axis=2)
    slot_of = (target * capacity + rank_of).reshape(-1)
    rank_flat = rank_of.reshape(-1)
    src_len = lax.dynamic_slice_in_dim(lengths, my_group * series_grp, series_grp)
    src_slot = lax.dynamic_slice_in_dim(slot_of, my_group * series_grp, series_grp)
    src_starts, _, src_capped, src_offset, src_live = packing(src_len, group_rows)
    dealt_places = jnp.arange(lengths.shape[0], dtype=jnp.int32)
    owner = jnp.sum(
        jnp.where(dealing[None, :] == dealt_places[:, None], dealt_places[None, :], 0), axis=1
    )
    my_series = lax.dynamic_slice_in_dim(owner, my_group * series_grp, series_grp)
    dst_len = lookup(lengths, my_series)
    dst_slot = my_series // series_grp * capacity + lookup(rank_flat, my_series)
    dst_starts, dst_at, dst_capped, dst_offset, dst_live = packing(dst_len, group_rows)
    slot_count = groups * capacity
    send_first, send_len = slot_table(src_slot, src_starts, src_len, slot_count)
    back_first, back_len = slot_table(dst_slot, dst_starts, dst_len, slot_count)
    src_index = lookup(src_slot, src_capped) * LMAX + src_offset
    dst_index = lookup(dst_slot, dst_capped) * LMAX + dst_offset
    key_live = jnp.where(dst_at < series_grp, dst_live, True)
    return (
        send_first,
        send_len,
        back_first,
        back_len,
        src_index,
        src_live,
        dst_index,
        dst_live,
        dst_at,
        key_live,
    )


def send_windows(values, slot_first, slot_length, my_group, groups):
    padded = jnp.pad(values, ((0, 0), (0, LMAX), (0, 0)))
    positions = jnp.arange(LMAX, dtype=jnp.int32)[None, :, None]
    windows = []
    for shift in range(groups):
        target = (my_group + shift) % groups
        window = lax.dynamic_slice_in_dim(padded, slot_first[target], LMAX, axis=1)
        windows.append(
            jnp.where(positions < slot_length[target], window, jnp.zeros((), values.dtype))
        )
    return windows


def place_slots(received, place_shift, place_start, place_len, out_rows):
    stacked = jnp.stack(received)
    rows = jnp.arange(out_rows, dtype=jnp.int32)[None, :, None]
    placed = jnp.zeros((stacked.shape[1], out_rows, stacked.shape[3]), stacked.dtype)
    for q in range(place_shift.shape[0]):
        window = lax.dynamic_index_in_dim(stacked, place_shift[q], axis=0, keepdims=False)
        padded = jnp.pad(window, ((0, 0), (out_rows, out_rows - LMAX), (0, 0)))
        shifted = lax.dynamic_slice_in_dim(padded, out_rows - place_start[q], out_rows, axis=1)
        inside = (rows >= place_start[q]) & (rows < place_start[q] + place_len[q])
        placed = jnp.where(inside, shifted, placed)
    return placed


def dealt_places(lengths, dealing, series_grp, my_group):
    dealt_places = jnp.arange(lengths.shape[0], dtype=jnp.int32)
    owner = jnp.sum(
        jnp.where(dealing[None, :] == dealt_places[:, None], dealt_places[None, :], 0), axis=1
    )
    my_series = lax.dynamic_slice_in_dim(owner, my_group * series_grp, series_grp)
    place_len = lookup(lengths, my_series)
    blocks = (place_len + BLK - 1) // BLK
    place_start = BLK * jnp.cumsum(blocks) - BLK * blocks
    return my_series // series_grp, place_start, place_len


def block_bounds(src_len, group_rows):
    starts, series_at, _, _, live_row = packing(src_len, group_rows)
    first_rows = jnp.arange(group_rows // TQ, dtype=jnp.int32) * TQ
    seg = series_at[first_rows]
    inside = seg < src_len.shape[0]
    seg_c = jnp.minimum(seg, src_len.shape[0] - 1)
    block_start = jnp.where(inside, lookup(starts, seg_c), 0)
    block_end = jnp.where(inside, block_start + lookup(src_len, seg_c), 0)
    return block_start.astype(jnp.int32), block_end.astype(jnp.int32), live_row


def _window(i, rows, width):
    qs = i * TQ
    ws = jnp.minimum(jnp.maximum(qs - (width - TQ), 0), rows - width)
    return qs, pl.multiple_of(ws, TQ)


def _allowed(qs, ws, s0, e0, width):
    a = qs + lax.broadcasted_iota(jnp.int32, (TQ, width), 0)
    b = ws + lax.broadcasted_iota(jnp.int32, (TQ, width), 1)
    return (b >= s0) & (b <= a) & (b < e0)


def _fwd_block(i, s0, e0, q_ref, k_ref, v_ref, o_ref, lse_ref, width):
    heads, rows = k_ref.shape[0], k_ref.shape[1]
    qs, ws = _window(i, rows, width)
    allowed = _allowed(qs, ws, s0, e0, width)
    for h in range(heads):
        q = q_ref[h]
        k = k_ref[h, pl.ds(ws, width), :]
        v = v_ref[h, pl.ds(ws, width), :]
        s = lax.dot_general(q, k, (((1,), (1,)), ((), ())), preferred_element_type=jnp.float32)
        s = jnp.where(allowed, s, masked_score)
        m = jnp.max(s, axis=1, keepdims=True)
        p = jnp.exp(s - m)
        l = jnp.sum(p, axis=1, keepdims=True)
        probs = (p / l).astype(jnp.bfloat16)
        o = jnp.dot(probs, v, preferred_element_type=jnp.float32)
        o_ref[h] = o.astype(o_ref.dtype)
        lse_ref[h] = m + jnp.log(l)


def attn_fwd_kernel(starts_ref, ends_ref, q_ref, k_ref, v_ref, o_ref, lse_ref):
    i = pl.program_id(0)
    s0 = starts_ref[i]
    e0 = ends_ref[i]
    short = i * TQ + TQ - s0 <= LMAX // 2

    @pl.when((s0 < e0) & short)
    def _():
        _fwd_block(i, s0, e0, q_ref, k_ref, v_ref, o_ref, lse_ref, LMAX // 2)

    @pl.when((s0 < e0) & jnp.logical_not(short))
    def _():
        _fwd_block(i, s0, e0, q_ref, k_ref, v_ref, o_ref, lse_ref, LMAX)

    @pl.when(s0 >= e0)
    def _():
        o_ref[...] = jnp.zeros(o_ref.shape, o_ref.dtype)
        lse_ref[...] = jnp.zeros(lse_ref.shape, lse_ref.dtype)


def _bwd_block(i, s0, e0, q_ref, k_ref, v_ref, do_ref, lse_ref, dq_ref, dk_acc, dv_acc, width):
    heads, rows = k_ref.shape[0], k_ref.shape[1]
    qs, ws = _window(i, rows, width)
    allowed = _allowed(qs, ws, s0, e0, width)
    for h in range(heads):
        q = q_ref[h]
        k = k_ref[h, pl.ds(ws, width), :]
        v = v_ref[h, pl.ds(ws, width), :]
        do = do_ref[h]
        s = lax.dot_general(q, k, (((1,), (1,)), ((), ())), preferred_element_type=jnp.float32)
        s = jnp.where(allowed, s, masked_score)
        probs = jnp.exp(s - lse_ref[h])
        dp = lax.dot_general(do, v, (((1,), (1,)), ((), ())), preferred_element_type=jnp.float32)
        row_dot = jnp.sum(probs * dp, axis=1, keepdims=True)
        ds = (probs * (dp - row_dot)).astype(jnp.bfloat16)
        dq = jnp.dot(ds, k, preferred_element_type=jnp.float32)
        dq_ref[h] = dq.astype(dq_ref.dtype)
        dk_acc[h, pl.ds(ws, width), :] += jnp.dot(ds.T, q, preferred_element_type=jnp.float32)
        dv_acc[h, pl.ds(ws, width), :] += jnp.dot(
            probs.astype(jnp.bfloat16).T, do, preferred_element_type=jnp.float32
        )


def attn_bwd_kernel(starts_ref, ends_ref, q_ref, k_ref, v_ref, do_ref, lse_ref,
                    dq_ref, dk_ref, dv_ref, dk_acc, dv_acc):
    i = pl.program_id(0)
    s0 = starts_ref[i]
    e0 = ends_ref[i]
    short = i * TQ + TQ - s0 <= LMAX // 2

    @pl.when(i == 0)
    def _():
        dk_acc[...] = jnp.zeros(dk_acc.shape, dk_acc.dtype)
        dv_acc[...] = jnp.zeros(dv_acc.shape, dv_acc.dtype)

    @pl.when((s0 < e0) & short)
    def _():
        _bwd_block(i, s0, e0, q_ref, k_ref, v_ref, do_ref, lse_ref, dq_ref, dk_acc, dv_acc, LMAX // 2)

    @pl.when((s0 < e0) & jnp.logical_not(short))
    def _():
        _bwd_block(i, s0, e0, q_ref, k_ref, v_ref, do_ref, lse_ref, dq_ref, dk_acc, dv_acc, LMAX)

    @pl.when(s0 >= e0)
    def _():
        dq_ref[...] = jnp.zeros(dq_ref.shape, dq_ref.dtype)

    @pl.when(i == pl.num_programs(0) - 1)
    def _():
        dk_ref[...] = dk_acc[...].astype(dk_ref.dtype)
        dv_ref[...] = dv_acc[...].astype(dv_ref.dtype)


def attention_forward(q, k, v, starts, ends):
    heads, rows, width = q.shape
    blocks = rows // TQ
    whole = pl.BlockSpec((heads, rows, width), lambda i, s, e: (0, 0, 0))
    part = pl.BlockSpec((heads, TQ, width), lambda i, s, e: (0, i, 0))
    flops = 4 * heads * rows * LMAX * width
    return pl.pallas_call(
        attn_fwd_kernel,
        grid_spec=pltpu.PrefetchScalarGridSpec(
            num_scalar_prefetch=2,
            grid=(blocks,),
            in_specs=[part, whole, whole],
            out_specs=[part, pl.BlockSpec((heads, TQ, 1), lambda i, s, e: (0, i, 0))],
        ),
        out_shape=[
            jax.ShapeDtypeStruct((heads, rows, width), jnp.bfloat16),
            jax.ShapeDtypeStruct((heads, rows, 1), jnp.float32),
        ],
        compiler_params=pltpu.CompilerParams(
            dimension_semantics=("arbitrary",), vmem_limit_bytes=48 * 1024 * 1024
        ),
        cost_estimate=pl.CostEstimate(
            flops=flops, transcendentals=heads * rows * LMAX, bytes_accessed=4 * q.size * 2
        ),
    )(starts, ends, q, k, v)


def attention_backward(q, k, v, do, lse, starts, ends):
    heads, rows, width = q.shape
    blocks = rows // TQ
    whole = pl.BlockSpec((heads, rows, width), lambda i, s, e: (0, 0, 0))
    part = pl.BlockSpec((heads, TQ, width), lambda i, s, e: (0, i, 0))
    flops = 10 * heads * rows * LMAX * width
    return pl.pallas_call(
        attn_bwd_kernel,
        grid_spec=pltpu.PrefetchScalarGridSpec(
            num_scalar_prefetch=2,
            grid=(blocks,),
            in_specs=[part, whole, whole, part, pl.BlockSpec((heads, TQ, 1), lambda i, s, e: (0, i, 0))],
            out_specs=[part, whole, whole],
            scratch_shapes=[
                pltpu.VMEM((heads, rows, width), jnp.float32),
                pltpu.VMEM((heads, rows, width), jnp.float32),
            ],
        ),
        out_shape=[jax.ShapeDtypeStruct((heads, rows, width), jnp.bfloat16)] * 3,
        compiler_params=pltpu.CompilerParams(
            dimension_semantics=("arbitrary",), vmem_limit_bytes=48 * 1024 * 1024
        ),
        cost_estimate=pl.CostEstimate(
            flops=flops, transcendentals=heads * rows * LMAX, bytes_accessed=7 * q.size * 2
        ),
    )(starts, ends, q, k, v, do, lse)


def per_device(
    tokens,
    cotangent,
    lengths,
    dealing,
    gain_one,
    gain_two,
    attention_in,
    query_scale,
    attention_out,
    hidden_in,
    hidden_out,
):
    out_all, in_all, down_all = (
        lax.all_gather(attention_out, "mp", axis=0, tiled=True),
        lax.all_gather(hidden_in, "mp", axis=0, tiled=True),
        lax.all_gather(hidden_out, "mp", axis=0, tiled=True),
    )
    row_count = tokens.shape[0]
    mp_count = lax.axis_size("mp")
    my_group = lax.axis_index("dp")
    my_part = lax.axis_index("mp")
    group_rows = row_count * mp_count
    series_grp = group_rows // LMAX
    heads_here = NH // mp_count
    width_here = heads_here * HD
    shard_width = D // mp_count
    maps = series_maps(lengths, dealing, series_grp, group_rows, my_group)
    send_first, send_len = maps[0], maps[1]
    place_slot, place_start, place_len = dealt_places(lengths, dealing, series_grp, my_group)
    src_len = lax.dynamic_slice_in_dim(lengths, my_group * series_grp, series_grp)
    block_start, block_end, src_live = block_bounds(src_len, group_rows)
    live_mine = lax.dynamic_slice_in_dim(src_live, my_part * row_count, row_count).astype(
        jnp.float32
    )[:, None]
    gain_rows = jnp.zeros((8, D), jnp.bfloat16)
    gain_rows = gain_rows.at[0, :shard_width].set(gain_one).at[0, shard_width : 2 * shard_width].set(gain_two)
    packed = lax.all_gather(jnp.concatenate([tokens, gain_rows]), "mp", axis=0, tiled=False)
    gain_first = packed[:, row_count, :shard_width].reshape(D).astype(jnp.float32)
    gain_second = packed[:, row_count, shard_width : 2 * shard_width].reshape(D).astype(jnp.float32)
    inputs_group = packed[:, :row_count].reshape(group_rows, D).astype(jnp.float32)
    inv_group = lax.rsqrt(jnp.mean(inputs_group * inputs_group, axis=1, keepdims=True) + epsilon)
    normed_group = (inputs_group * inv_group * gain_first).astype(jnp.bfloat16)
    inputs = tokens.astype(jnp.float32)
    inv_one = lax.rsqrt(jnp.mean(inputs * inputs, axis=1, keepdims=True) + epsilon)
    weight_heads = attention_in.reshape(heads_here, HD, 3, D)
    projected = jnp.einsum(
        "rd,hecd->chre", normed_group, weight_heads, preferred_element_type=jnp.float32
    )
    dim_scale = scale_base / math.sqrt(HD) * jax.nn.softplus(query_scale)
    query_raw = projected[0]
    queries = (query_raw * dim_scale).astype(jnp.bfloat16)
    keys = projected[1].astype(jnp.bfloat16)
    values = projected[2].astype(jnp.bfloat16)
    kv_rows = jnp.stack([keys, values]).transpose(0, 2, 1, 3).reshape(2, group_rows, width_here)
    groups = lax.axis_size("dp")
    windows = send_windows(kv_rows, send_first, send_len, my_group, groups)
    received = [windows[0]] + [
        lax.ppermute(
            windows[shift], "dp", [(r, (r + shift) % groups) for r in range(groups)]
        )
        for shift in range(1, groups)
    ]
    place_shift = (my_group - place_slot) % groups
    cache = place_slots(received, place_shift, place_start, place_len, group_rows)
    mixed, log_total = attention_forward(queries, keys, values, block_start, block_end)
    att_group = jnp.where(src_live[None, :, None], mixed, jnp.zeros((), jnp.bfloat16))
    att_heads = lax.all_to_all(att_group, "mp", split_axis=1, concat_axis=0, tiled=True)
    out_heads = out_all.reshape(NH, HD, D)
    branch = jnp.einsum("hie,hed->id", att_heads, out_heads, preferred_element_type=jnp.float32)
    first_sum = inputs + branch
    inv_two = lax.rsqrt(jnp.mean(first_sum * first_sum, axis=1, keepdims=True) + epsilon)
    normed_two = (first_sum * inv_two * gain_second).astype(jnp.bfloat16)
    preact = jnp.einsum("rd,fd->rf", normed_two, in_all, preferred_element_type=jnp.float32)
    hidden = jax.nn.silu(preact).astype(jnp.bfloat16)
    feed = jnp.dot(hidden, down_all, preferred_element_type=jnp.float32)
    layer_out = ((first_sum + feed) * live_mine).astype(jnp.bfloat16)
    out_grad = cotangent.astype(jnp.float32) * live_mine
    feed_grad = out_grad.astype(jnp.bfloat16)
    hidden_grad = jnp.einsum("rd,fd->rf", feed_grad, down_all, preferred_element_type=jnp.float32)
    gate_sig = jax.nn.sigmoid(preact)
    preact_grad = (hidden_grad * gate_sig * (1.0 + preact * (1.0 - gate_sig))).astype(jnp.bfloat16)
    normed_two_grad = jnp.dot(preact_grad, in_all, preferred_element_type=jnp.float32)
    scaled_two = gain_second * normed_two_grad
    first_grad = (
        out_grad
        + inv_two * scaled_two
        - first_sum * inv_two**3 * jnp.mean(scaled_two * first_sum, axis=1, keepdims=True)
    )
    branch_grad = first_grad.astype(jnp.bfloat16)
    att_heads_grad = jnp.einsum(
        "id,hed->hie", branch_grad, out_heads, preferred_element_type=jnp.float32
    ).astype(jnp.bfloat16)
    grad_group = lax.all_to_all(att_heads_grad, "mp", split_axis=0, concat_axis=1, tiled=True)
    grad_heads = jnp.where(src_live[None, :, None], grad_group, jnp.zeros((), jnp.bfloat16))
    query_scaled_grad, key_grad, value_grad = attention_backward(
        queries, keys, values, grad_heads, log_total, block_start, block_end
    )
    live_heads = src_live[None, :, None]
    query_scaled_grad = jnp.where(live_heads, query_scaled_grad, jnp.zeros((), jnp.bfloat16)).astype(
        jnp.float32
    )
    scale_part = (
        jnp.sum(query_scaled_grad * query_raw, axis=(0, 1))
        * (scale_base / math.sqrt(HD))
        * jax.nn.sigmoid(query_scale)
    )
    query_grad = (query_scaled_grad * dim_scale).astype(jnp.bfloat16)
    proj_grad = jnp.stack(
        [
            query_grad,
            jnp.where(live_heads, key_grad, jnp.zeros((), jnp.bfloat16)),
            jnp.where(live_heads, value_grad, jnp.zeros((), jnp.bfloat16)),
        ]
    )
    qkv_part = jnp.einsum(
        "chre,rd->hecd", proj_grad, normed_group, preferred_element_type=jnp.float32
    ).reshape(width_here, 3, D)
    normed_one_part = jnp.einsum(
        "chre,hecd->rd", proj_grad, weight_heads, preferred_element_type=jnp.float32
    )
    normed_one_grad = lax.psum_scatter(
        normed_one_part.astype(jnp.bfloat16), "mp", scatter_dimension=0, tiled=True
    ).astype(jnp.float32)
    scaled_one = gain_first * normed_one_grad
    tokens_grad = (
        first_grad
        + inv_one * scaled_one
        - inputs * inv_one**3 * jnp.mean(scaled_one * inputs, axis=1, keepdims=True)
    )
    gain_one_part = jnp.sum(normed_one_part * inputs_group * inv_group, axis=0)
    gain_two_part = jnp.sum(normed_two_grad * first_sum * inv_two, axis=0)
    small = jnp.concatenate(
        [
            gain_one_part.reshape(mp_count, shard_width),
            gain_two_part.reshape(mp_count, shard_width),
            jnp.broadcast_to(scale_part, (mp_count, HD)),
        ],
        axis=1,
    )
    small = lax.psum(lax.psum_scatter(small, "mp", scatter_dimension=0, tiled=True), "dp")
    gain_one_grad = small[0, :shard_width]
    gain_two_grad = small[0, shard_width : 2 * shard_width]
    query_scale_grad = small[0, 2 * shard_width :]
    out_part = jnp.einsum(
        "hie,id->hed", att_heads, branch_grad, preferred_element_type=jnp.float32
    ).reshape(D, D)
    in_part = jnp.einsum("ru,rd->ud", preact_grad, normed_two, preferred_element_type=jnp.float32)
    down_part = jnp.einsum("ru,rd->ud", hidden, feed_grad, preferred_element_type=jnp.float32)
    row_terms = jnp.stack([out_part, in_part, down_part], axis=1)
    shares = lax.psum_scatter(
        row_terms.astype(jnp.bfloat16), "mp", scatter_dimension=0, tiled=True
    )
    totals = lax.psum(
        jnp.concatenate([qkv_part.astype(jnp.bfloat16), shares], axis=1), "dp"
    ).astype(jnp.float32)
    return (
        layer_out,
        tokens_grad,
        cache,
        gain_one_grad,
        gain_two_grad,
        totals[:, 0:3],
        query_scale_grad,
        totals[:, 3],
        totals[:, 4],
        totals[:, 5],
    )


def solution(mesh):
    placed = (
        P(("dp", "mp"), None),
        P(("dp", "mp"), None),
        P(),
        P(),
        P("mp"),
        P("mp"),
        P("mp", None, None),
        P(),
        P("mp", None),
        P("mp", None),
        P("mp", None),
    )
    return jax.shard_map(
        per_device,
        mesh=mesh,
        in_specs=placed,
        out_specs=(
            P(("dp", "mp"), None),
            P(("dp", "mp"), None),
            P(None, "dp", "mp"),
            P("mp"),
            P("mp"),
            P("mp", None, None),
            P(),
            P("mp", None),
            P("mp", None),
            P("mp", None),
        ),
        check_vma=False,
    )
```

```python
import math

import jax
import jax.numpy as jnp
from jax import lax
from jax.experimental import pallas as pl
from jax.experimental.pallas import tpu as pltpu
from jax.sharding import PartitionSpec as P


D = 1280
NH = 16
HD = 80
LMAX = 1024
BLK = 128
TQ = 128


epsilon = 1e-06
scale_base = 1.442695041
masked_score = -1e30


def lookup(values_table, positions):
    entries = jnp.arange(values_table.shape[0], dtype=jnp.int32)
    picked = jnp.where(positions[:, None] == entries[None, :], values_table[None, :], 0)
    return jnp.sum(picked, axis=1)


def packing(span_len, group_rows):
    blocks = (span_len + BLK - 1) // BLK
    block_ends = BLK * jnp.cumsum(blocks)
    starts = block_ends - BLK * blocks
    in_group = jnp.arange(group_rows, dtype=jnp.int32)
    series_at = jnp.sum((block_ends[None, :] <= in_group[:, None]).astype(jnp.int32), axis=1)
    capped = jnp.minimum(series_at, span_len.shape[0] - 1)
    offset = in_group - lookup(starts, capped)
    live_row = (series_at < span_len.shape[0]) & (offset < lookup(span_len, capped))
    return (starts, series_at, capped, offset, live_row)


def slot_table(slot_of, starts, span_len, slot_count):
    entries = jnp.arange(slot_count, dtype=jnp.int32)
    matched = slot_of[None, :] == entries[:, None]
    slot_first = jnp.sum(jnp.where(matched, starts[None, :], 0), axis=1)
    slot_length = jnp.sum(jnp.where(matched, span_len[None, :], 0), axis=1)
    return (slot_first, slot_length)


def series_maps(lengths, dealing, series_grp, group_rows, my_group):
    groups = lengths.shape[0] // series_grp
    capacity = (series_grp + groups - 1) // groups
    places = jnp.arange(series_grp, dtype=jnp.int32)
    target = dealing.reshape(groups, series_grp) // series_grp
    earlier = (target[:, :, None] == target[:, None, :]) & (
        places[None, None, :] < places[None, :, None]
    )
    rank_of = jnp.sum(earlier.astype(jnp.int32), axis=2)
    slot_of = (target * capacity + rank_of).reshape(-1)
    rank_flat = rank_of.reshape(-1)
    src_len = lax.dynamic_slice_in_dim(lengths, my_group * series_grp, series_grp)
    src_slot = lax.dynamic_slice_in_dim(slot_of, my_group * series_grp, series_grp)
    src_starts, _, src_capped, src_offset, src_live = packing(src_len, group_rows)
    dealt_places = jnp.arange(lengths.shape[0], dtype=jnp.int32)
    owner = jnp.sum(
        jnp.where(dealing[None, :] == dealt_places[:, None], dealt_places[None, :], 0), axis=1
    )
    my_series = lax.dynamic_slice_in_dim(owner, my_group * series_grp, series_grp)
    dst_len = lookup(lengths, my_series)
    dst_slot = my_series // series_grp * capacity + lookup(rank_flat, my_series)
    dst_starts, dst_at, dst_capped, dst_offset, dst_live = packing(dst_len, group_rows)
    slot_count = groups * capacity
    send_first, send_len = slot_table(src_slot, src_starts, src_len, slot_count)
    back_first, back_len = slot_table(dst_slot, dst_starts, dst_len, slot_count)
    src_index = lookup(src_slot, src_capped) * LMAX + src_offset
    dst_index = lookup(dst_slot, dst_capped) * LMAX + dst_offset
    key_live = jnp.where(dst_at < series_grp, dst_live, True)
    return (
        send_first,
        send_len,
        back_first,
        back_len,
        src_index,
        src_live,
        dst_index,
        dst_live,
        dst_at,
        key_live,
    )


def send_windows(values, slot_first, slot_length, my_group, groups):
    padded = jnp.pad(values, ((0, 0), (0, LMAX), (0, 0)))
    positions = jnp.arange(LMAX, dtype=jnp.int32)[None, :, None]
    windows = []
    for shift in range(groups):
        target = (my_group + shift) % groups
        window = lax.dynamic_slice_in_dim(padded, slot_first[target], LMAX, axis=1)
        windows.append(
            jnp.where(positions < slot_length[target], window, jnp.zeros((), values.dtype))
        )
    return windows


def place_slots(received, place_shift, place_start, place_len, out_rows):
    stacked = jnp.stack(received)
    rows = jnp.arange(out_rows, dtype=jnp.int32)[None, :, None]
    placed = jnp.zeros((stacked.shape[1], out_rows, stacked.shape[3]), stacked.dtype)
    for q in range(place_shift.shape[0]):
        window = lax.dynamic_index_in_dim(stacked, place_shift[q], axis=0, keepdims=False)
        padded = jnp.pad(window, ((0, 0), (out_rows, out_rows - LMAX), (0, 0)))
        shifted = lax.dynamic_slice_in_dim(padded, out_rows - place_start[q], out_rows, axis=1)
        inside = (rows >= place_start[q]) & (rows < place_start[q] + place_len[q])
        placed = jnp.where(inside, shifted, placed)
    return placed


def pair_then_line_sum(values, axis, count):
    me = lax.axis_index(axis)
    half = values.shape[0] // 2
    pairs = [(r, r ^ 1) for r in range(count)]
    mine = lax.dynamic_slice_in_dim(values, (me % 2) * half, half, 0)
    other = lax.dynamic_slice_in_dim(values, (1 - me % 2) * half, half, 0)
    got = lax.ppermute(other, axis, pairs)
    part = (mine.astype(jnp.float32) + got.astype(jnp.float32)).astype(values.dtype)
    lines = [list(range(c, count, 2)) for c in range(2)]
    summed = lax.psum(part, axis, axis_index_groups=lines)
    back = lax.ppermute(summed, axis, pairs)
    even = me % 2 == 0
    return jnp.concatenate([jnp.where(even, summed, back), jnp.where(even, back, summed)], 0)


def dealt_places(lengths, dealing, series_grp, my_group):
    dealt_places = jnp.arange(lengths.shape[0], dtype=jnp.int32)
    owner = jnp.sum(
        jnp.where(dealing[None, :] == dealt_places[:, None], dealt_places[None, :], 0), axis=1
    )
    my_series = lax.dynamic_slice_in_dim(owner, my_group * series_grp, series_grp)
    place_len = lookup(lengths, my_series)
    blocks = (place_len + BLK - 1) // BLK
    place_start = BLK * jnp.cumsum(blocks) - BLK * blocks
    return my_series // series_grp, place_start, place_len


def block_bounds(src_len, group_rows):
    starts, series_at, _, _, live_row = packing(src_len, group_rows)
    first_rows = jnp.arange(group_rows // TQ, dtype=jnp.int32) * TQ
    seg = series_at[first_rows]
    inside = seg < src_len.shape[0]
    seg_c = jnp.minimum(seg, src_len.shape[0] - 1)
    block_start = jnp.where(inside, lookup(starts, seg_c), 0)
    block_end = jnp.where(inside, block_start + lookup(src_len, seg_c), 0)
    return block_start.astype(jnp.int32), block_end.astype(jnp.int32), live_row


def _window(i, rows, width):
    qs = i * TQ
    ws = jnp.minimum(jnp.maximum(qs - (width - TQ), 0), rows - width)
    return qs, pl.multiple_of(ws, TQ)


def _allowed(qs, ws, s0, e0, width):
    a = qs + lax.broadcasted_iota(jnp.int32, (TQ, width), 0)
    b = ws + lax.broadcasted_iota(jnp.int32, (TQ, width), 1)
    return (b >= s0) & (b <= a) & (b < e0)


def _fwd_block(i, s0, e0, q_ref, k_ref, v_ref, o_ref, lse_ref, width):
    heads, rows = k_ref.shape[0], k_ref.shape[1]
    qs, ws = _window(i, rows, width)
    allowed = _allowed(qs, ws, s0, e0, width)
    for h in range(heads):
        q = q_ref[h]
        k = k_ref[h, pl.ds(ws, width), :]
        v = v_ref[h, pl.ds(ws, width), :]
        s = lax.dot_general(q, k, (((1,), (1,)), ((), ())), preferred_element_type=jnp.float32)
        s = jnp.where(allowed, s, masked_score)
        m = jnp.max(s, axis=1, keepdims=True)
        p = jnp.exp(s - m)
        l = jnp.sum(p, axis=1, keepdims=True)
        probs = (p / l).astype(jnp.bfloat16)
        o = jnp.dot(probs, v, preferred_element_type=jnp.float32)
        o_ref[h] = o.astype(o_ref.dtype)
        lse_ref[h] = m + jnp.log(l)


def attn_fwd_kernel(starts_ref, ends_ref, q_ref, k_ref, v_ref, o_ref, lse_ref):
    i = pl.program_id(0)
    s0 = starts_ref[i]
    e0 = ends_ref[i]
    short = i * TQ + TQ - s0 <= LMAX // 2

    @pl.when((s0 < e0) & short)
    def _():
        _fwd_block(i, s0, e0, q_ref, k_ref, v_ref, o_ref, lse_ref, LMAX // 2)

    @pl.when((s0 < e0) & jnp.logical_not(short))
    def _():
        _fwd_block(i, s0, e0, q_ref, k_ref, v_ref, o_ref, lse_ref, LMAX)

    @pl.when(s0 >= e0)
    def _():
        o_ref[...] = jnp.zeros(o_ref.shape, o_ref.dtype)
        lse_ref[...] = jnp.zeros(lse_ref.shape, lse_ref.dtype)


def _bwd_block(i, s0, e0, q_ref, k_ref, v_ref, do_ref, lse_ref, dq_ref, dk_acc, dv_acc, width):
    heads, rows = k_ref.shape[0], k_ref.shape[1]
    qs, ws = _window(i, rows, width)
    allowed = _allowed(qs, ws, s0, e0, width)
    for h in range(heads):
        q = q_ref[h]
        k = k_ref[h, pl.ds(ws, width), :]
        v = v_ref[h, pl.ds(ws, width), :]
        do = do_ref[h]
        s = lax.dot_general(q, k, (((1,), (1,)), ((), ())), preferred_element_type=jnp.float32)
        s = jnp.where(allowed, s, masked_score)
        probs = jnp.exp(s - lse_ref[h])
        dp = lax.dot_general(do, v, (((1,), (1,)), ((), ())), preferred_element_type=jnp.float32)
        row_dot = jnp.sum(probs * dp, axis=1, keepdims=True)
        ds = (probs * (dp - row_dot)).astype(jnp.bfloat16)
        dq = jnp.dot(ds, k, preferred_element_type=jnp.float32)
        dq_ref[h] = dq.astype(dq_ref.dtype)
        dk_acc[h, pl.ds(ws, width), :] += jnp.dot(ds.T, q, preferred_element_type=jnp.float32)
        dv_acc[h, pl.ds(ws, width), :] += jnp.dot(
            probs.astype(jnp.bfloat16).T, do, preferred_element_type=jnp.float32
        )


def attn_bwd_kernel(starts_ref, ends_ref, q_ref, k_ref, v_ref, do_ref, lse_ref,
                    dq_ref, dk_ref, dv_ref, dk_acc, dv_acc):
    i = pl.program_id(0)
    s0 = starts_ref[i]
    e0 = ends_ref[i]
    short = i * TQ + TQ - s0 <= LMAX // 2

    @pl.when(i == 0)
    def _():
        dk_acc[...] = jnp.zeros(dk_acc.shape, dk_acc.dtype)
        dv_acc[...] = jnp.zeros(dv_acc.shape, dv_acc.dtype)

    @pl.when((s0 < e0) & short)
    def _():
        _bwd_block(i, s0, e0, q_ref, k_ref, v_ref, do_ref, lse_ref, dq_ref, dk_acc, dv_acc, LMAX // 2)

    @pl.when((s0 < e0) & jnp.logical_not(short))
    def _():
        _bwd_block(i, s0, e0, q_ref, k_ref, v_ref, do_ref, lse_ref, dq_ref, dk_acc, dv_acc, LMAX)

    @pl.when(s0 >= e0)
    def _():
        dq_ref[...] = jnp.zeros(dq_ref.shape, dq_ref.dtype)

    @pl.when(i == pl.num_programs(0) - 1)
    def _():
        dk_ref[...] = dk_acc[...].astype(dk_ref.dtype)
        dv_ref[...] = dv_acc[...].astype(dv_ref.dtype)


def attention_forward(q, k, v, starts, ends):
    heads, rows, width = q.shape
    blocks = rows // TQ
    whole = pl.BlockSpec((heads, rows, width), lambda i, s, e: (0, 0, 0))
    part = pl.BlockSpec((heads, TQ, width), lambda i, s, e: (0, i, 0))
    flops = 4 * heads * rows * LMAX * width
    return pl.pallas_call(
        attn_fwd_kernel,
        grid_spec=pltpu.PrefetchScalarGridSpec(
            num_scalar_prefetch=2,
            grid=(blocks,),
            in_specs=[part, whole, whole],
            out_specs=[part, pl.BlockSpec((heads, TQ, 1), lambda i, s, e: (0, i, 0))],
        ),
        out_shape=[
            jax.ShapeDtypeStruct((heads, rows, width), jnp.bfloat16),
            jax.ShapeDtypeStruct((heads, rows, 1), jnp.float32),
        ],
        compiler_params=pltpu.CompilerParams(
            dimension_semantics=("arbitrary",), vmem_limit_bytes=48 * 1024 * 1024
        ),
        cost_estimate=pl.CostEstimate(
            flops=flops, transcendentals=heads * rows * LMAX, bytes_accessed=4 * q.size * 2
        ),
    )(starts, ends, q, k, v)


def attention_backward(q, k, v, do, lse, starts, ends):
    heads, rows, width = q.shape
    blocks = rows // TQ
    whole = pl.BlockSpec((heads, rows, width), lambda i, s, e: (0, 0, 0))
    part = pl.BlockSpec((heads, TQ, width), lambda i, s, e: (0, i, 0))
    flops = 10 * heads * rows * LMAX * width
    return pl.pallas_call(
        attn_bwd_kernel,
        grid_spec=pltpu.PrefetchScalarGridSpec(
            num_scalar_prefetch=2,
            grid=(blocks,),
            in_specs=[part, whole, whole, part, pl.BlockSpec((heads, TQ, 1), lambda i, s, e: (0, i, 0))],
            out_specs=[part, whole, whole],
            scratch_shapes=[
                pltpu.VMEM((heads, rows, width), jnp.float32),
                pltpu.VMEM((heads, rows, width), jnp.float32),
            ],
        ),
        out_shape=[jax.ShapeDtypeStruct((heads, rows, width), jnp.bfloat16)] * 3,
        compiler_params=pltpu.CompilerParams(
            dimension_semantics=("arbitrary",), vmem_limit_bytes=48 * 1024 * 1024
        ),
        cost_estimate=pl.CostEstimate(
            flops=flops, transcendentals=heads * rows * LMAX, bytes_accessed=7 * q.size * 2
        ),
    )(starts, ends, q, k, v, do, lse)


def per_device(
    tokens,
    cotangent,
    lengths,
    dealing,
    gain_one,
    gain_two,
    attention_in,
    query_scale,
    attention_out,
    hidden_in,
    hidden_out,
):
    out_all, in_all, down_all = (
        lax.all_gather(attention_out, "mp", axis=0, tiled=True),
        lax.all_gather(hidden_in, "mp", axis=0, tiled=True),
        lax.all_gather(hidden_out, "mp", axis=0, tiled=True),
    )
    row_count = tokens.shape[0]
    mp_count = lax.axis_size("mp")
    my_group = lax.axis_index("dp")
    my_part = lax.axis_index("mp")
    group_rows = row_count * mp_count
    series_grp = group_rows // LMAX
    heads_here = NH // mp_count
    width_here = heads_here * HD
    shard_width = D // mp_count
    maps = series_maps(lengths, dealing, series_grp, group_rows, my_group)
    send_first, send_len = maps[0], maps[1]
    place_slot, place_start, place_len = dealt_places(lengths, dealing, series_grp, my_group)
    src_len = lax.dynamic_slice_in_dim(lengths, my_group * series_grp, series_grp)
    block_start, block_end, src_live = block_bounds(src_len, group_rows)
    live_mine = lax.dynamic_slice_in_dim(src_live, my_part * row_count, row_count).astype(
        jnp.float32
    )[:, None]
    gain_rows = jnp.zeros((8, D), jnp.bfloat16)
    gain_rows = gain_rows.at[0, :shard_width].set(gain_one).at[0, shard_width : 2 * shard_width].set(gain_two)
    packed = lax.all_gather(jnp.concatenate([tokens, gain_rows]), "mp", axis=0, tiled=False)
    gain_first = packed[:, row_count, :shard_width].reshape(D).astype(jnp.float32)
    gain_second = packed[:, row_count, shard_width : 2 * shard_width].reshape(D).astype(jnp.float32)
    inputs_group = packed[:, :row_count].reshape(group_rows, D).astype(jnp.float32)
    inv_group = lax.rsqrt(jnp.mean(inputs_group * inputs_group, axis=1, keepdims=True) + epsilon)
    normed_group = (inputs_group * inv_group * gain_first).astype(jnp.bfloat16)
    inputs = tokens.astype(jnp.float32)
    inv_one = lax.rsqrt(jnp.mean(inputs * inputs, axis=1, keepdims=True) + epsilon)
    weight_heads = attention_in.reshape(heads_here, HD, 3, D)
    projected = jnp.einsum(
        "rd,hecd->chre", normed_group, weight_heads, preferred_element_type=jnp.float32
    )
    dim_scale = scale_base / math.sqrt(HD) * jax.nn.softplus(query_scale)
    query_raw = projected[0]
    queries = (query_raw * dim_scale).astype(jnp.bfloat16)
    keys = projected[1].astype(jnp.bfloat16)
    values = projected[2].astype(jnp.bfloat16)
    kv_rows = jnp.stack([keys, values]).transpose(0, 2, 1, 3).reshape(2, group_rows, width_here)
    groups = lax.axis_size("dp")
    windows = send_windows(kv_rows, send_first, send_len, my_group, groups)
    received = [windows[0]] + [
        lax.ppermute(
            windows[shift], "dp", [(r, (r + shift) % groups) for r in range(groups)]
        )
        for shift in range(1, groups)
    ]
    place_shift = (my_group - place_slot) % groups
    cache = place_slots(received, place_shift, place_start, place_len, group_rows)
    mixed, log_total = attention_forward(queries, keys, values, block_start, block_end)
    att_group = jnp.where(src_live[None, :, None], mixed, jnp.zeros((), jnp.bfloat16))
    att_heads = lax.all_to_all(att_group, "mp", split_axis=1, concat_axis=0, tiled=True)
    out_heads = out_all.reshape(NH, HD, D)
    branch = jnp.einsum("hie,hed->id", att_heads, out_heads, preferred_element_type=jnp.float32)
    first_sum = inputs + branch
    inv_two = lax.rsqrt(jnp.mean(first_sum * first_sum, axis=1, keepdims=True) + epsilon)
    normed_two = (first_sum * inv_two * gain_second).astype(jnp.bfloat16)
    preact = jnp.einsum("rd,fd->rf", normed_two, in_all, preferred_element_type=jnp.float32)
    hidden = jax.nn.silu(preact).astype(jnp.bfloat16)
    feed = jnp.dot(hidden, down_all, preferred_element_type=jnp.float32)
    layer_out = ((first_sum + feed) * live_mine).astype(jnp.bfloat16)
    out_grad = cotangent.astype(jnp.float32) * live_mine
    feed_grad = out_grad.astype(jnp.bfloat16)
    hidden_grad = jnp.einsum("rd,fd->rf", feed_grad, down_all, preferred_element_type=jnp.float32)
    gate_sig = jax.nn.sigmoid(preact)
    preact_grad = (hidden_grad * gate_sig * (1.0 + preact * (1.0 - gate_sig))).astype(jnp.bfloat16)
    normed_two_grad = jnp.dot(preact_grad, in_all, preferred_element_type=jnp.float32)
    scaled_two = gain_second * normed_two_grad
    first_grad = (
        out_grad
        + inv_two * scaled_two
        - first_sum * inv_two**3 * jnp.mean(scaled_two * first_sum, axis=1, keepdims=True)
    )
    branch_grad = first_grad.astype(jnp.bfloat16)
    att_heads_grad = jnp.einsum(
        "id,hed->hie", branch_grad, out_heads, preferred_element_type=jnp.float32
    ).astype(jnp.bfloat16)
    grad_group = lax.all_to_all(att_heads_grad, "mp", split_axis=0, concat_axis=1, tiled=True)
    grad_heads = jnp.where(src_live[None, :, None], grad_group, jnp.zeros((), jnp.bfloat16))
    query_scaled_grad, key_grad, value_grad = attention_backward(
        queries, keys, values, grad_heads, log_total, block_start, block_end
    )
    live_heads = src_live[None, :, None]
    query_scaled_grad = jnp.where(live_heads, query_scaled_grad, jnp.zeros((), jnp.bfloat16)).astype(
        jnp.float32
    )
    scale_part = (
        jnp.sum(query_scaled_grad * query_raw, axis=(0, 1))
        * (scale_base / math.sqrt(HD))
        * jax.nn.sigmoid(query_scale)
    )
    query_grad = (query_scaled_grad * dim_scale).astype(jnp.bfloat16)
    proj_grad = jnp.stack(
        [
            query_grad,
            jnp.where(live_heads, key_grad, jnp.zeros((), jnp.bfloat16)),
            jnp.where(live_heads, value_grad, jnp.zeros((), jnp.bfloat16)),
        ]
    )
    qkv_part = jnp.einsum(
        "chre,rd->hecd", proj_grad, normed_group, preferred_element_type=jnp.float32
    ).reshape(width_here, 3, D)
    normed_one_part = jnp.einsum(
        "chre,hecd->rd", proj_grad, weight_heads, preferred_element_type=jnp.float32
    )
    normed_one_grad = lax.psum_scatter(
        normed_one_part.astype(jnp.bfloat16), "mp", scatter_dimension=0, tiled=True
    ).astype(jnp.float32)
    scaled_one = gain_first * normed_one_grad
    tokens_grad = (
        first_grad
        + inv_one * scaled_one
        - inputs * inv_one**3 * jnp.mean(scaled_one * inputs, axis=1, keepdims=True)
    )
    gain_one_part = jnp.sum(normed_one_part * inputs_group * inv_group, axis=0)
    gain_two_part = jnp.sum(normed_two_grad * first_sum * inv_two, axis=0)
    small = jnp.concatenate(
        [
            gain_one_part.reshape(mp_count, shard_width),
            gain_two_part.reshape(mp_count, shard_width),
            jnp.broadcast_to(scale_part, (mp_count, HD)),
        ],
        axis=1,
    )
    small = lax.psum(lax.psum_scatter(small, "mp", scatter_dimension=0, tiled=True), "dp")
    gain_one_grad = small[0, :shard_width]
    gain_two_grad = small[0, shard_width : 2 * shard_width]
    query_scale_grad = small[0, 2 * shard_width :]
    out_part = jnp.einsum(
        "hie,id->hed", att_heads, branch_grad, preferred_element_type=jnp.float32
    ).reshape(D, D)
    in_part = jnp.einsum("ru,rd->ud", preact_grad, normed_two, preferred_element_type=jnp.float32)
    down_part = jnp.einsum("ru,rd->ud", hidden, feed_grad, preferred_element_type=jnp.float32)
    row_terms = jnp.stack([out_part, in_part, down_part], axis=1)
    shares = lax.psum_scatter(
        row_terms.astype(jnp.bfloat16), "mp", scatter_dimension=0, tiled=True
    )
    totals = pair_then_line_sum(
        jnp.concatenate([qkv_part.astype(jnp.bfloat16), shares], axis=1), "dp", lax.axis_size("dp")
    ).astype(jnp.float32)
    return (
        layer_out,
        tokens_grad,
        cache,
        gain_one_grad,
        gain_two_grad,
        totals[:, 0:3],
        query_scale_grad,
        totals[:, 3],
        totals[:, 4],
        totals[:, 5],
    )


def solution(mesh):
    placed = (
        P(("dp", "mp"), None),
        P(("dp", "mp"), None),
        P(),
        P(),
        P("mp"),
        P("mp"),
        P("mp", None, None),
        P(),
        P("mp", None),
        P("mp", None),
        P("mp", None),
    )
    return jax.shard_map(
        per_device,
        mesh=mesh,
        in_specs=placed,
        out_specs=(
            P(("dp", "mp"), None),
            P(("dp", "mp"), None),
            P(None, "dp", "mp"),
            P("mp"),
            P("mp"),
            P("mp", None, None),
            P(),
            P("mp", None),
            P("mp", None),
            P("mp", None),
        ),
        check_vma=False,
    )
```

```python
import math

import jax
import jax.numpy as jnp
from jax import lax
from jax.experimental import pallas as pl
from jax.experimental.pallas import tpu as pltpu
from jax.sharding import PartitionSpec as P


D = 1280
NH = 16
HD = 80
LMAX = 1024
BLK = 128
TQ = 128


epsilon = 1e-06
scale_base = 1.442695041
masked_score = -1e30


def lookup(values_table, positions):
    entries = jnp.arange(values_table.shape[0], dtype=jnp.int32)
    picked = jnp.where(positions[:, None] == entries[None, :], values_table[None, :], 0)
    return jnp.sum(picked, axis=1)


def packing(span_len, group_rows):
    blocks = (span_len + BLK - 1) // BLK
    block_ends = BLK * jnp.cumsum(blocks)
    starts = block_ends - BLK * blocks
    in_group = jnp.arange(group_rows, dtype=jnp.int32)
    series_at = jnp.sum((block_ends[None, :] <= in_group[:, None]).astype(jnp.int32), axis=1)
    capped = jnp.minimum(series_at, span_len.shape[0] - 1)
    offset = in_group - lookup(starts, capped)
    live_row = (series_at < span_len.shape[0]) & (offset < lookup(span_len, capped))
    return (starts, series_at, capped, offset, live_row)


def slot_table(slot_of, starts, span_len, slot_count):
    entries = jnp.arange(slot_count, dtype=jnp.int32)
    matched = slot_of[None, :] == entries[:, None]
    slot_first = jnp.sum(jnp.where(matched, starts[None, :], 0), axis=1)
    slot_length = jnp.sum(jnp.where(matched, span_len[None, :], 0), axis=1)
    return (slot_first, slot_length)


def series_maps(lengths, dealing, series_grp, group_rows, my_group):
    groups = lengths.shape[0] // series_grp
    capacity = (series_grp + groups - 1) // groups
    places = jnp.arange(series_grp, dtype=jnp.int32)
    target = dealing.reshape(groups, series_grp) // series_grp
    earlier = (target[:, :, None] == target[:, None, :]) & (
        places[None, None, :] < places[None, :, None]
    )
    rank_of = jnp.sum(earlier.astype(jnp.int32), axis=2)
    slot_of = (target * capacity + rank_of).reshape(-1)
    rank_flat = rank_of.reshape(-1)
    src_len = lax.dynamic_slice_in_dim(lengths, my_group * series_grp, series_grp)
    src_slot = lax.dynamic_slice_in_dim(slot_of, my_group * series_grp, series_grp)
    src_starts, _, src_capped, src_offset, src_live = packing(src_len, group_rows)
    dealt_places = jnp.arange(lengths.shape[0], dtype=jnp.int32)
    owner = jnp.sum(
        jnp.where(dealing[None, :] == dealt_places[:, None], dealt_places[None, :], 0), axis=1
    )
    my_series = lax.dynamic_slice_in_dim(owner, my_group * series_grp, series_grp)
    dst_len = lookup(lengths, my_series)
    dst_slot = my_series // series_grp * capacity + lookup(rank_flat, my_series)
    dst_starts, dst_at, dst_capped, dst_offset, dst_live = packing(dst_len, group_rows)
    slot_count = groups * capacity
    send_first, send_len = slot_table(src_slot, src_starts, src_len, slot_count)
    back_first, back_len = slot_table(dst_slot, dst_starts, dst_len, slot_count)
    src_index = lookup(src_slot, src_capped) * LMAX + src_offset
    dst_index = lookup(dst_slot, dst_capped) * LMAX + dst_offset
    key_live = jnp.where(dst_at < series_grp, dst_live, True)
    return (
        send_first,
        send_len,
        back_first,
        back_len,
        src_index,
        src_live,
        dst_index,
        dst_live,
        dst_at,
        key_live,
    )


def send_windows(values, slot_first, slot_length, my_group, groups):
    padded = jnp.pad(values, ((0, 0), (0, LMAX), (0, 0)))
    positions = jnp.arange(LMAX, dtype=jnp.int32)[None, :, None]
    windows = []
    for shift in range(groups):
        target = (my_group + shift) % groups
        window = lax.dynamic_slice_in_dim(padded, slot_first[target], LMAX, axis=1)
        windows.append(
            jnp.where(positions < slot_length[target], window, jnp.zeros((), values.dtype))
        )
    return windows


def place_slots(stacked, place_shift, place_start, place_len, out_rows):
    rows = jnp.arange(out_rows, dtype=jnp.int32)[None, :, None]
    placed = jnp.zeros((stacked.shape[1], out_rows, stacked.shape[3]), stacked.dtype)
    for q in range(place_shift.shape[0]):
        window = lax.dynamic_index_in_dim(stacked, place_shift[q], axis=0, keepdims=False)
        padded = jnp.pad(window, ((0, 0), (out_rows, out_rows - LMAX), (0, 0)))
        shifted = lax.dynamic_slice_in_dim(padded, out_rows - place_start[q], out_rows, axis=1)
        inside = (rows >= place_start[q]) & (rows < place_start[q] + place_len[q])
        placed = jnp.where(inside, shifted, placed)
    return placed


def dealt_places(lengths, dealing, series_grp, my_group):
    dealt_places = jnp.arange(lengths.shape[0], dtype=jnp.int32)
    owner = jnp.sum(
        jnp.where(dealing[None, :] == dealt_places[:, None], dealt_places[None, :], 0), axis=1
    )
    my_series = lax.dynamic_slice_in_dim(owner, my_group * series_grp, series_grp)
    place_len = lookup(lengths, my_series)
    blocks = (place_len + BLK - 1) // BLK
    place_start = BLK * jnp.cumsum(blocks) - BLK * blocks
    return my_series // series_grp, place_start, place_len


def block_bounds(src_len, group_rows):
    starts, series_at, _, _, live_row = packing(src_len, group_rows)
    first_rows = jnp.arange(group_rows // TQ, dtype=jnp.int32) * TQ
    seg = series_at[first_rows]
    inside = seg < src_len.shape[0]
    seg_c = jnp.minimum(seg, src_len.shape[0] - 1)
    block_start = jnp.where(inside, lookup(starts, seg_c), 0)
    block_end = jnp.where(inside, block_start + lookup(src_len, seg_c), 0)
    return block_start.astype(jnp.int32), block_end.astype(jnp.int32), live_row


def _window(i, rows, width):
    qs = i * TQ
    ws = jnp.minimum(jnp.maximum(qs - (width - TQ), 0), rows - width)
    return qs, pl.multiple_of(ws, TQ)


def _allowed(qs, ws, s0, e0, width):
    a = qs + lax.broadcasted_iota(jnp.int32, (TQ, width), 0)
    b = ws + lax.broadcasted_iota(jnp.int32, (TQ, width), 1)
    return (b >= s0) & (b <= a) & (b < e0)


def _fwd_block(i, s0, e0, q_ref, k_ref, v_ref, o_ref, lse_ref, width):
    heads, rows = k_ref.shape[0], k_ref.shape[1]
    qs, ws = _window(i, rows, width)
    allowed = _allowed(qs, ws, s0, e0, width)
    for h in range(heads):
        q = q_ref[h]
        k = k_ref[h, pl.ds(ws, width), :]
        v = v_ref[h, pl.ds(ws, width), :]
        s = lax.dot_general(q, k, (((1,), (1,)), ((), ())), preferred_element_type=jnp.float32)
        s = jnp.where(allowed, s, masked_score)
        m = jnp.max(s, axis=1, keepdims=True)
        p = jnp.exp(s - m)
        l = jnp.sum(p, axis=1, keepdims=True)
        probs = (p / l).astype(jnp.bfloat16)
        o = jnp.dot(probs, v, preferred_element_type=jnp.float32)
        o_ref[h] = o.astype(o_ref.dtype)
        lse_ref[h] = m + jnp.log(l)


def attn_fwd_kernel(starts_ref, ends_ref, q_ref, k_ref, v_ref, o_ref, lse_ref):
    i = pl.program_id(0)
    s0 = starts_ref[i]
    e0 = ends_ref[i]
    short = i * TQ + TQ - s0 <= LMAX // 2

    @pl.when((s0 < e0) & short)
    def _():
        _fwd_block(i, s0, e0, q_ref, k_ref, v_ref, o_ref, lse_ref, LMAX // 2)

    @pl.when((s0 < e0) & jnp.logical_not(short))
    def _():
        _fwd_block(i, s0, e0, q_ref, k_ref, v_ref, o_ref, lse_ref, LMAX)

    @pl.when(s0 >= e0)
    def _():
        o_ref[...] = jnp.zeros(o_ref.shape, o_ref.dtype)
        lse_ref[...] = jnp.zeros(lse_ref.shape, lse_ref.dtype)


def _bwd_block(i, s0, e0, q_ref, k_ref, v_ref, do_ref, lse_ref, dq_ref, dk_acc, dv_acc, width):
    heads, rows = k_ref.shape[0], k_ref.shape[1]
    qs, ws = _window(i, rows, width)
    allowed = _allowed(qs, ws, s0, e0, width)
    for h in range(heads):
        q = q_ref[h]
        k = k_ref[h, pl.ds(ws, width), :]
        v = v_ref[h, pl.ds(ws, width), :]
        do = do_ref[h]
        s = lax.dot_general(q, k, (((1,), (1,)), ((), ())), preferred_element_type=jnp.float32)
        s = jnp.where(allowed, s, masked_score)
        probs = jnp.exp(s - lse_ref[h])
        dp = lax.dot_general(do, v, (((1,), (1,)), ((), ())), preferred_element_type=jnp.float32)
        row_dot = jnp.sum(probs * dp, axis=1, keepdims=True)
        ds = (probs * (dp - row_dot)).astype(jnp.bfloat16)
        dq = jnp.dot(ds, k, preferred_element_type=jnp.float32)
        dq_ref[h] = dq.astype(dq_ref.dtype)
        dk_acc[h, pl.ds(ws, width), :] += jnp.dot(ds.T, q, preferred_element_type=jnp.float32)
        dv_acc[h, pl.ds(ws, width), :] += jnp.dot(
            probs.astype(jnp.bfloat16).T, do, preferred_element_type=jnp.float32
        )


def attn_bwd_kernel(starts_ref, ends_ref, q_ref, k_ref, v_ref, do_ref, lse_ref,
                    dq_ref, dk_ref, dv_ref, dk_acc, dv_acc):
    i = pl.program_id(0)
    s0 = starts_ref[i]
    e0 = ends_ref[i]
    short = i * TQ + TQ - s0 <= LMAX // 2

    @pl.when(i == 0)
    def _():
        dk_acc[...] = jnp.zeros(dk_acc.shape, dk_acc.dtype)
        dv_acc[...] = jnp.zeros(dv_acc.shape, dv_acc.dtype)

    @pl.when((s0 < e0) & short)
    def _():
        _bwd_block(i, s0, e0, q_ref, k_ref, v_ref, do_ref, lse_ref, dq_ref, dk_acc, dv_acc, LMAX // 2)

    @pl.when((s0 < e0) & jnp.logical_not(short))
    def _():
        _bwd_block(i, s0, e0, q_ref, k_ref, v_ref, do_ref, lse_ref, dq_ref, dk_acc, dv_acc, LMAX)

    @pl.when(s0 >= e0)
    def _():
        dq_ref[...] = jnp.zeros(dq_ref.shape, dq_ref.dtype)

    @pl.when(i == pl.num_programs(0) - 1)
    def _():
        dk_ref[...] = dk_acc[...].astype(dk_ref.dtype)
        dv_ref[...] = dv_acc[...].astype(dv_ref.dtype)


def attention_forward(q, k, v, starts, ends):
    heads, rows, width = q.shape
    blocks = rows // TQ
    whole = pl.BlockSpec((heads, rows, width), lambda i, s, e: (0, 0, 0))
    part = pl.BlockSpec((heads, TQ, width), lambda i, s, e: (0, i, 0))
    flops = 4 * heads * rows * LMAX * width
    return pl.pallas_call(
        attn_fwd_kernel,
        grid_spec=pltpu.PrefetchScalarGridSpec(
            num_scalar_prefetch=2,
            grid=(blocks,),
            in_specs=[part, whole, whole],
            out_specs=[part, pl.BlockSpec((heads, TQ, 1), lambda i, s, e: (0, i, 0))],
        ),
        out_shape=[
            jax.ShapeDtypeStruct((heads, rows, width), jnp.bfloat16),
            jax.ShapeDtypeStruct((heads, rows, 1), jnp.float32),
        ],
        compiler_params=pltpu.CompilerParams(
            dimension_semantics=("arbitrary",), vmem_limit_bytes=48 * 1024 * 1024
        ),
        cost_estimate=pl.CostEstimate(
            flops=flops, transcendentals=heads * rows * LMAX, bytes_accessed=4 * q.size * 2
        ),
    )(starts, ends, q, k, v)


def attention_backward(q, k, v, do, lse, starts, ends):
    heads, rows, width = q.shape
    blocks = rows // TQ
    whole = pl.BlockSpec((heads, rows, width), lambda i, s, e: (0, 0, 0))
    part = pl.BlockSpec((heads, TQ, width), lambda i, s, e: (0, i, 0))
    flops = 10 * heads * rows * LMAX * width
    return pl.pallas_call(
        attn_bwd_kernel,
        grid_spec=pltpu.PrefetchScalarGridSpec(
            num_scalar_prefetch=2,
            grid=(blocks,),
            in_specs=[part, whole, whole, part, pl.BlockSpec((heads, TQ, 1), lambda i, s, e: (0, i, 0))],
            out_specs=[part, whole, whole],
            scratch_shapes=[
                pltpu.VMEM((heads, rows, width), jnp.float32),
                pltpu.VMEM((heads, rows, width), jnp.float32),
            ],
        ),
        out_shape=[jax.ShapeDtypeStruct((heads, rows, width), jnp.bfloat16)] * 3,
        compiler_params=pltpu.CompilerParams(
            dimension_semantics=("arbitrary",), vmem_limit_bytes=48 * 1024 * 1024
        ),
        cost_estimate=pl.CostEstimate(
            flops=flops, transcendentals=heads * rows * LMAX, bytes_accessed=7 * q.size * 2
        ),
    )(starts, ends, q, k, v, do, lse)


def per_device(
    tokens,
    cotangent,
    lengths,
    dealing,
    gain_one,
    gain_two,
    attention_in,
    query_scale,
    attention_out,
    hidden_in,
    hidden_out,
):
    out_all, in_all, down_all = (
        lax.all_gather(attention_out, "mp", axis=0, tiled=True),
        lax.all_gather(hidden_in, "mp", axis=0, tiled=True),
        lax.all_gather(hidden_out, "mp", axis=0, tiled=True),
    )
    row_count = tokens.shape[0]
    mp_count = lax.axis_size("mp")
    my_group = lax.axis_index("dp")
    my_part = lax.axis_index("mp")
    group_rows = row_count * mp_count
    series_grp = group_rows // LMAX
    heads_here = NH // mp_count
    width_here = heads_here * HD
    shard_width = D // mp_count
    maps = series_maps(lengths, dealing, series_grp, group_rows, my_group)
    send_first, send_len = maps[0], maps[1]
    place_slot, place_start, place_len = dealt_places(lengths, dealing, series_grp, my_group)
    src_len = lax.dynamic_slice_in_dim(lengths, my_group * series_grp, series_grp)
    block_start, block_end, src_live = block_bounds(src_len, group_rows)
    live_mine = lax.dynamic_slice_in_dim(src_live, my_part * row_count, row_count).astype(
        jnp.float32
    )[:, None]
    gain_rows = jnp.zeros((8, D), jnp.bfloat16)
    gain_rows = gain_rows.at[0, :shard_width].set(gain_one).at[0, shard_width : 2 * shard_width].set(gain_two)
    packed = lax.all_gather(jnp.concatenate([tokens, gain_rows]), "mp", axis=0, tiled=False)
    gain_first = packed[:, row_count, :shard_width].reshape(D).astype(jnp.float32)
    gain_second = packed[:, row_count, shard_width : 2 * shard_width].reshape(D).astype(jnp.float32)
    inputs_group = packed[:, :row_count].reshape(group_rows, D).astype(jnp.float32)
    inv_group = lax.rsqrt(jnp.mean(inputs_group * inputs_group, axis=1, keepdims=True) + epsilon)
    normed_group = (inputs_group * inv_group * gain_first).astype(jnp.bfloat16)
    inputs = tokens.astype(jnp.float32)
    inv_one = lax.rsqrt(jnp.mean(inputs * inputs, axis=1, keepdims=True) + epsilon)
    weight_heads = attention_in.reshape(heads_here, HD, 3, D)
    projected = jnp.einsum(
        "rd,hecd->chre", normed_group, weight_heads, preferred_element_type=jnp.float32
    )
    dim_scale = scale_base / math.sqrt(HD) * jax.nn.softplus(query_scale)
    query_raw = projected[0]
    queries = (query_raw * dim_scale).astype(jnp.bfloat16)
    keys = projected[1].astype(jnp.bfloat16)
    values = projected[2].astype(jnp.bfloat16)
    kv_rows = jnp.stack([keys, values]).transpose(0, 2, 1, 3).reshape(2, group_rows, width_here)
    groups = lax.axis_size("dp")
    windows = send_windows(kv_rows, send_first, send_len, my_group, groups)
    received = [windows[0]] + [
        lax.ppermute(
            windows[shift], "dp", [(r, (r + shift) % groups) for r in range(groups)]
        )
        for shift in range(1, groups)
    ]
    place_shift = (my_group - place_slot) % groups
    received = jnp.stack(received)
    mixed, log_total = attention_forward(queries, keys, values, block_start, block_end)
    att_group = jnp.where(src_live[None, :, None], mixed, jnp.zeros((), jnp.bfloat16))
    att_heads = lax.all_to_all(att_group, "mp", split_axis=1, concat_axis=0, tiled=True)
    out_heads = out_all.reshape(NH, HD, D)
    branch = jnp.einsum("hie,hed->id", att_heads, out_heads, preferred_element_type=jnp.float32)
    first_sum = inputs + branch
    inv_two = lax.rsqrt(jnp.mean(first_sum * first_sum, axis=1, keepdims=True) + epsilon)
    normed_two = (first_sum * inv_two * gain_second).astype(jnp.bfloat16)
    preact = jnp.einsum("rd,fd->rf", normed_two, in_all, preferred_element_type=jnp.float32)
    hidden = jax.nn.silu(preact).astype(jnp.bfloat16)
    feed = jnp.dot(hidden, down_all, preferred_element_type=jnp.float32)
    layer_out = ((first_sum + feed) * live_mine).astype(jnp.bfloat16)
    out_grad = cotangent.astype(jnp.float32) * live_mine
    feed_grad = out_grad.astype(jnp.bfloat16)
    hidden_grad = jnp.einsum("rd,fd->rf", feed_grad, down_all, preferred_element_type=jnp.float32)
    gate_sig = jax.nn.sigmoid(preact)
    preact_grad = (hidden_grad * gate_sig * (1.0 + preact * (1.0 - gate_sig))).astype(jnp.bfloat16)
    normed_two_grad = jnp.dot(preact_grad, in_all, preferred_element_type=jnp.float32)
    scaled_two = gain_second * normed_two_grad
    first_grad = (
        out_grad
        + inv_two * scaled_two
        - first_sum * inv_two**3 * jnp.mean(scaled_two * first_sum, axis=1, keepdims=True)
    )
    branch_grad = first_grad.astype(jnp.bfloat16)
    att_heads_grad = jnp.einsum(
        "id,hed->hie", branch_grad, out_heads, preferred_element_type=jnp.float32
    ).astype(jnp.bfloat16)
    grad_group = lax.all_to_all(att_heads_grad, "mp", split_axis=0, concat_axis=1, tiled=True)
    grad_heads = jnp.where(src_live[None, :, None], grad_group, jnp.zeros((), jnp.bfloat16))
    out_part = jnp.einsum(
        "hie,id->hed", att_heads, branch_grad, preferred_element_type=jnp.float32
    ).reshape(D, D)
    in_part = jnp.einsum("ru,rd->ud", preact_grad, normed_two, preferred_element_type=jnp.float32)
    down_part = jnp.einsum("ru,rd->ud", hidden, feed_grad, preferred_element_type=jnp.float32)
    row_terms = jnp.stack([out_part, in_part, down_part], axis=1)
    shares = lax.psum_scatter(
        row_terms.astype(jnp.bfloat16), "mp", scatter_dimension=0, tiled=True
    )
    query_scaled_grad, key_grad, value_grad = attention_backward(
        queries, keys, values, grad_heads, log_total, block_start, block_end
    )
    live_heads = src_live[None, :, None]
    query_scaled_grad = jnp.where(live_heads, query_scaled_grad, jnp.zeros((), jnp.bfloat16)).astype(
        jnp.float32
    )
    query_grad = (query_scaled_grad * dim_scale).astype(jnp.bfloat16)
    proj_grad = jnp.stack(
        [
            query_grad,
            jnp.where(live_heads, key_grad, jnp.zeros((), jnp.bfloat16)),
            jnp.where(live_heads, value_grad, jnp.zeros((), jnp.bfloat16)),
        ]
    )
    qkv_part = jnp.einsum(
        "chre,rd->hecd", proj_grad, normed_group, preferred_element_type=jnp.float32
    ).reshape(width_here, 3, D)
    normed_one_part = jnp.einsum(
        "chre,hecd->rd", proj_grad, weight_heads, preferred_element_type=jnp.float32
    )
    normed_one_part, qkv_part, shares, query_raw = lax.optimization_barrier(
        (normed_one_part, qkv_part, shares, query_raw)
    )
    cache = place_slots(received, place_shift, place_start, place_len, group_rows)
    scale_part = (
        jnp.sum(query_scaled_grad * query_raw, axis=(0, 1))
        * (scale_base / math.sqrt(HD))
        * jax.nn.sigmoid(query_scale)
    )
    normed_one_grad = lax.psum_scatter(
        normed_one_part.astype(jnp.bfloat16), "mp", scatter_dimension=0, tiled=True
    ).astype(jnp.float32)
    scaled_one = gain_first * normed_one_grad
    tokens_grad = (
        first_grad
        + inv_one * scaled_one
        - inputs * inv_one**3 * jnp.mean(scaled_one * inputs, axis=1, keepdims=True)
    )
    gain_one_part = jnp.sum(normed_one_part * inputs_group * inv_group, axis=0)
    gain_two_part = jnp.sum(normed_two_grad * first_sum * inv_two, axis=0)
    small = jnp.concatenate(
        [
            gain_one_part.reshape(mp_count, shard_width),
            gain_two_part.reshape(mp_count, shard_width),
            jnp.broadcast_to(scale_part, (mp_count, HD)),
        ],
        axis=1,
    )
    small = lax.psum(lax.psum_scatter(small, "mp", scatter_dimension=0, tiled=True), "dp")
    gain_one_grad = small[0, :shard_width]
    gain_two_grad = small[0, shard_width : 2 * shard_width]
    query_scale_grad = small[0, 2 * shard_width :]
    totals = lax.psum(
        jnp.concatenate([qkv_part.astype(jnp.bfloat16), shares], axis=1), "dp"
    ).astype(jnp.float32)
    return (
        layer_out,
        tokens_grad,
        cache,
        gain_one_grad,
        gain_two_grad,
        totals[:, 0:3],
        query_scale_grad,
        totals[:, 3],
        totals[:, 4],
        totals[:, 5],
    )


def solution(mesh):
    placed = (
        P(("dp", "mp"), None),
        P(("dp", "mp"), None),
        P(),
        P(),
        P("mp"),
        P("mp"),
        P("mp", None, None),
        P(),
        P("mp", None),
        P("mp", None),
        P("mp", None),
    )
    return jax.shard_map(
        per_device,
        mesh=mesh,
        in_specs=placed,
        out_specs=(
            P(("dp", "mp"), None),
            P(("dp", "mp"), None),
            P(None, "dp", "mp"),
            P("mp"),
            P("mp"),
            P("mp", None, None),
            P(),
            P("mp", None),
            P("mp", None),
            P("mp", None),
        ),
        check_vma=False,
    )
```

```python
import math

import jax
import jax.numpy as jnp
from jax import lax
from jax.experimental import pallas as pl
from jax.experimental.pallas import tpu as pltpu
from jax.sharding import PartitionSpec as P


D = 1280
NH = 16
HD = 80
LMAX = 1024
BLK = 128
TQ = 128


epsilon = 1e-06
scale_base = 1.442695041
masked_score = -1e30


def lookup(values_table, positions):
    entries = jnp.arange(values_table.shape[0], dtype=jnp.int32)
    picked = jnp.where(positions[:, None] == entries[None, :], values_table[None, :], 0)
    return jnp.sum(picked, axis=1)


def packing(span_len, group_rows):
    blocks = (span_len + BLK - 1) // BLK
    block_ends = BLK * jnp.cumsum(blocks)
    starts = block_ends - BLK * blocks
    in_group = jnp.arange(group_rows, dtype=jnp.int32)
    series_at = jnp.sum((block_ends[None, :] <= in_group[:, None]).astype(jnp.int32), axis=1)
    capped = jnp.minimum(series_at, span_len.shape[0] - 1)
    offset = in_group - lookup(starts, capped)
    live_row = (series_at < span_len.shape[0]) & (offset < lookup(span_len, capped))
    return (starts, series_at, capped, offset, live_row)


def slot_table(slot_of, starts, span_len, slot_count):
    entries = jnp.arange(slot_count, dtype=jnp.int32)
    matched = slot_of[None, :] == entries[:, None]
    slot_first = jnp.sum(jnp.where(matched, starts[None, :], 0), axis=1)
    slot_length = jnp.sum(jnp.where(matched, span_len[None, :], 0), axis=1)
    return (slot_first, slot_length)


def series_maps(lengths, dealing, series_grp, group_rows, my_group):
    groups = lengths.shape[0] // series_grp
    capacity = (series_grp + groups - 1) // groups
    places = jnp.arange(series_grp, dtype=jnp.int32)
    target = dealing.reshape(groups, series_grp) // series_grp
    earlier = (target[:, :, None] == target[:, None, :]) & (
        places[None, None, :] < places[None, :, None]
    )
    rank_of = jnp.sum(earlier.astype(jnp.int32), axis=2)
    slot_of = (target * capacity + rank_of).reshape(-1)
    rank_flat = rank_of.reshape(-1)
    src_len = lax.dynamic_slice_in_dim(lengths, my_group * series_grp, series_grp)
    src_slot = lax.dynamic_slice_in_dim(slot_of, my_group * series_grp, series_grp)
    src_starts, _, src_capped, src_offset, src_live = packing(src_len, group_rows)
    dealt_places = jnp.arange(lengths.shape[0], dtype=jnp.int32)
    owner = jnp.sum(
        jnp.where(dealing[None, :] == dealt_places[:, None], dealt_places[None, :], 0), axis=1
    )
    my_series = lax.dynamic_slice_in_dim(owner, my_group * series_grp, series_grp)
    dst_len = lookup(lengths, my_series)
    dst_slot = my_series // series_grp * capacity + lookup(rank_flat, my_series)
    dst_starts, dst_at, dst_capped, dst_offset, dst_live = packing(dst_len, group_rows)
    slot_count = groups * capacity
    send_first, send_len = slot_table(src_slot, src_starts, src_len, slot_count)
    back_first, back_len = slot_table(dst_slot, dst_starts, dst_len, slot_count)
    src_index = lookup(src_slot, src_capped) * LMAX + src_offset
    dst_index = lookup(dst_slot, dst_capped) * LMAX + dst_offset
    key_live = jnp.where(dst_at < series_grp, dst_live, True)
    return (
        send_first,
        send_len,
        back_first,
        back_len,
        src_index,
        src_live,
        dst_index,
        dst_live,
        dst_at,
        key_live,
    )


def send_windows(values, slot_first, slot_length, my_group, groups):
    padded = jnp.pad(values, ((0, 0), (0, LMAX), (0, 0)))
    positions = jnp.arange(LMAX, dtype=jnp.int32)[None, :, None]
    windows = []
    for shift in range(groups):
        target = (my_group + shift) % groups
        window = lax.dynamic_slice_in_dim(padded, slot_first[target], LMAX, axis=1)
        windows.append(
            jnp.where(positions < slot_length[target], window, jnp.zeros((), values.dtype))
        )
    return windows


def place_slots(stacked, place_shift, place_start, place_len, out_rows):
    rows = jnp.arange(out_rows, dtype=jnp.int32)[None, :, None]
    placed = jnp.zeros((stacked.shape[1], out_rows, stacked.shape[3]), stacked.dtype)
    for q in range(place_shift.shape[0]):
        window = lax.dynamic_index_in_dim(stacked, place_shift[q], axis=0, keepdims=False)
        padded = jnp.pad(window, ((0, 0), (out_rows, out_rows - LMAX), (0, 0)))
        shifted = lax.dynamic_slice_in_dim(padded, out_rows - place_start[q], out_rows, axis=1)
        inside = (rows >= place_start[q]) & (rows < place_start[q] + place_len[q])
        placed = jnp.where(inside, shifted, placed)
    return placed


def scatter_sum(partial, axis, count, me):
    size = partial.shape[0] // count
    total = lax.dynamic_slice_in_dim(partial, me * size, size, 0).astype(jnp.float32)
    for shift in range(1, count):
        piece = lax.dynamic_slice_in_dim(partial, ((me + shift) % count) * size, size, 0)
        total = total + lax.ppermute(
            piece, axis, [(r, (r + shift) % count) for r in range(count)]
        ).astype(jnp.float32)
    return total


def dealt_places(lengths, dealing, series_grp, my_group):
    dealt_places = jnp.arange(lengths.shape[0], dtype=jnp.int32)
    owner = jnp.sum(
        jnp.where(dealing[None, :] == dealt_places[:, None], dealt_places[None, :], 0), axis=1
    )
    my_series = lax.dynamic_slice_in_dim(owner, my_group * series_grp, series_grp)
    place_len = lookup(lengths, my_series)
    blocks = (place_len + BLK - 1) // BLK
    place_start = BLK * jnp.cumsum(blocks) - BLK * blocks
    return my_series // series_grp, place_start, place_len


def block_bounds(src_len, group_rows):
    starts, series_at, _, _, live_row = packing(src_len, group_rows)
    first_rows = jnp.arange(group_rows // TQ, dtype=jnp.int32) * TQ
    seg = series_at[first_rows]
    inside = seg < src_len.shape[0]
    seg_c = jnp.minimum(seg, src_len.shape[0] - 1)
    block_start = jnp.where(inside, lookup(starts, seg_c), 0)
    block_end = jnp.where(inside, block_start + lookup(src_len, seg_c), 0)
    return block_start.astype(jnp.int32), block_end.astype(jnp.int32), live_row


def _window(i, rows, width):
    qs = i * TQ
    ws = jnp.minimum(jnp.maximum(qs - (width - TQ), 0), rows - width)
    return qs, pl.multiple_of(ws, TQ)


def _allowed(qs, ws, s0, e0, width):
    a = qs + lax.broadcasted_iota(jnp.int32, (TQ, width), 0)
    b = ws + lax.broadcasted_iota(jnp.int32, (TQ, width), 1)
    return (b >= s0) & (b <= a) & (b < e0)


def _fwd_block(i, s0, e0, q_ref, k_ref, v_ref, o_ref, lse_ref, width):
    heads, rows = k_ref.shape[0], k_ref.shape[1]
    qs, ws = _window(i, rows, width)
    allowed = _allowed(qs, ws, s0, e0, width)
    for h in range(heads):
        q = q_ref[h]
        k = k_ref[h, pl.ds(ws, width), :]
        v = v_ref[h, pl.ds(ws, width), :]
        s = lax.dot_general(q, k, (((1,), (1,)), ((), ())), preferred_element_type=jnp.float32)
        s = jnp.where(allowed, s, masked_score)
        m = jnp.max(s, axis=1, keepdims=True)
        p = jnp.exp(s - m)
        l = jnp.sum(p, axis=1, keepdims=True)
        probs = (p / l).astype(jnp.bfloat16)
        o = jnp.dot(probs, v, preferred_element_type=jnp.float32)
        o_ref[h] = o.astype(o_ref.dtype)
        lse_ref[h] = m + jnp.log(l)


def attn_fwd_kernel(starts_ref, ends_ref, q_ref, k_ref, v_ref, o_ref, lse_ref):
    i = pl.program_id(0)
    s0 = starts_ref[i]
    e0 = ends_ref[i]
    short = i * TQ + TQ - s0 <= LMAX // 2

    @pl.when((s0 < e0) & short)
    def _():
        _fwd_block(i, s0, e0, q_ref, k_ref, v_ref, o_ref, lse_ref, LMAX // 2)

    @pl.when((s0 < e0) & jnp.logical_not(short))
    def _():
        _fwd_block(i, s0, e0, q_ref, k_ref, v_ref, o_ref, lse_ref, LMAX)

    @pl.when(s0 >= e0)
    def _():
        o_ref[...] = jnp.zeros(o_ref.shape, o_ref.dtype)
        lse_ref[...] = jnp.zeros(lse_ref.shape, lse_ref.dtype)


def _bwd_block(i, s0, e0, q_ref, k_ref, v_ref, do_ref, lse_ref, dq_ref, dk_acc, dv_acc, width):
    heads, rows = k_ref.shape[0], k_ref.shape[1]
    qs, ws = _window(i, rows, width)
    allowed = _allowed(qs, ws, s0, e0, width)
    for h in range(heads):
        q = q_ref[h]
        k = k_ref[h, pl.ds(ws, width), :]
        v = v_ref[h, pl.ds(ws, width), :]
        do = do_ref[h]
        s = lax.dot_general(q, k, (((1,), (1,)), ((), ())), preferred_element_type=jnp.float32)
        s = jnp.where(allowed, s, masked_score)
        probs = jnp.exp(s - lse_ref[h])
        dp = lax.dot_general(do, v, (((1,), (1,)), ((), ())), preferred_element_type=jnp.float32)
        row_dot = jnp.sum(probs * dp, axis=1, keepdims=True)
        ds = (probs * (dp - row_dot)).astype(jnp.bfloat16)
        dq = jnp.dot(ds, k, preferred_element_type=jnp.float32)
        dq_ref[h] = dq.astype(dq_ref.dtype)
        dk_acc[h, pl.ds(ws, width), :] += jnp.dot(ds.T, q, preferred_element_type=jnp.float32)
        dv_acc[h, pl.ds(ws, width), :] += jnp.dot(
            probs.astype(jnp.bfloat16).T, do, preferred_element_type=jnp.float32
        )


def attn_bwd_kernel(starts_ref, ends_ref, q_ref, k_ref, v_ref, do_ref, lse_ref,
                    dq_ref, dk_ref, dv_ref, dk_acc, dv_acc):
    i = pl.program_id(0)
    s0 = starts_ref[i]
    e0 = ends_ref[i]
    short = i * TQ + TQ - s0 <= LMAX // 2

    @pl.when(i == 0)
    def _():
        dk_acc[...] = jnp.zeros(dk_acc.shape, dk_acc.dtype)
        dv_acc[...] = jnp.zeros(dv_acc.shape, dv_acc.dtype)

    @pl.when((s0 < e0) & short)
    def _():
        _bwd_block(i, s0, e0, q_ref, k_ref, v_ref, do_ref, lse_ref, dq_ref, dk_acc, dv_acc, LMAX // 2)

    @pl.when((s0 < e0) & jnp.logical_not(short))
    def _():
        _bwd_block(i, s0, e0, q_ref, k_ref, v_ref, do_ref, lse_ref, dq_ref, dk_acc, dv_acc, LMAX)

    @pl.when(s0 >= e0)
    def _():
        dq_ref[...] = jnp.zeros(dq_ref.shape, dq_ref.dtype)

    @pl.when(i == pl.num_programs(0) - 1)
    def _():
        dk_ref[...] = dk_acc[...].astype(dk_ref.dtype)
        dv_ref[...] = dv_acc[...].astype(dv_ref.dtype)


def attention_forward(q, k, v, starts, ends):
    heads, rows, width = q.shape
    blocks = rows // TQ
    whole = pl.BlockSpec((heads, rows, width), lambda i, s, e: (0, 0, 0))
    part = pl.BlockSpec((heads, TQ, width), lambda i, s, e: (0, i, 0))
    flops = 4 * heads * rows * LMAX * width
    return pl.pallas_call(
        attn_fwd_kernel,
        grid_spec=pltpu.PrefetchScalarGridSpec(
            num_scalar_prefetch=2,
            grid=(blocks,),
            in_specs=[part, whole, whole],
            out_specs=[part, pl.BlockSpec((heads, TQ, 1), lambda i, s, e: (0, i, 0))],
        ),
        out_shape=[
            jax.ShapeDtypeStruct((heads, rows, width), jnp.bfloat16),
            jax.ShapeDtypeStruct((heads, rows, 1), jnp.float32),
        ],
        compiler_params=pltpu.CompilerParams(
            dimension_semantics=("arbitrary",), vmem_limit_bytes=48 * 1024 * 1024
        ),
        cost_estimate=pl.CostEstimate(
            flops=flops, transcendentals=heads * rows * LMAX, bytes_accessed=4 * q.size * 2
        ),
    )(starts, ends, q, k, v)


def attention_backward(q, k, v, do, lse, starts, ends):
    heads, rows, width = q.shape
    blocks = rows // TQ
    whole = pl.BlockSpec((heads, rows, width), lambda i, s, e: (0, 0, 0))
    part = pl.BlockSpec((heads, TQ, width), lambda i, s, e: (0, i, 0))
    flops = 10 * heads * rows * LMAX * width
    return pl.pallas_call(
        attn_bwd_kernel,
        grid_spec=pltpu.PrefetchScalarGridSpec(
            num_scalar_prefetch=2,
            grid=(blocks,),
            in_specs=[part, whole, whole, part, pl.BlockSpec((heads, TQ, 1), lambda i, s, e: (0, i, 0))],
            out_specs=[part, whole, whole],
            scratch_shapes=[
                pltpu.VMEM((heads, rows, width), jnp.float32),
                pltpu.VMEM((heads, rows, width), jnp.float32),
            ],
        ),
        out_shape=[jax.ShapeDtypeStruct((heads, rows, width), jnp.bfloat16)] * 3,
        compiler_params=pltpu.CompilerParams(
            dimension_semantics=("arbitrary",), vmem_limit_bytes=48 * 1024 * 1024
        ),
        cost_estimate=pl.CostEstimate(
            flops=flops, transcendentals=heads * rows * LMAX, bytes_accessed=7 * q.size * 2
        ),
    )(starts, ends, q, k, v, do, lse)


def per_device(
    tokens,
    cotangent,
    lengths,
    dealing,
    gain_one,
    gain_two,
    attention_in,
    query_scale,
    attention_out,
    hidden_in,
    hidden_out,
):
    out_all, in_all, down_all = (
        lax.all_gather(attention_out, "mp", axis=0, tiled=True),
        lax.all_gather(hidden_in, "mp", axis=0, tiled=True),
        lax.all_gather(hidden_out, "mp", axis=0, tiled=True),
    )
    row_count = tokens.shape[0]
    mp_count = lax.axis_size("mp")
    my_group = lax.axis_index("dp")
    my_part = lax.axis_index("mp")
    group_rows = row_count * mp_count
    series_grp = group_rows // LMAX
    heads_here = NH // mp_count
    width_here = heads_here * HD
    shard_width = D // mp_count
    maps = series_maps(lengths, dealing, series_grp, group_rows, my_group)
    send_first, send_len = maps[0], maps[1]
    place_slot, place_start, place_len = dealt_places(lengths, dealing, series_grp, my_group)
    src_len = lax.dynamic_slice_in_dim(lengths, my_group * series_grp, series_grp)
    block_start, block_end, src_live = block_bounds(src_len, group_rows)
    live_mine = lax.dynamic_slice_in_dim(src_live, my_part * row_count, row_count).astype(
        jnp.float32
    )[:, None]
    gain_rows = jnp.zeros((8, D), jnp.bfloat16)
    gain_rows = gain_rows.at[0, :shard_width].set(gain_one).at[0, shard_width : 2 * shard_width].set(gain_two)
    packed = lax.all_gather(jnp.concatenate([tokens, gain_rows]), "mp", axis=0, tiled=False)
    gain_first = packed[:, row_count, :shard_width].reshape(D).astype(jnp.float32)
    gain_second = packed[:, row_count, shard_width : 2 * shard_width].reshape(D).astype(jnp.float32)
    inputs_group = packed[:, :row_count].reshape(group_rows, D).astype(jnp.float32)
    inv_group = lax.rsqrt(jnp.mean(inputs_group * inputs_group, axis=1, keepdims=True) + epsilon)
    normed_group = (inputs_group * inv_group * gain_first).astype(jnp.bfloat16)
    inputs = tokens.astype(jnp.float32)
    inv_one = lax.rsqrt(jnp.mean(inputs * inputs, axis=1, keepdims=True) + epsilon)
    weight_heads = attention_in.reshape(heads_here, HD, 3, D)
    projected = jnp.einsum(
        "rd,hecd->chre", normed_group, weight_heads, preferred_element_type=jnp.float32
    )
    dim_scale = scale_base / math.sqrt(HD) * jax.nn.softplus(query_scale)
    query_raw = projected[0]
    queries = (query_raw * dim_scale).astype(jnp.bfloat16)
    keys = projected[1].astype(jnp.bfloat16)
    values = projected[2].astype(jnp.bfloat16)
    kv_rows = jnp.stack([keys, values]).transpose(0, 2, 1, 3).reshape(2, group_rows, width_here)
    groups = lax.axis_size("dp")
    windows = send_windows(kv_rows, send_first, send_len, my_group, groups)
    received = [windows[0]] + [
        lax.ppermute(
            windows[shift], "dp", [(r, (r + shift) % groups) for r in range(groups)]
        )
        for shift in range(1, groups)
    ]
    place_shift = (my_group - place_slot) % groups
    received = jnp.stack(received)
    mixed, log_total = attention_forward(queries, keys, values, block_start, block_end)
    att_group = jnp.where(src_live[None, :, None], mixed, jnp.zeros((), jnp.bfloat16))
    att_heads = lax.all_to_all(att_group, "mp", split_axis=1, concat_axis=0, tiled=True)
    out_heads = out_all.reshape(NH, HD, D)
    branch = jnp.einsum("hie,hed->id", att_heads, out_heads, preferred_element_type=jnp.float32)
    first_sum = inputs + branch
    inv_two = lax.rsqrt(jnp.mean(first_sum * first_sum, axis=1, keepdims=True) + epsilon)
    normed_two = (first_sum * inv_two * gain_second).astype(jnp.bfloat16)
    preact = jnp.einsum("rd,fd->rf", normed_two, in_all, preferred_element_type=jnp.float32)
    hidden = jax.nn.silu(preact).astype(jnp.bfloat16)
    feed = jnp.dot(hidden, down_all, preferred_element_type=jnp.float32)
    layer_out = ((first_sum + feed) * live_mine).astype(jnp.bfloat16)
    out_grad = cotangent.astype(jnp.float32) * live_mine
    feed_grad = out_grad.astype(jnp.bfloat16)
    hidden_grad = jnp.einsum("rd,fd->rf", feed_grad, down_all, preferred_element_type=jnp.float32)
    gate_sig = jax.nn.sigmoid(preact)
    preact_grad = (hidden_grad * gate_sig * (1.0 + preact * (1.0 - gate_sig))).astype(jnp.bfloat16)
    normed_two_grad = jnp.dot(preact_grad, in_all, preferred_element_type=jnp.float32)
    scaled_two = gain_second * normed_two_grad
    first_grad = (
        out_grad
        + inv_two * scaled_two
        - first_sum * inv_two**3 * jnp.mean(scaled_two * first_sum, axis=1, keepdims=True)
    )
    branch_grad = first_grad.astype(jnp.bfloat16)
    att_heads_grad = jnp.einsum(
        "id,hed->hie", branch_grad, out_heads, preferred_element_type=jnp.float32
    ).astype(jnp.bfloat16)
    grad_group = lax.all_to_all(att_heads_grad, "mp", split_axis=0, concat_axis=1, tiled=True)
    grad_heads = jnp.where(src_live[None, :, None], grad_group, jnp.zeros((), jnp.bfloat16))
    out_part = jnp.einsum(
        "hie,id->hed", att_heads, branch_grad, preferred_element_type=jnp.float32
    ).reshape(D, D)
    in_part = jnp.einsum("ru,rd->ud", preact_grad, normed_two, preferred_element_type=jnp.float32)
    down_part = jnp.einsum("ru,rd->ud", hidden, feed_grad, preferred_element_type=jnp.float32)
    row_terms = jnp.stack([out_part, in_part, down_part], axis=1)
    shares = lax.psum_scatter(
        row_terms.astype(jnp.bfloat16), "mp", scatter_dimension=0, tiled=True
    )
    query_scaled_grad, key_grad, value_grad = attention_backward(
        queries, keys, values, grad_heads, log_total, block_start, block_end
    )
    live_heads = src_live[None, :, None]
    query_scaled_grad = jnp.where(live_heads, query_scaled_grad, jnp.zeros((), jnp.bfloat16)).astype(
        jnp.float32
    )
    query_grad = (query_scaled_grad * dim_scale).astype(jnp.bfloat16)
    proj_grad = jnp.stack(
        [
            query_grad,
            jnp.where(live_heads, key_grad, jnp.zeros((), jnp.bfloat16)),
            jnp.where(live_heads, value_grad, jnp.zeros((), jnp.bfloat16)),
        ]
    )
    qkv_part = jnp.einsum(
        "chre,rd->hecd", proj_grad, normed_group, preferred_element_type=jnp.float32
    ).reshape(width_here, 3, D)
    normed_one_part = jnp.einsum(
        "chre,hecd->rd", proj_grad, weight_heads, preferred_element_type=jnp.float32
    )
    normed_one_part, qkv_part, shares, query_raw = lax.optimization_barrier(
        (normed_one_part, qkv_part, shares, query_raw)
    )
    cache = place_slots(received, place_shift, place_start, place_len, group_rows)
    scale_part = (
        jnp.sum(query_scaled_grad * query_raw, axis=(0, 1))
        * (scale_base / math.sqrt(HD))
        * jax.nn.sigmoid(query_scale)
    )
    normed_one_grad = scatter_sum(normed_one_part.astype(jnp.bfloat16), "mp", mp_count, my_part)
    scaled_one = gain_first * normed_one_grad
    tokens_grad = (
        first_grad
        + inv_one * scaled_one
        - inputs * inv_one**3 * jnp.mean(scaled_one * inputs, axis=1, keepdims=True)
    )
    gain_one_part = jnp.sum(normed_one_part * inputs_group * inv_group, axis=0)
    gain_two_part = jnp.sum(normed_two_grad * first_sum * inv_two, axis=0)
    small = jnp.concatenate(
        [
            gain_one_part.reshape(mp_count, shard_width),
            gain_two_part.reshape(mp_count, shard_width),
            jnp.broadcast_to(scale_part, (mp_count, HD)),
        ],
        axis=1,
    )
    small = lax.psum(lax.psum_scatter(small, "mp", scatter_dimension=0, tiled=True), "dp")
    gain_one_grad = small[0, :shard_width]
    gain_two_grad = small[0, shard_width : 2 * shard_width]
    query_scale_grad = small[0, 2 * shard_width :]
    totals = lax.psum(
        jnp.concatenate([qkv_part.astype(jnp.bfloat16), shares], axis=1), "dp"
    ).astype(jnp.float32)
    return (
        layer_out,
        tokens_grad,
        cache,
        gain_one_grad,
        gain_two_grad,
        totals[:, 0:3],
        query_scale_grad,
        totals[:, 3],
        totals[:, 4],
        totals[:, 5],
    )


def solution(mesh):
    placed = (
        P(("dp", "mp"), None),
        P(("dp", "mp"), None),
        P(),
        P(),
        P("mp"),
        P("mp"),
        P("mp", None, None),
        P(),
        P("mp", None),
        P("mp", None),
        P("mp", None),
    )
    return jax.shard_map(
        per_device,
        mesh=mesh,
        in_specs=placed,
        out_specs=(
            P(("dp", "mp"), None),
            P(("dp", "mp"), None),
            P(None, "dp", "mp"),
            P("mp"),
            P("mp"),
            P("mp", None, None),
            P(),
            P("mp", None),
            P("mp", None),
            P("mp", None),
        ),
        check_vma=False,
    )
```

```python
import math

import jax
import jax.numpy as jnp
from jax import lax
from jax.experimental import pallas as pl
from jax.experimental.pallas import tpu as pltpu
from jax.sharding import PartitionSpec as P


D = 1280
NH = 16
HD = 80
LMAX = 1024
BLK = 128
TQ = 128


epsilon = 1e-06
scale_base = 1.442695041
masked_score = -1e30


def lookup(values_table, positions):
    entries = jnp.arange(values_table.shape[0], dtype=jnp.int32)
    picked = jnp.where(positions[:, None] == entries[None, :], values_table[None, :], 0)
    return jnp.sum(picked, axis=1)


def packing(span_len, group_rows):
    blocks = (span_len + BLK - 1) // BLK
    block_ends = BLK * jnp.cumsum(blocks)
    starts = block_ends - BLK * blocks
    in_group = jnp.arange(group_rows, dtype=jnp.int32)
    series_at = jnp.sum((block_ends[None, :] <= in_group[:, None]).astype(jnp.int32), axis=1)
    capped = jnp.minimum(series_at, span_len.shape[0] - 1)
    offset = in_group - lookup(starts, capped)
    live_row = (series_at < span_len.shape[0]) & (offset < lookup(span_len, capped))
    return (starts, series_at, capped, offset, live_row)


def slot_table(slot_of, starts, span_len, slot_count):
    entries = jnp.arange(slot_count, dtype=jnp.int32)
    matched = slot_of[None, :] == entries[:, None]
    slot_first = jnp.sum(jnp.where(matched, starts[None, :], 0), axis=1)
    slot_length = jnp.sum(jnp.where(matched, span_len[None, :], 0), axis=1)
    return (slot_first, slot_length)


def series_maps(lengths, dealing, series_grp, group_rows, my_group):
    groups = lengths.shape[0] // series_grp
    capacity = (series_grp + groups - 1) // groups
    places = jnp.arange(series_grp, dtype=jnp.int32)
    target = dealing.reshape(groups, series_grp) // series_grp
    earlier = (target[:, :, None] == target[:, None, :]) & (
        places[None, None, :] < places[None, :, None]
    )
    rank_of = jnp.sum(earlier.astype(jnp.int32), axis=2)
    slot_of = (target * capacity + rank_of).reshape(-1)
    rank_flat = rank_of.reshape(-1)
    src_len = lax.dynamic_slice_in_dim(lengths, my_group * series_grp, series_grp)
    src_slot = lax.dynamic_slice_in_dim(slot_of, my_group * series_grp, series_grp)
    src_starts, _, src_capped, src_offset, src_live = packing(src_len, group_rows)
    dealt_places = jnp.arange(lengths.shape[0], dtype=jnp.int32)
    owner = jnp.sum(
        jnp.where(dealing[None, :] == dealt_places[:, None], dealt_places[None, :], 0), axis=1
    )
    my_series = lax.dynamic_slice_in_dim(owner, my_group * series_grp, series_grp)
    dst_len = lookup(lengths, my_series)
    dst_slot = my_series // series_grp * capacity + lookup(rank_flat, my_series)
    dst_starts, dst_at, dst_capped, dst_offset, dst_live = packing(dst_len, group_rows)
    slot_count = groups * capacity
    send_first, send_len = slot_table(src_slot, src_starts, src_len, slot_count)
    back_first, back_len = slot_table(dst_slot, dst_starts, dst_len, slot_count)
    src_index = lookup(src_slot, src_capped) * LMAX + src_offset
    dst_index = lookup(dst_slot, dst_capped) * LMAX + dst_offset
    key_live = jnp.where(dst_at < series_grp, dst_live, True)
    return (
        send_first,
        send_len,
        back_first,
        back_len,
        src_index,
        src_live,
        dst_index,
        dst_live,
        dst_at,
        key_live,
    )


def send_windows(values, slot_first, slot_length, my_group, groups):
    padded = jnp.pad(values, ((0, 0), (0, LMAX), (0, 0)))
    positions = jnp.arange(LMAX, dtype=jnp.int32)[None, :, None]
    windows = []
    for shift in range(groups):
        target = (my_group + shift) % groups
        window = lax.dynamic_slice_in_dim(padded, slot_first[target], LMAX, axis=1)
        windows.append(
            jnp.where(positions < slot_length[target], window, jnp.zeros((), values.dtype))
        )
    return windows


def place_slots(stacked, place_shift, place_start, place_len, out_rows):
    rows = jnp.arange(out_rows, dtype=jnp.int32)[None, :, None]
    placed = jnp.zeros((stacked.shape[1], out_rows, stacked.shape[3]), stacked.dtype)
    for q in range(place_shift.shape[0]):
        window = lax.dynamic_index_in_dim(stacked, place_shift[q], axis=0, keepdims=False)
        padded = jnp.pad(window, ((0, 0), (out_rows, out_rows - LMAX), (0, 0)))
        shifted = lax.dynamic_slice_in_dim(padded, out_rows - place_start[q], out_rows, axis=1)
        inside = (rows >= place_start[q]) & (rows < place_start[q] + place_len[q])
        placed = jnp.where(inside, shifted, placed)
    return placed


def scatter_sum(partial, axis, count, me):
    size = partial.shape[0] // count
    total = lax.dynamic_slice_in_dim(partial, me * size, size, 0).astype(jnp.float32)
    for shift in range(1, count):
        piece = lax.dynamic_slice_in_dim(partial, ((me + shift) % count) * size, size, 0)
        total = total + lax.ppermute(
            piece, axis, [(r, (r + shift) % count) for r in range(count)]
        ).astype(jnp.float32)
    return total


def exchange_rows(piece_for, axis, count, me):
    received = [piece_for(me)]
    for shift in range(1, count):
        received.append(
            lax.ppermute(
                piece_for((me + shift) % count), axis, [(r, (r + shift) % count) for r in range(count)]
            )
        )
    stacked = jnp.stack(received)
    order = (me - jnp.arange(count, dtype=jnp.int32)) % count
    return jnp.take(stacked, order, axis=0)


def dealt_places(lengths, dealing, series_grp, my_group):
    dealt_places = jnp.arange(lengths.shape[0], dtype=jnp.int32)
    owner = jnp.sum(
        jnp.where(dealing[None, :] == dealt_places[:, None], dealt_places[None, :], 0), axis=1
    )
    my_series = lax.dynamic_slice_in_dim(owner, my_group * series_grp, series_grp)
    place_len = lookup(lengths, my_series)
    blocks = (place_len + BLK - 1) // BLK
    place_start = BLK * jnp.cumsum(blocks) - BLK * blocks
    return my_series // series_grp, place_start, place_len


def block_bounds(src_len, group_rows):
    starts, series_at, _, _, live_row = packing(src_len, group_rows)
    first_rows = jnp.arange(group_rows // TQ, dtype=jnp.int32) * TQ
    seg = series_at[first_rows]
    inside = seg < src_len.shape[0]
    seg_c = jnp.minimum(seg, src_len.shape[0] - 1)
    block_start = jnp.where(inside, lookup(starts, seg_c), 0)
    block_end = jnp.where(inside, block_start + lookup(src_len, seg_c), 0)
    return block_start.astype(jnp.int32), block_end.astype(jnp.int32), live_row


def _window(i, rows, width):
    qs = i * TQ
    ws = jnp.minimum(jnp.maximum(qs - (width - TQ), 0), rows - width)
    return qs, pl.multiple_of(ws, TQ)


def _allowed(qs, ws, s0, e0, width):
    a = qs + lax.broadcasted_iota(jnp.int32, (TQ, width), 0)
    b = ws + lax.broadcasted_iota(jnp.int32, (TQ, width), 1)
    return (b >= s0) & (b <= a) & (b < e0)


def _fwd_block(i, s0, e0, q_ref, k_ref, v_ref, o_ref, lse_ref, width):
    heads, rows = k_ref.shape[0], k_ref.shape[1]
    qs, ws = _window(i, rows, width)
    allowed = _allowed(qs, ws, s0, e0, width)
    for h in range(heads):
        q = q_ref[h]
        k = k_ref[h, pl.ds(ws, width), :]
        v = v_ref[h, pl.ds(ws, width), :]
        s = lax.dot_general(q, k, (((1,), (1,)), ((), ())), preferred_element_type=jnp.float32)
        s = jnp.where(allowed, s, masked_score)
        m = jnp.max(s, axis=1, keepdims=True)
        p = jnp.exp(s - m)
        l = jnp.sum(p, axis=1, keepdims=True)
        probs = (p / l).astype(jnp.bfloat16)
        o = jnp.dot(probs, v, preferred_element_type=jnp.float32)
        o_ref[h] = o.astype(o_ref.dtype)
        lse_ref[h] = m + jnp.log(l)


def attn_fwd_kernel(starts_ref, ends_ref, q_ref, k_ref, v_ref, o_ref, lse_ref):
    i = pl.program_id(0)
    s0 = starts_ref[i]
    e0 = ends_ref[i]
    short = i * TQ + TQ - s0 <= LMAX // 2

    @pl.when((s0 < e0) & short)
    def _():
        _fwd_block(i, s0, e0, q_ref, k_ref, v_ref, o_ref, lse_ref, LMAX // 2)

    @pl.when((s0 < e0) & jnp.logical_not(short))
    def _():
        _fwd_block(i, s0, e0, q_ref, k_ref, v_ref, o_ref, lse_ref, LMAX)

    @pl.when(s0 >= e0)
    def _():
        o_ref[...] = jnp.zeros(o_ref.shape, o_ref.dtype)
        lse_ref[...] = jnp.zeros(lse_ref.shape, lse_ref.dtype)


def _bwd_block(i, s0, e0, q_ref, k_ref, v_ref, do_ref, lse_ref, dq_ref, dk_acc, dv_acc, width):
    heads, rows = k_ref.shape[0], k_ref.shape[1]
    qs, ws = _window(i, rows, width)
    allowed = _allowed(qs, ws, s0, e0, width)
    for h in range(heads):
        q = q_ref[h]
        k = k_ref[h, pl.ds(ws, width), :]
        v = v_ref[h, pl.ds(ws, width), :]
        do = do_ref[h]
        s = lax.dot_general(q, k, (((1,), (1,)), ((), ())), preferred_element_type=jnp.float32)
        s = jnp.where(allowed, s, masked_score)
        probs = jnp.exp(s - lse_ref[h])
        dp = lax.dot_general(do, v, (((1,), (1,)), ((), ())), preferred_element_type=jnp.float32)
        row_dot = jnp.sum(probs * dp, axis=1, keepdims=True)
        ds = (probs * (dp - row_dot)).astype(jnp.bfloat16)
        dq = jnp.dot(ds, k, preferred_element_type=jnp.float32)
        dq_ref[h] = dq.astype(dq_ref.dtype)
        dk_acc[h, pl.ds(ws, width), :] += jnp.dot(ds.T, q, preferred_element_type=jnp.float32)
        dv_acc[h, pl.ds(ws, width), :] += jnp.dot(
            probs.astype(jnp.bfloat16).T, do, preferred_element_type=jnp.float32
        )


def attn_bwd_kernel(starts_ref, ends_ref, q_ref, k_ref, v_ref, do_ref, lse_ref,
                    dq_ref, dk_ref, dv_ref, dk_acc, dv_acc):
    i = pl.program_id(0)
    s0 = starts_ref[i]
    e0 = ends_ref[i]
    short = i * TQ + TQ - s0 <= LMAX // 2

    @pl.when(i == 0)
    def _():
        dk_acc[...] = jnp.zeros(dk_acc.shape, dk_acc.dtype)
        dv_acc[...] = jnp.zeros(dv_acc.shape, dv_acc.dtype)

    @pl.when((s0 < e0) & short)
    def _():
        _bwd_block(i, s0, e0, q_ref, k_ref, v_ref, do_ref, lse_ref, dq_ref, dk_acc, dv_acc, LMAX // 2)

    @pl.when((s0 < e0) & jnp.logical_not(short))
    def _():
        _bwd_block(i, s0, e0, q_ref, k_ref, v_ref, do_ref, lse_ref, dq_ref, dk_acc, dv_acc, LMAX)

    @pl.when(s0 >= e0)
    def _():
        dq_ref[...] = jnp.zeros(dq_ref.shape, dq_ref.dtype)

    @pl.when(i == pl.num_programs(0) - 1)
    def _():
        dk_ref[...] = dk_acc[...].astype(dk_ref.dtype)
        dv_ref[...] = dv_acc[...].astype(dv_ref.dtype)


def attention_forward(q, k, v, starts, ends):
    heads, rows, width = q.shape
    blocks = rows // TQ
    whole = pl.BlockSpec((heads, rows, width), lambda i, s, e: (0, 0, 0))
    part = pl.BlockSpec((heads, TQ, width), lambda i, s, e: (0, i, 0))
    flops = 4 * heads * rows * LMAX * width
    return pl.pallas_call(
        attn_fwd_kernel,
        grid_spec=pltpu.PrefetchScalarGridSpec(
            num_scalar_prefetch=2,
            grid=(blocks,),
            in_specs=[part, whole, whole],
            out_specs=[part, pl.BlockSpec((heads, TQ, 1), lambda i, s, e: (0, i, 0))],
        ),
        out_shape=[
            jax.ShapeDtypeStruct((heads, rows, width), jnp.bfloat16),
            jax.ShapeDtypeStruct((heads, rows, 1), jnp.float32),
        ],
        compiler_params=pltpu.CompilerParams(
            dimension_semantics=("arbitrary",), vmem_limit_bytes=48 * 1024 * 1024
        ),
        cost_estimate=pl.CostEstimate(
            flops=flops, transcendentals=heads * rows * LMAX, bytes_accessed=4 * q.size * 2
        ),
    )(starts, ends, q, k, v)


def attention_backward(q, k, v, do, lse, starts, ends):
    heads, rows, width = q.shape
    blocks = rows // TQ
    whole = pl.BlockSpec((heads, rows, width), lambda i, s, e: (0, 0, 0))
    part = pl.BlockSpec((heads, TQ, width), lambda i, s, e: (0, i, 0))
    flops = 10 * heads * rows * LMAX * width
    return pl.pallas_call(
        attn_bwd_kernel,
        grid_spec=pltpu.PrefetchScalarGridSpec(
            num_scalar_prefetch=2,
            grid=(blocks,),
            in_specs=[part, whole, whole, part, pl.BlockSpec((heads, TQ, 1), lambda i, s, e: (0, i, 0))],
            out_specs=[part, whole, whole],
            scratch_shapes=[
                pltpu.VMEM((heads, rows, width), jnp.float32),
                pltpu.VMEM((heads, rows, width), jnp.float32),
            ],
        ),
        out_shape=[jax.ShapeDtypeStruct((heads, rows, width), jnp.bfloat16)] * 3,
        compiler_params=pltpu.CompilerParams(
            dimension_semantics=("arbitrary",), vmem_limit_bytes=48 * 1024 * 1024
        ),
        cost_estimate=pl.CostEstimate(
            flops=flops, transcendentals=heads * rows * LMAX, bytes_accessed=7 * q.size * 2
        ),
    )(starts, ends, q, k, v, do, lse)


def per_device(
    tokens,
    cotangent,
    lengths,
    dealing,
    gain_one,
    gain_two,
    attention_in,
    query_scale,
    attention_out,
    hidden_in,
    hidden_out,
):
    out_all, in_all, down_all = (
        lax.all_gather(attention_out, "mp", axis=0, tiled=True),
        lax.all_gather(hidden_in, "mp", axis=0, tiled=True),
        lax.all_gather(hidden_out, "mp", axis=0, tiled=True),
    )
    row_count = tokens.shape[0]
    mp_count = lax.axis_size("mp")
    my_group = lax.axis_index("dp")
    my_part = lax.axis_index("mp")
    group_rows = row_count * mp_count
    series_grp = group_rows // LMAX
    heads_here = NH // mp_count
    width_here = heads_here * HD
    shard_width = D // mp_count
    maps = series_maps(lengths, dealing, series_grp, group_rows, my_group)
    send_first, send_len = maps[0], maps[1]
    place_slot, place_start, place_len = dealt_places(lengths, dealing, series_grp, my_group)
    src_len = lax.dynamic_slice_in_dim(lengths, my_group * series_grp, series_grp)
    block_start, block_end, src_live = block_bounds(src_len, group_rows)
    live_mine = lax.dynamic_slice_in_dim(src_live, my_part * row_count, row_count).astype(
        jnp.float32
    )[:, None]
    gain_rows = jnp.zeros((8, D), jnp.bfloat16)
    gain_rows = gain_rows.at[0, :shard_width].set(gain_one).at[0, shard_width : 2 * shard_width].set(gain_two)
    packed = lax.all_gather(jnp.concatenate([tokens, gain_rows]), "mp", axis=0, tiled=False)
    gain_first = packed[:, row_count, :shard_width].reshape(D).astype(jnp.float32)
    gain_second = packed[:, row_count, shard_width : 2 * shard_width].reshape(D).astype(jnp.float32)
    inputs_group = packed[:, :row_count].reshape(group_rows, D).astype(jnp.float32)
    inv_group = lax.rsqrt(jnp.mean(inputs_group * inputs_group, axis=1, keepdims=True) + epsilon)
    normed_group = (inputs_group * inv_group * gain_first).astype(jnp.bfloat16)
    inputs = tokens.astype(jnp.float32)
    inv_one = lax.rsqrt(jnp.mean(inputs * inputs, axis=1, keepdims=True) + epsilon)
    weight_heads = attention_in.reshape(heads_here, HD, 3, D)
    projected = jnp.einsum(
        "rd,hecd->chre", normed_group, weight_heads, preferred_element_type=jnp.float32
    )
    dim_scale = scale_base / math.sqrt(HD) * jax.nn.softplus(query_scale)
    query_raw = projected[0]
    queries = (query_raw * dim_scale).astype(jnp.bfloat16)
    keys = projected[1].astype(jnp.bfloat16)
    values = projected[2].astype(jnp.bfloat16)
    kv_rows = jnp.stack([keys, values]).transpose(0, 2, 1, 3).reshape(2, group_rows, width_here)
    groups = lax.axis_size("dp")
    windows = send_windows(kv_rows, send_first, send_len, my_group, groups)
    received = [windows[0]] + [
        lax.ppermute(
            windows[shift], "dp", [(r, (r + shift) % groups) for r in range(groups)]
        )
        for shift in range(1, groups)
    ]
    place_shift = (my_group - place_slot) % groups
    received = jnp.stack(received)
    mixed, log_total = attention_forward(queries, keys, values, block_start, block_end)
    att_group = jnp.where(src_live[None, :, None], mixed, jnp.zeros((), jnp.bfloat16))
    att_heads = lax.all_to_all(att_group, "mp", split_axis=1, concat_axis=0, tiled=True)
    out_heads = out_all.reshape(NH, HD, D)
    branch = jnp.einsum("hie,hed->id", att_heads, out_heads, preferred_element_type=jnp.float32)
    first_sum = inputs + branch
    inv_two = lax.rsqrt(jnp.mean(first_sum * first_sum, axis=1, keepdims=True) + epsilon)
    normed_two = (first_sum * inv_two * gain_second).astype(jnp.bfloat16)
    preact = jnp.einsum("rd,fd->rf", normed_two, in_all, preferred_element_type=jnp.float32)
    hidden = jax.nn.silu(preact).astype(jnp.bfloat16)
    feed = jnp.dot(hidden, down_all, preferred_element_type=jnp.float32)
    layer_out = ((first_sum + feed) * live_mine).astype(jnp.bfloat16)
    out_grad = cotangent.astype(jnp.float32) * live_mine
    feed_grad = out_grad.astype(jnp.bfloat16)
    hidden_grad = jnp.einsum("rd,fd->rf", feed_grad, down_all, preferred_element_type=jnp.float32)
    gate_sig = jax.nn.sigmoid(preact)
    preact_grad = (hidden_grad * gate_sig * (1.0 + preact * (1.0 - gate_sig))).astype(jnp.bfloat16)
    normed_two_grad = jnp.dot(preact_grad, in_all, preferred_element_type=jnp.float32)
    scaled_two = gain_second * normed_two_grad
    first_grad = (
        out_grad
        + inv_two * scaled_two
        - first_sum * inv_two**3 * jnp.mean(scaled_two * first_sum, axis=1, keepdims=True)
    )
    branch_grad = first_grad.astype(jnp.bfloat16)
    att_heads_grad = jnp.einsum(
        "id,hed->hie", branch_grad, out_heads, preferred_element_type=jnp.float32
    ).astype(jnp.bfloat16)
    grad_group = lax.all_to_all(att_heads_grad, "mp", split_axis=0, concat_axis=1, tiled=True)
    grad_heads = jnp.where(src_live[None, :, None], grad_group, jnp.zeros((), jnp.bfloat16))
    out_part = jnp.einsum(
        "hie,id->hed", att_heads, branch_grad, preferred_element_type=jnp.float32
    ).reshape(D, D)
    in_part = jnp.einsum("ru,rd->ud", preact_grad, normed_two, preferred_element_type=jnp.float32)
    down_part = jnp.einsum("ru,rd->ud", hidden, feed_grad, preferred_element_type=jnp.float32)
    row_terms = jnp.stack([out_part, in_part, down_part], axis=1)
    shares = lax.psum_scatter(
        row_terms.astype(jnp.bfloat16), "mp", scatter_dimension=0, tiled=True
    )
    query_scaled_grad, key_grad, value_grad = attention_backward(
        queries, keys, values, grad_heads, log_total, block_start, block_end
    )
    live_heads = src_live[None, :, None]
    query_scaled_grad = jnp.where(live_heads, query_scaled_grad, jnp.zeros((), jnp.bfloat16)).astype(
        jnp.float32
    )
    query_grad = (query_scaled_grad * dim_scale).astype(jnp.bfloat16)
    proj_grad = jnp.stack(
        [
            query_grad,
            jnp.where(live_heads, key_grad, jnp.zeros((), jnp.bfloat16)),
            jnp.where(live_heads, value_grad, jnp.zeros((), jnp.bfloat16)),
        ]
    )
    qkv_part = jnp.einsum(
        "chre,rd->hecd", proj_grad, normed_group, preferred_element_type=jnp.float32
    ).reshape(width_here, 3, D)
    normed_one_part = jnp.einsum(
        "chre,hecd->rd", proj_grad, weight_heads, preferred_element_type=jnp.float32
    )
    normed_one_part, qkv_part, shares, query_raw = lax.optimization_barrier(
        (normed_one_part, qkv_part, shares, query_raw)
    )
    cache = place_slots(received, place_shift, place_start, place_len, group_rows)
    scale_part = (
        jnp.sum(query_scaled_grad * query_raw, axis=(0, 1))
        * (scale_base / math.sqrt(HD))
        * jax.nn.sigmoid(query_scale)
    )
    normed_one_grad = scatter_sum(normed_one_part.astype(jnp.bfloat16), "mp", mp_count, my_part)
    scaled_one = gain_first * normed_one_grad
    tokens_grad = (
        first_grad
        + inv_one * scaled_one
        - inputs * inv_one**3 * jnp.mean(scaled_one * inputs, axis=1, keepdims=True)
    )
    gain_one_part = jnp.sum(normed_one_part * inputs_group * inv_group, axis=0)
    gain_two_part = jnp.sum(normed_two_grad * first_sum * inv_two, axis=0)
    small = jnp.concatenate(
        [
            gain_one_part.reshape(mp_count, shard_width),
            gain_two_part.reshape(mp_count, shard_width),
            jnp.broadcast_to(scale_part, (mp_count, HD)),
        ],
        axis=1,
    )
    small = jnp.sum(
        exchange_rows(lambda target: small[target], "mp", mp_count, my_part), axis=0
    )
    small = jnp.sum(
        exchange_rows(lambda target: small, "dp", lax.axis_size("dp"), my_group), axis=0
    )[None]
    gain_one_grad = small[0, :shard_width]
    gain_two_grad = small[0, shard_width : 2 * shard_width]
    query_scale_grad = small[0, 2 * shard_width :]
    totals = lax.psum(
        jnp.concatenate([qkv_part.astype(jnp.bfloat16), shares], axis=1), "dp"
    ).astype(jnp.float32)
    return (
        layer_out,
        tokens_grad,
        cache,
        gain_one_grad,
        gain_two_grad,
        totals[:, 0:3],
        query_scale_grad,
        totals[:, 3],
        totals[:, 4],
        totals[:, 5],
    )


def solution(mesh):
    placed = (
        P(("dp", "mp"), None),
        P(("dp", "mp"), None),
        P(),
        P(),
        P("mp"),
        P("mp"),
        P("mp", None, None),
        P(),
        P("mp", None),
        P("mp", None),
        P("mp", None),
    )
    return jax.shard_map(
        per_device,
        mesh=mesh,
        in_specs=placed,
        out_specs=(
            P(("dp", "mp"), None),
            P(("dp", "mp"), None),
            P(None, "dp", "mp"),
            P("mp"),
            P("mp"),
            P("mp", None, None),
            P(),
            P("mp", None),
            P("mp", None),
            P("mp", None),
        ),
        check_vma=False,
    )
```

```python
import math

import jax
import jax.numpy as jnp
from jax import lax
from jax.experimental import pallas as pl
from jax.experimental.pallas import tpu as pltpu
from jax.sharding import PartitionSpec as P


D = 1280
NH = 16
HD = 80
LMAX = 1024
BLK = 128
TQ = 128


epsilon = 1e-06
scale_base = 1.442695041
masked_score = -1e30


def lookup(values_table, positions):
    entries = jnp.arange(values_table.shape[0], dtype=jnp.int32)
    picked = jnp.where(positions[:, None] == entries[None, :], values_table[None, :], 0)
    return jnp.sum(picked, axis=1)


def packing(span_len, group_rows):
    blocks = (span_len + BLK - 1) // BLK
    block_ends = BLK * jnp.cumsum(blocks)
    starts = block_ends - BLK * blocks
    in_group = jnp.arange(group_rows, dtype=jnp.int32)
    series_at = jnp.sum((block_ends[None, :] <= in_group[:, None]).astype(jnp.int32), axis=1)
    capped = jnp.minimum(series_at, span_len.shape[0] - 1)
    offset = in_group - lookup(starts, capped)
    live_row = (series_at < span_len.shape[0]) & (offset < lookup(span_len, capped))
    return (starts, series_at, capped, offset, live_row)


def slot_table(slot_of, starts, span_len, slot_count):
    entries = jnp.arange(slot_count, dtype=jnp.int32)
    matched = slot_of[None, :] == entries[:, None]
    slot_first = jnp.sum(jnp.where(matched, starts[None, :], 0), axis=1)
    slot_length = jnp.sum(jnp.where(matched, span_len[None, :], 0), axis=1)
    return (slot_first, slot_length)


def series_maps(lengths, dealing, series_grp, group_rows, my_group):
    groups = lengths.shape[0] // series_grp
    capacity = (series_grp + groups - 1) // groups
    places = jnp.arange(series_grp, dtype=jnp.int32)
    target = dealing.reshape(groups, series_grp) // series_grp
    earlier = (target[:, :, None] == target[:, None, :]) & (
        places[None, None, :] < places[None, :, None]
    )
    rank_of = jnp.sum(earlier.astype(jnp.int32), axis=2)
    slot_of = (target * capacity + rank_of).reshape(-1)
    rank_flat = rank_of.reshape(-1)
    src_len = lax.dynamic_slice_in_dim(lengths, my_group * series_grp, series_grp)
    src_slot = lax.dynamic_slice_in_dim(slot_of, my_group * series_grp, series_grp)
    src_starts, _, src_capped, src_offset, src_live = packing(src_len, group_rows)
    dealt_places = jnp.arange(lengths.shape[0], dtype=jnp.int32)
    owner = jnp.sum(
        jnp.where(dealing[None, :] == dealt_places[:, None], dealt_places[None, :], 0), axis=1
    )
    my_series = lax.dynamic_slice_in_dim(owner, my_group * series_grp, series_grp)
    dst_len = lookup(lengths, my_series)
    dst_slot = my_series // series_grp * capacity + lookup(rank_flat, my_series)
    dst_starts, dst_at, dst_capped, dst_offset, dst_live = packing(dst_len, group_rows)
    slot_count = groups * capacity
    send_first, send_len = slot_table(src_slot, src_starts, src_len, slot_count)
    back_first, back_len = slot_table(dst_slot, dst_starts, dst_len, slot_count)
    src_index = lookup(src_slot, src_capped) * LMAX + src_offset
    dst_index = lookup(dst_slot, dst_capped) * LMAX + dst_offset
    key_live = jnp.where(dst_at < series_grp, dst_live, True)
    return (
        send_first,
        send_len,
        back_first,
        back_len,
        src_index,
        src_live,
        dst_index,
        dst_live,
        dst_at,
        key_live,
    )


def send_windows(values, slot_first, slot_length, my_group, groups):
    padded = jnp.pad(values, ((0, 0), (0, LMAX), (0, 0)))
    positions = jnp.arange(LMAX, dtype=jnp.int32)[None, :, None]
    windows = []
    for shift in range(groups):
        target = (my_group + shift) % groups
        window = lax.dynamic_slice_in_dim(padded, slot_first[target], LMAX, axis=1)
        windows.append(
            jnp.where(positions < slot_length[target], window, jnp.zeros((), values.dtype))
        )
    return windows


def place_slots(received, place_shift, place_start, place_len, out_rows):
    stacked = jnp.stack(received)
    rows = jnp.arange(out_rows, dtype=jnp.int32)[None, :, None]
    placed = jnp.zeros((stacked.shape[1], out_rows, stacked.shape[3]), stacked.dtype)
    for q in range(place_shift.shape[0]):
        window = lax.dynamic_index_in_dim(stacked, place_shift[q], axis=0, keepdims=False)
        padded = jnp.pad(window, ((0, 0), (out_rows, out_rows - LMAX), (0, 0)))
        shifted = lax.dynamic_slice_in_dim(padded, out_rows - place_start[q], out_rows, axis=1)
        inside = (rows >= place_start[q]) & (rows < place_start[q] + place_len[q])
        placed = jnp.where(inside, shifted, placed)
    return placed


def scatter_sum(partial, axis, count, me):
    size = partial.shape[0] // count
    total = lax.dynamic_slice_in_dim(partial, me * size, size, 0).astype(jnp.float32)
    for shift in range(1, count):
        piece = lax.dynamic_slice_in_dim(partial, ((me + shift) % count) * size, size, 0)
        total = total + lax.ppermute(
            piece, axis, [(r, (r + shift) % count) for r in range(count)]
        ).astype(jnp.float32)
    return total


def dealt_places(lengths, dealing, series_grp, my_group):
    dealt_places = jnp.arange(lengths.shape[0], dtype=jnp.int32)
    owner = jnp.sum(
        jnp.where(dealing[None, :] == dealt_places[:, None], dealt_places[None, :], 0), axis=1
    )
    my_series = lax.dynamic_slice_in_dim(owner, my_group * series_grp, series_grp)
    place_len = lookup(lengths, my_series)
    blocks = (place_len + BLK - 1) // BLK
    place_start = BLK * jnp.cumsum(blocks) - BLK * blocks
    return my_series // series_grp, place_start, place_len


def block_bounds(src_len, group_rows):
    starts, series_at, _, _, live_row = packing(src_len, group_rows)
    first_rows = jnp.arange(group_rows // TQ, dtype=jnp.int32) * TQ
    seg = series_at[first_rows]
    inside = seg < src_len.shape[0]
    seg_c = jnp.minimum(seg, src_len.shape[0] - 1)
    block_start = jnp.where(inside, lookup(starts, seg_c), 0)
    block_end = jnp.where(inside, block_start + lookup(src_len, seg_c), 0)
    return block_start.astype(jnp.int32), block_end.astype(jnp.int32), live_row


def _window(i, rows, width):
    qs = i * TQ
    ws = jnp.minimum(jnp.maximum(qs - (width - TQ), 0), rows - width)
    return qs, pl.multiple_of(ws, TQ)


def _allowed(qs, ws, s0, e0, width):
    a = qs + lax.broadcasted_iota(jnp.int32, (TQ, width), 0)
    b = ws + lax.broadcasted_iota(jnp.int32, (TQ, width), 1)
    return (b >= s0) & (b <= a) & (b < e0)


def _fwd_block(i, s0, e0, q_ref, k_ref, v_ref, o_ref, lse_ref, width):
    heads, rows = k_ref.shape[0], k_ref.shape[1]
    qs, ws = _window(i, rows, width)
    allowed = _allowed(qs, ws, s0, e0, width)
    for h in range(heads):
        q = q_ref[h]
        k = k_ref[h, pl.ds(ws, width), :]
        v = v_ref[h, pl.ds(ws, width), :]
        s = lax.dot_general(q, k, (((1,), (1,)), ((), ())), preferred_element_type=jnp.float32)
        s = jnp.where(allowed, s, masked_score)
        m = jnp.max(s, axis=1, keepdims=True)
        p = jnp.exp(s - m)
        l = jnp.sum(p, axis=1, keepdims=True)
        probs = (p / l).astype(jnp.bfloat16)
        o = jnp.dot(probs, v, preferred_element_type=jnp.float32)
        o_ref[h] = o.astype(o_ref.dtype)
        lse_ref[h] = m + jnp.log(l)


def attn_fwd_kernel(starts_ref, ends_ref, q_ref, k_ref, v_ref, o_ref, lse_ref):
    i = pl.program_id(0)
    s0 = starts_ref[i]
    e0 = ends_ref[i]
    short = i * TQ + TQ - s0 <= LMAX // 2

    @pl.when((s0 < e0) & short)
    def _():
        _fwd_block(i, s0, e0, q_ref, k_ref, v_ref, o_ref, lse_ref, LMAX // 2)

    @pl.when((s0 < e0) & jnp.logical_not(short))
    def _():
        _fwd_block(i, s0, e0, q_ref, k_ref, v_ref, o_ref, lse_ref, LMAX)

    @pl.when(s0 >= e0)
    def _():
        o_ref[...] = jnp.zeros(o_ref.shape, o_ref.dtype)
        lse_ref[...] = jnp.zeros(lse_ref.shape, lse_ref.dtype)


def _bwd_block(i, s0, e0, q_ref, k_ref, v_ref, do_ref, lse_ref, dq_ref, dk_acc, dv_acc, width):
    heads, rows = k_ref.shape[0], k_ref.shape[1]
    qs, ws = _window(i, rows, width)
    allowed = _allowed(qs, ws, s0, e0, width)
    for h in range(heads):
        q = q_ref[h]
        k = k_ref[h, pl.ds(ws, width), :]
        v = v_ref[h, pl.ds(ws, width), :]
        do = do_ref[h]
        s = lax.dot_general(q, k, (((1,), (1,)), ((), ())), preferred_element_type=jnp.float32)
        s = jnp.where(allowed, s, masked_score)
        probs = jnp.exp(s - lse_ref[h])
        dp = lax.dot_general(do, v, (((1,), (1,)), ((), ())), preferred_element_type=jnp.float32)
        row_dot = jnp.sum(probs * dp, axis=1, keepdims=True)
        ds = (probs * (dp - row_dot)).astype(jnp.bfloat16)
        dq = jnp.dot(ds, k, preferred_element_type=jnp.float32)
        dq_ref[h] = dq.astype(dq_ref.dtype)
        dk_acc[h, pl.ds(ws, width), :] += jnp.dot(ds.T, q, preferred_element_type=jnp.float32)
        dv_acc[h, pl.ds(ws, width), :] += jnp.dot(
            probs.astype(jnp.bfloat16).T, do, preferred_element_type=jnp.float32
        )


def attn_bwd_kernel(starts_ref, ends_ref, q_ref, k_ref, v_ref, do_ref, lse_ref,
                    dq_ref, dk_ref, dv_ref, dk_acc, dv_acc):
    i = pl.program_id(0)
    s0 = starts_ref[i]
    e0 = ends_ref[i]
    short = i * TQ + TQ - s0 <= LMAX // 2

    @pl.when(i == 0)
    def _():
        dk_acc[...] = jnp.zeros(dk_acc.shape, dk_acc.dtype)
        dv_acc[...] = jnp.zeros(dv_acc.shape, dv_acc.dtype)

    @pl.when((s0 < e0) & short)
    def _():
        _bwd_block(i, s0, e0, q_ref, k_ref, v_ref, do_ref, lse_ref, dq_ref, dk_acc, dv_acc, LMAX // 2)

    @pl.when((s0 < e0) & jnp.logical_not(short))
    def _():
        _bwd_block(i, s0, e0, q_ref, k_ref, v_ref, do_ref, lse_ref, dq_ref, dk_acc, dv_acc, LMAX)

    @pl.when(s0 >= e0)
    def _():
        dq_ref[...] = jnp.zeros(dq_ref.shape, dq_ref.dtype)

    @pl.when(i == pl.num_programs(0) - 1)
    def _():
        dk_ref[...] = dk_acc[...].astype(dk_ref.dtype)
        dv_ref[...] = dv_acc[...].astype(dv_ref.dtype)


def attention_forward(q, k, v, starts, ends):
    heads, rows, width = q.shape
    blocks = rows // TQ
    whole = pl.BlockSpec((heads, rows, width), lambda i, s, e: (0, 0, 0))
    part = pl.BlockSpec((heads, TQ, width), lambda i, s, e: (0, i, 0))
    flops = 4 * heads * rows * LMAX * width
    return pl.pallas_call(
        attn_fwd_kernel,
        grid_spec=pltpu.PrefetchScalarGridSpec(
            num_scalar_prefetch=2,
            grid=(blocks,),
            in_specs=[part, whole, whole],
            out_specs=[part, pl.BlockSpec((heads, TQ, 1), lambda i, s, e: (0, i, 0))],
        ),
        out_shape=[
            jax.ShapeDtypeStruct((heads, rows, width), jnp.bfloat16),
            jax.ShapeDtypeStruct((heads, rows, 1), jnp.float32),
        ],
        compiler_params=pltpu.CompilerParams(
            dimension_semantics=("arbitrary",), vmem_limit_bytes=48 * 1024 * 1024
        ),
        cost_estimate=pl.CostEstimate(
            flops=flops, transcendentals=heads * rows * LMAX, bytes_accessed=4 * q.size * 2
        ),
    )(starts, ends, q, k, v)


def attention_backward(q, k, v, do, lse, starts, ends):
    heads, rows, width = q.shape
    blocks = rows // TQ
    whole = pl.BlockSpec((heads, rows, width), lambda i, s, e: (0, 0, 0))
    part = pl.BlockSpec((heads, TQ, width), lambda i, s, e: (0, i, 0))
    flops = 10 * heads * rows * LMAX * width
    return pl.pallas_call(
        attn_bwd_kernel,
        grid_spec=pltpu.PrefetchScalarGridSpec(
            num_scalar_prefetch=2,
            grid=(blocks,),
            in_specs=[part, whole, whole, part, pl.BlockSpec((heads, TQ, 1), lambda i, s, e: (0, i, 0))],
            out_specs=[part, whole, whole],
            scratch_shapes=[
                pltpu.VMEM((heads, rows, width), jnp.float32),
                pltpu.VMEM((heads, rows, width), jnp.float32),
            ],
        ),
        out_shape=[jax.ShapeDtypeStruct((heads, rows, width), jnp.bfloat16)] * 3,
        compiler_params=pltpu.CompilerParams(
            dimension_semantics=("arbitrary",), vmem_limit_bytes=48 * 1024 * 1024
        ),
        cost_estimate=pl.CostEstimate(
            flops=flops, transcendentals=heads * rows * LMAX, bytes_accessed=7 * q.size * 2
        ),
    )(starts, ends, q, k, v, do, lse)


def per_device(
    tokens,
    cotangent,
    lengths,
    dealing,
    gain_one,
    gain_two,
    attention_in,
    query_scale,
    attention_out,
    hidden_in,
    hidden_out,
):
    out_all, in_all, down_all = (
        lax.all_gather(attention_out, "mp", axis=0, tiled=True),
        lax.all_gather(hidden_in, "mp", axis=0, tiled=True),
        lax.all_gather(hidden_out, "mp", axis=0, tiled=True),
    )
    row_count = tokens.shape[0]
    mp_count = lax.axis_size("mp")
    my_group = lax.axis_index("dp")
    my_part = lax.axis_index("mp")
    group_rows = row_count * mp_count
    series_grp = group_rows // LMAX
    heads_here = NH // mp_count
    width_here = heads_here * HD
    shard_width = D // mp_count
    maps = series_maps(lengths, dealing, series_grp, group_rows, my_group)
    send_first, send_len = maps[0], maps[1]
    place_slot, place_start, place_len = dealt_places(lengths, dealing, series_grp, my_group)
    src_len = lax.dynamic_slice_in_dim(lengths, my_group * series_grp, series_grp)
    block_start, block_end, src_live = block_bounds(src_len, group_rows)
    live_mine = lax.dynamic_slice_in_dim(src_live, my_part * row_count, row_count).astype(
        jnp.float32
    )[:, None]
    gain_rows = jnp.zeros((8, D), jnp.bfloat16)
    gain_rows = gain_rows.at[0, :shard_width].set(gain_one).at[0, shard_width : 2 * shard_width].set(gain_two)
    packed = lax.all_gather(jnp.concatenate([tokens, gain_rows]), "mp", axis=0, tiled=False)
    gain_first = packed[:, row_count, :shard_width].reshape(D).astype(jnp.float32)
    gain_second = packed[:, row_count, shard_width : 2 * shard_width].reshape(D).astype(jnp.float32)
    inputs_group = packed[:, :row_count].reshape(group_rows, D).astype(jnp.float32)
    inv_group = lax.rsqrt(jnp.mean(inputs_group * inputs_group, axis=1, keepdims=True) + epsilon)
    normed_group = (inputs_group * inv_group * gain_first).astype(jnp.bfloat16)
    inputs = tokens.astype(jnp.float32)
    inv_one = lax.rsqrt(jnp.mean(inputs * inputs, axis=1, keepdims=True) + epsilon)
    weight_heads = attention_in.reshape(heads_here, HD, 3, D)
    projected = jnp.einsum(
        "rd,hecd->chre", normed_group, weight_heads, preferred_element_type=jnp.float32
    )
    dim_scale = scale_base / math.sqrt(HD) * jax.nn.softplus(query_scale)
    query_raw = projected[0]
    queries = (query_raw * dim_scale).astype(jnp.bfloat16)
    keys = projected[1].astype(jnp.bfloat16)
    values = projected[2].astype(jnp.bfloat16)
    kv_rows = jnp.stack([keys, values]).transpose(0, 2, 1, 3).reshape(2, group_rows, width_here)
    groups = lax.axis_size("dp")
    windows = send_windows(kv_rows, send_first, send_len, my_group, groups)
    received = [windows[0]] + [
        lax.ppermute(
            windows[shift], "dp", [(r, (r + shift) % groups) for r in range(groups)]
        )
        for shift in range(1, groups)
    ]
    place_shift = (my_group - place_slot) % groups
    cache = place_slots(received, place_shift, place_start, place_len, group_rows)
    mixed, log_total = attention_forward(queries, keys, values, block_start, block_end)
    att_group = jnp.where(src_live[None, :, None], mixed, jnp.zeros((), jnp.bfloat16))
    att_heads = lax.all_to_all(att_group, "mp", split_axis=1, concat_axis=0, tiled=True)
    out_heads = out_all.reshape(NH, HD, D)
    branch = jnp.einsum("hie,hed->id", att_heads, out_heads, preferred_element_type=jnp.float32)
    first_sum = inputs + branch
    inv_two = lax.rsqrt(jnp.mean(first_sum * first_sum, axis=1, keepdims=True) + epsilon)
    normed_two = (first_sum * inv_two * gain_second).astype(jnp.bfloat16)
    preact = jnp.einsum("rd,fd->rf", normed_two, in_all, preferred_element_type=jnp.float32)
    hidden = jax.nn.silu(preact).astype(jnp.bfloat16)
    feed = jnp.dot(hidden, down_all, preferred_element_type=jnp.float32)
    layer_out = ((first_sum + feed) * live_mine).astype(jnp.bfloat16)
    out_grad = cotangent.astype(jnp.float32) * live_mine
    feed_grad = out_grad.astype(jnp.bfloat16)
    hidden_grad = jnp.einsum("rd,fd->rf", feed_grad, down_all, preferred_element_type=jnp.float32)
    gate_sig = jax.nn.sigmoid(preact)
    preact_grad = (hidden_grad * gate_sig * (1.0 + preact * (1.0 - gate_sig))).astype(jnp.bfloat16)
    normed_two_grad = jnp.dot(preact_grad, in_all, preferred_element_type=jnp.float32)
    scaled_two = gain_second * normed_two_grad
    first_grad = (
        out_grad
        + inv_two * scaled_two
        - first_sum * inv_two**3 * jnp.mean(scaled_two * first_sum, axis=1, keepdims=True)
    )
    branch_grad = first_grad.astype(jnp.bfloat16)
    att_heads_grad = jnp.einsum(
        "id,hed->hie", branch_grad, out_heads, preferred_element_type=jnp.float32
    ).astype(jnp.bfloat16)
    grad_group = lax.all_to_all(att_heads_grad, "mp", split_axis=0, concat_axis=1, tiled=True)
    grad_heads = jnp.where(src_live[None, :, None], grad_group, jnp.zeros((), jnp.bfloat16))
    query_scaled_grad, key_grad, value_grad = attention_backward(
        queries, keys, values, grad_heads, log_total, block_start, block_end
    )
    live_heads = src_live[None, :, None]
    query_scaled_grad = jnp.where(live_heads, query_scaled_grad, jnp.zeros((), jnp.bfloat16)).astype(
        jnp.float32
    )
    scale_part = (
        jnp.sum(query_scaled_grad * query_raw, axis=(0, 1))
        * (scale_base / math.sqrt(HD))
        * jax.nn.sigmoid(query_scale)
    )
    query_grad = (query_scaled_grad * dim_scale).astype(jnp.bfloat16)
    proj_grad = jnp.stack(
        [
            query_grad,
            jnp.where(live_heads, key_grad, jnp.zeros((), jnp.bfloat16)),
            jnp.where(live_heads, value_grad, jnp.zeros((), jnp.bfloat16)),
        ]
    )
    qkv_part = jnp.einsum(
        "chre,rd->hecd", proj_grad, normed_group, preferred_element_type=jnp.float32
    ).reshape(width_here, 3, D)
    normed_one_part = jnp.einsum(
        "chre,hecd->rd", proj_grad, weight_heads, preferred_element_type=jnp.float32
    )
    normed_one_grad = lax.psum_scatter(
        normed_one_part.astype(jnp.bfloat16), "mp", scatter_dimension=0, tiled=True
    ).astype(jnp.float32)
    scaled_one = gain_first * normed_one_grad
    tokens_grad = (
        first_grad
        + inv_one * scaled_one
        - inputs * inv_one**3 * jnp.mean(scaled_one * inputs, axis=1, keepdims=True)
    )
    gain_one_part = jnp.sum(normed_one_part * inputs_group * inv_group, axis=0)
    gain_two_part = jnp.sum(normed_two_grad * first_sum * inv_two, axis=0)
    small = jnp.concatenate(
        [
            gain_one_part.reshape(mp_count, shard_width),
            gain_two_part.reshape(mp_count, shard_width),
            jnp.broadcast_to(scale_part, (mp_count, HD)),
        ],
        axis=1,
    )
    small = lax.psum(lax.psum_scatter(small, "mp", scatter_dimension=0, tiled=True), "dp")
    gain_one_grad = small[0, :shard_width]
    gain_two_grad = small[0, shard_width : 2 * shard_width]
    query_scale_grad = small[0, 2 * shard_width :]
    out_part = jnp.einsum(
        "hie,id->hed", att_heads, branch_grad, preferred_element_type=jnp.float32
    ).reshape(D, D)
    in_part = jnp.einsum("ru,rd->ud", preact_grad, normed_two, preferred_element_type=jnp.float32)
    down_part = jnp.einsum("ru,rd->ud", hidden, feed_grad, preferred_element_type=jnp.float32)
    row_terms = jnp.stack([out_part, in_part, down_part], axis=1)
    shares = scatter_sum(row_terms.astype(jnp.bfloat16), "mp", mp_count, my_part).astype(
        jnp.bfloat16
    )
    totals = lax.psum(
        jnp.concatenate([qkv_part.astype(jnp.bfloat16), shares], axis=1), "dp"
    ).astype(jnp.float32)
    return (
        layer_out,
        tokens_grad,
        cache,
        gain_one_grad,
        gain_two_grad,
        totals[:, 0:3],
        query_scale_grad,
        totals[:, 3],
        totals[:, 4],
        totals[:, 5],
    )


def solution(mesh):
    placed = (
        P(("dp", "mp"), None),
        P(("dp", "mp"), None),
        P(),
        P(),
        P("mp"),
        P("mp"),
        P("mp", None, None),
        P(),
        P("mp", None),
        P("mp", None),
        P("mp", None),
    )
    return jax.shard_map(
        per_device,
        mesh=mesh,
        in_specs=placed,
        out_specs=(
            P(("dp", "mp"), None),
            P(("dp", "mp"), None),
            P(None, "dp", "mp"),
            P("mp"),
            P("mp"),
            P("mp", None, None),
            P(),
            P("mp", None),
            P("mp", None),
            P("mp", None),
        ),
        check_vma=False,
    )
```

```python
import math

import jax
import jax.numpy as jnp
from jax import lax
from jax.experimental import pallas as pl
from jax.experimental.pallas import tpu as pltpu
from jax.sharding import PartitionSpec as P


D = 1280
NH = 16
HD = 80
LMAX = 1024
BLK = 128
TQ = 128


epsilon = 1e-06
scale_base = 1.442695041
masked_score = -1e30


def lookup(values_table, positions):
    entries = jnp.arange(values_table.shape[0], dtype=jnp.int32)
    picked = jnp.where(positions[:, None] == entries[None, :], values_table[None, :], 0)
    return jnp.sum(picked, axis=1)


def packing(span_len, group_rows):
    blocks = (span_len + BLK - 1) // BLK
    block_ends = BLK * jnp.cumsum(blocks)
    starts = block_ends - BLK * blocks
    in_group = jnp.arange(group_rows, dtype=jnp.int32)
    series_at = jnp.sum((block_ends[None, :] <= in_group[:, None]).astype(jnp.int32), axis=1)
    capped = jnp.minimum(series_at, span_len.shape[0] - 1)
    offset = in_group - lookup(starts, capped)
    live_row = (series_at < span_len.shape[0]) & (offset < lookup(span_len, capped))
    return (starts, series_at, capped, offset, live_row)


def slot_table(slot_of, starts, span_len, slot_count):
    entries = jnp.arange(slot_count, dtype=jnp.int32)
    matched = slot_of[None, :] == entries[:, None]
    slot_first = jnp.sum(jnp.where(matched, starts[None, :], 0), axis=1)
    slot_length = jnp.sum(jnp.where(matched, span_len[None, :], 0), axis=1)
    return (slot_first, slot_length)


def series_maps(lengths, dealing, series_grp, group_rows, my_group):
    groups = lengths.shape[0] // series_grp
    capacity = (series_grp + groups - 1) // groups
    places = jnp.arange(series_grp, dtype=jnp.int32)
    target = dealing.reshape(groups, series_grp) // series_grp
    earlier = (target[:, :, None] == target[:, None, :]) & (
        places[None, None, :] < places[None, :, None]
    )
    rank_of = jnp.sum(earlier.astype(jnp.int32), axis=2)
    slot_of = (target * capacity + rank_of).reshape(-1)
    rank_flat = rank_of.reshape(-1)
    src_len = lax.dynamic_slice_in_dim(lengths, my_group * series_grp, series_grp)
    src_slot = lax.dynamic_slice_in_dim(slot_of, my_group * series_grp, series_grp)
    src_starts, _, src_capped, src_offset, src_live = packing(src_len, group_rows)
    dealt_places = jnp.arange(lengths.shape[0], dtype=jnp.int32)
    owner = jnp.sum(
        jnp.where(dealing[None, :] == dealt_places[:, None], dealt_places[None, :], 0), axis=1
    )
    my_series = lax.dynamic_slice_in_dim(owner, my_group * series_grp, series_grp)
    dst_len = lookup(lengths, my_series)
    dst_slot = my_series // series_grp * capacity + lookup(rank_flat, my_series)
    dst_starts, dst_at, dst_capped, dst_offset, dst_live = packing(dst_len, group_rows)
    slot_count = groups * capacity
    send_first, send_len = slot_table(src_slot, src_starts, src_len, slot_count)
    back_first, back_len = slot_table(dst_slot, dst_starts, dst_len, slot_count)
    src_index = lookup(src_slot, src_capped) * LMAX + src_offset
    dst_index = lookup(dst_slot, dst_capped) * LMAX + dst_offset
    key_live = jnp.where(dst_at < series_grp, dst_live, True)
    return (
        send_first,
        send_len,
        back_first,
        back_len,
        src_index,
        src_live,
        dst_index,
        dst_live,
        dst_at,
        key_live,
    )


def send_windows(values, slot_first, slot_length, my_group, groups):
    padded = jnp.pad(values, ((0, 0), (0, LMAX), (0, 0)))
    positions = jnp.arange(LMAX, dtype=jnp.int32)[None, :, None]
    windows = []
    for shift in range(groups):
        target = (my_group + shift) % groups
        window = lax.dynamic_slice_in_dim(padded, slot_first[target], LMAX, axis=1)
        windows.append(
            jnp.where(positions < slot_length[target], window, jnp.zeros((), values.dtype))
        )
    return windows


def place_slots(received, place_shift, place_start, place_len, out_rows):
    stacked = jnp.stack(received)
    rows = jnp.arange(out_rows, dtype=jnp.int32)[None, :, None]
    placed = jnp.zeros((stacked.shape[1], out_rows, stacked.shape[3]), stacked.dtype)
    for q in range(place_shift.shape[0]):
        window = lax.dynamic_index_in_dim(stacked, place_shift[q], axis=0, keepdims=False)
        padded = jnp.pad(window, ((0, 0), (out_rows, out_rows - LMAX), (0, 0)))
        shifted = lax.dynamic_slice_in_dim(padded, out_rows - place_start[q], out_rows, axis=1)
        inside = (rows >= place_start[q]) & (rows < place_start[q] + place_len[q])
        placed = jnp.where(inside, shifted, placed)
    return placed


def dealt_places(lengths, dealing, series_grp, my_group):
    dealt_places = jnp.arange(lengths.shape[0], dtype=jnp.int32)
    owner = jnp.sum(
        jnp.where(dealing[None, :] == dealt_places[:, None], dealt_places[None, :], 0), axis=1
    )
    my_series = lax.dynamic_slice_in_dim(owner, my_group * series_grp, series_grp)
    place_len = lookup(lengths, my_series)
    blocks = (place_len + BLK - 1) // BLK
    place_start = BLK * jnp.cumsum(blocks) - BLK * blocks
    return my_series // series_grp, place_start, place_len


def block_bounds(src_len, group_rows):
    starts, series_at, _, _, live_row = packing(src_len, group_rows)
    first_rows = jnp.arange(group_rows // TQ, dtype=jnp.int32) * TQ
    seg = series_at[first_rows]
    inside = seg < src_len.shape[0]
    seg_c = jnp.minimum(seg, src_len.shape[0] - 1)
    block_start = jnp.where(inside, lookup(starts, seg_c), 0)
    block_end = jnp.where(inside, block_start + lookup(src_len, seg_c), 0)
    return block_start.astype(jnp.int32), block_end.astype(jnp.int32), live_row


def _window(i, rows, width):
    qs = i * TQ
    ws = jnp.minimum(jnp.maximum(qs - (width - TQ), 0), rows - width)
    return qs, pl.multiple_of(ws, TQ)


def _allowed(qs, ws, s0, e0, width):
    a = qs + lax.broadcasted_iota(jnp.int32, (TQ, width), 0)
    b = ws + lax.broadcasted_iota(jnp.int32, (TQ, width), 1)
    return (b >= s0) & (b <= a) & (b < e0)


def _fwd_block(i, s0, e0, q_ref, k_ref, v_ref, o_ref, lse_ref, width):
    heads, rows = k_ref.shape[0], k_ref.shape[1]
    qs, ws = _window(i, rows, width)
    allowed = _allowed(qs, ws, s0, e0, width)
    for h in range(heads):
        q = q_ref[h]
        k = k_ref[h, pl.ds(ws, width), :]
        v = v_ref[h, pl.ds(ws, width), :]
        s = lax.dot_general(q, k, (((1,), (1,)), ((), ())), preferred_element_type=jnp.float32)
        s = jnp.where(allowed, s, masked_score)
        m = jnp.max(s, axis=1, keepdims=True)
        p = jnp.exp(s - m)
        l = jnp.sum(p, axis=1, keepdims=True)
        probs = (p / l).astype(jnp.bfloat16)
        o = jnp.dot(probs, v, preferred_element_type=jnp.float32)
        o_ref[h] = o.astype(o_ref.dtype)
        lse_ref[h] = m + jnp.log(l)


def attn_fwd_kernel(starts_ref, ends_ref, q_ref, k_ref, v_ref, o_ref, lse_ref):
    i = pl.program_id(0)
    s0 = starts_ref[i]
    e0 = ends_ref[i]
    short = i * TQ + TQ - s0 <= LMAX // 2

    @pl.when((s0 < e0) & short)
    def _():
        _fwd_block(i, s0, e0, q_ref, k_ref, v_ref, o_ref, lse_ref, LMAX // 2)

    @pl.when((s0 < e0) & jnp.logical_not(short))
    def _():
        _fwd_block(i, s0, e0, q_ref, k_ref, v_ref, o_ref, lse_ref, LMAX)

    @pl.when(s0 >= e0)
    def _():
        o_ref[...] = jnp.zeros(o_ref.shape, o_ref.dtype)
        lse_ref[...] = jnp.zeros(lse_ref.shape, lse_ref.dtype)


def _bwd_block(i, s0, e0, q_ref, k_ref, v_ref, do_ref, lse_ref, dq_ref, dk_acc, dv_acc, width):
    heads, rows = k_ref.shape[0], k_ref.shape[1]
    qs, ws = _window(i, rows, width)
    allowed = _allowed(qs, ws, s0, e0, width)
    for h in range(heads):
        q = q_ref[h]
        k = k_ref[h, pl.ds(ws, width), :]
        v = v_ref[h, pl.ds(ws, width), :]
        do = do_ref[h]
        s = lax.dot_general(q, k, (((1,), (1,)), ((), ())), preferred_element_type=jnp.float32)
        s = jnp.where(allowed, s, masked_score)
        probs = jnp.exp(s - lse_ref[h])
        dp = lax.dot_general(do, v, (((1,), (1,)), ((), ())), preferred_element_type=jnp.float32)
        row_dot = jnp.sum(probs * dp, axis=1, keepdims=True)
        ds = (probs * (dp - row_dot)).astype(jnp.bfloat16)
        dq = jnp.dot(ds, k, preferred_element_type=jnp.float32)
        dq_ref[h] = dq.astype(dq_ref.dtype)
        dk_acc[h, pl.ds(ws, width), :] += jnp.dot(ds.T, q, preferred_element_type=jnp.float32)
        dv_acc[h, pl.ds(ws, width), :] += jnp.dot(
            probs.astype(jnp.bfloat16).T, do, preferred_element_type=jnp.float32
        )


def attn_bwd_kernel(starts_ref, ends_ref, q_ref, k_ref, v_ref, do_ref, lse_ref,
                    dq_ref, dk_ref, dv_ref, dk_acc, dv_acc):
    i = pl.program_id(0)
    s0 = starts_ref[i]
    e0 = ends_ref[i]
    short = i * TQ + TQ - s0 <= LMAX // 2

    @pl.when(i == 0)
    def _():
        dk_acc[...] = jnp.zeros(dk_acc.shape, dk_acc.dtype)
        dv_acc[...] = jnp.zeros(dv_acc.shape, dv_acc.dtype)

    @pl.when((s0 < e0) & short)
    def _():
        _bwd_block(i, s0, e0, q_ref, k_ref, v_ref, do_ref, lse_ref, dq_ref, dk_acc, dv_acc, LMAX // 2)

    @pl.when((s0 < e0) & jnp.logical_not(short))
    def _():
        _bwd_block(i, s0, e0, q_ref, k_ref, v_ref, do_ref, lse_ref, dq_ref, dk_acc, dv_acc, LMAX)

    @pl.when(s0 >= e0)
    def _():
        dq_ref[...] = jnp.zeros(dq_ref.shape, dq_ref.dtype)

    @pl.when(i == pl.num_programs(0) - 1)
    def _():
        dk_ref[...] = dk_acc[...].astype(dk_ref.dtype)
        dv_ref[...] = dv_acc[...].astype(dv_ref.dtype)


def attention_forward(q, k, v, starts, ends):
    heads, rows, width = q.shape
    blocks = rows // TQ
    whole = pl.BlockSpec((heads, rows, width), lambda i, s, e: (0, 0, 0))
    part = pl.BlockSpec((heads, TQ, width), lambda i, s, e: (0, i, 0))
    flops = 4 * heads * rows * LMAX * width
    return pl.pallas_call(
        attn_fwd_kernel,
        grid_spec=pltpu.PrefetchScalarGridSpec(
            num_scalar_prefetch=2,
            grid=(blocks,),
            in_specs=[part, whole, whole],
            out_specs=[part, pl.BlockSpec((heads, TQ, 1), lambda i, s, e: (0, i, 0))],
        ),
        out_shape=[
            jax.ShapeDtypeStruct((heads, rows, width), jnp.bfloat16),
            jax.ShapeDtypeStruct((heads, rows, 1), jnp.float32),
        ],
        compiler_params=pltpu.CompilerParams(
            dimension_semantics=("arbitrary",), vmem_limit_bytes=48 * 1024 * 1024
        ),
        cost_estimate=pl.CostEstimate(
            flops=flops, transcendentals=heads * rows * LMAX, bytes_accessed=4 * q.size * 2
        ),
    )(starts, ends, q, k, v)


def attention_backward(q, k, v, do, lse, starts, ends):
    heads, rows, width = q.shape
    blocks = rows // TQ
    whole = pl.BlockSpec((heads, rows, width), lambda i, s, e: (0, 0, 0))
    part = pl.BlockSpec((heads, TQ, width), lambda i, s, e: (0, i, 0))
    flops = 10 * heads * rows * LMAX * width
    return pl.pallas_call(
        attn_bwd_kernel,
        grid_spec=pltpu.PrefetchScalarGridSpec(
            num_scalar_prefetch=2,
            grid=(blocks,),
            in_specs=[part, whole, whole, part, pl.BlockSpec((heads, TQ, 1), lambda i, s, e: (0, i, 0))],
            out_specs=[part, whole, whole],
            scratch_shapes=[
                pltpu.VMEM((heads, rows, width), jnp.float32),
                pltpu.VMEM((heads, rows, width), jnp.float32),
            ],
        ),
        out_shape=[jax.ShapeDtypeStruct((heads, rows, width), jnp.bfloat16)] * 3,
        compiler_params=pltpu.CompilerParams(
            dimension_semantics=("arbitrary",), vmem_limit_bytes=48 * 1024 * 1024
        ),
        cost_estimate=pl.CostEstimate(
            flops=flops, transcendentals=heads * rows * LMAX, bytes_accessed=7 * q.size * 2
        ),
    )(starts, ends, q, k, v, do, lse)


def per_device(
    tokens,
    cotangent,
    lengths,
    dealing,
    gain_one,
    gain_two,
    attention_in,
    query_scale,
    attention_out,
    hidden_in,
    hidden_out,
):
    weights_all = lax.all_gather(
        jnp.stack([attention_out, hidden_in, hidden_out]), "mp", axis=1, tiled=True
    )
    out_all, in_all, down_all = weights_all[0], weights_all[1], weights_all[2]
    row_count = tokens.shape[0]
    mp_count = lax.axis_size("mp")
    my_group = lax.axis_index("dp")
    my_part = lax.axis_index("mp")
    group_rows = row_count * mp_count
    series_grp = group_rows // LMAX
    heads_here = NH // mp_count
    width_here = heads_here * HD
    shard_width = D // mp_count
    maps = series_maps(lengths, dealing, series_grp, group_rows, my_group)
    send_first, send_len = maps[0], maps[1]
    place_slot, place_start, place_len = dealt_places(lengths, dealing, series_grp, my_group)
    src_len = lax.dynamic_slice_in_dim(lengths, my_group * series_grp, series_grp)
    block_start, block_end, src_live = block_bounds(src_len, group_rows)
    live_mine = lax.dynamic_slice_in_dim(src_live, my_part * row_count, row_count).astype(
        jnp.float32
    )[:, None]
    gain_rows = jnp.zeros((8, D), jnp.bfloat16)
    gain_rows = gain_rows.at[0, :shard_width].set(gain_one).at[0, shard_width : 2 * shard_width].set(gain_two)
    packed = lax.all_gather(jnp.concatenate([tokens, gain_rows]), "mp", axis=0, tiled=False)
    gain_first = packed[:, row_count, :shard_width].reshape(D).astype(jnp.float32)
    gain_second = packed[:, row_count, shard_width : 2 * shard_width].reshape(D).astype(jnp.float32)
    inputs_group = packed[:, :row_count].reshape(group_rows, D).astype(jnp.float32)
    inv_group = lax.rsqrt(jnp.mean(inputs_group * inputs_group, axis=1, keepdims=True) + epsilon)
    normed_group = (inputs_group * inv_group * gain_first).astype(jnp.bfloat16)
    inputs = tokens.astype(jnp.float32)
    inv_one = lax.rsqrt(jnp.mean(inputs * inputs, axis=1, keepdims=True) + epsilon)
    weight_heads = attention_in.reshape(heads_here, HD, 3, D)
    projected = jnp.einsum(
        "rd,hecd->chre", normed_group, weight_heads, preferred_element_type=jnp.float32
    )
    dim_scale = scale_base / math.sqrt(HD) * jax.nn.softplus(query_scale)
    query_raw = projected[0]
    queries = (query_raw * dim_scale).astype(jnp.bfloat16)
    keys = projected[1].astype(jnp.bfloat16)
    values = projected[2].astype(jnp.bfloat16)
    kv_rows = jnp.stack([keys, values]).transpose(0, 2, 1, 3).reshape(2, group_rows, width_here)
    groups = lax.axis_size("dp")
    windows = send_windows(kv_rows, send_first, send_len, my_group, groups)
    received = [windows[0]] + [
        lax.ppermute(
            windows[shift], "dp", [(r, (r + shift) % groups) for r in range(groups)]
        )
        for shift in range(1, groups)
    ]
    place_shift = (my_group - place_slot) % groups
    cache = place_slots(received, place_shift, place_start, place_len, group_rows)
    mixed, log_total = attention_forward(queries, keys, values, block_start, block_end)
    att_group = jnp.where(src_live[None, :, None], mixed, jnp.zeros((), jnp.bfloat16))
    att_heads = lax.all_to_all(att_group, "mp", split_axis=1, concat_axis=0, tiled=True)
    out_heads = out_all.reshape(NH, HD, D)
    branch = jnp.einsum("hie,hed->id", att_heads, out_heads, preferred_element_type=jnp.float32)
    first_sum = inputs + branch
    inv_two = lax.rsqrt(jnp.mean(first_sum * first_sum, axis=1, keepdims=True) + epsilon)
    normed_two = (first_sum * inv_two * gain_second).astype(jnp.bfloat16)
    preact = jnp.einsum("rd,fd->rf", normed_two, in_all, preferred_element_type=jnp.float32)
    hidden = jax.nn.silu(preact).astype(jnp.bfloat16)
    feed = jnp.dot(hidden, down_all, preferred_element_type=jnp.float32)
    layer_out = ((first_sum + feed) * live_mine).astype(jnp.bfloat16)
    out_grad = cotangent.astype(jnp.float32) * live_mine
    feed_grad = out_grad.astype(jnp.bfloat16)
    hidden_grad = jnp.einsum("rd,fd->rf", feed_grad, down_all, preferred_element_type=jnp.float32)
    gate_sig = jax.nn.sigmoid(preact)
    preact_grad = (hidden_grad * gate_sig * (1.0 + preact * (1.0 - gate_sig))).astype(jnp.bfloat16)
    normed_two_grad = jnp.dot(preact_grad, in_all, preferred_element_type=jnp.float32)
    scaled_two = gain_second * normed_two_grad
    first_grad = (
        out_grad
        + inv_two * scaled_two
        - first_sum * inv_two**3 * jnp.mean(scaled_two * first_sum, axis=1, keepdims=True)
    )
    branch_grad = first_grad.astype(jnp.bfloat16)
    att_heads_grad = jnp.einsum(
        "id,hed->hie", branch_grad, out_heads, preferred_element_type=jnp.float32
    ).astype(jnp.bfloat16)
    grad_group = lax.all_to_all(att_heads_grad, "mp", split_axis=0, concat_axis=1, tiled=True)
    grad_heads = jnp.where(src_live[None, :, None], grad_group, jnp.zeros((), jnp.bfloat16))
    query_scaled_grad, key_grad, value_grad = attention_backward(
        queries, keys, values, grad_heads, log_total, block_start, block_end
    )
    live_heads = src_live[None, :, None]
    query_scaled_grad = jnp.where(live_heads, query_scaled_grad, jnp.zeros((), jnp.bfloat16)).astype(
        jnp.float32
    )
    scale_part = (
        jnp.sum(query_scaled_grad * query_raw, axis=(0, 1))
        * (scale_base / math.sqrt(HD))
        * jax.nn.sigmoid(query_scale)
    )
    query_grad = (query_scaled_grad * dim_scale).astype(jnp.bfloat16)
    proj_grad = jnp.stack(
        [
            query_grad,
            jnp.where(live_heads, key_grad, jnp.zeros((), jnp.bfloat16)),
            jnp.where(live_heads, value_grad, jnp.zeros((), jnp.bfloat16)),
        ]
    )
    qkv_part = jnp.einsum(
        "chre,rd->hecd", proj_grad, normed_group, preferred_element_type=jnp.float32
    ).reshape(width_here, 3, D)
    normed_one_part = jnp.einsum(
        "chre,hecd->rd", proj_grad, weight_heads, preferred_element_type=jnp.float32
    )
    normed_one_grad = lax.psum_scatter(
        normed_one_part.astype(jnp.bfloat16), "mp", scatter_dimension=0, tiled=True
    ).astype(jnp.float32)
    scaled_one = gain_first * normed_one_grad
    tokens_grad = (
        first_grad
        + inv_one * scaled_one
        - inputs * inv_one**3 * jnp.mean(scaled_one * inputs, axis=1, keepdims=True)
    )
    gain_one_part = jnp.sum(normed_one_part * inputs_group * inv_group, axis=0)
    gain_two_part = jnp.sum(normed_two_grad * first_sum * inv_two, axis=0)
    small = jnp.concatenate(
        [
            gain_one_part.reshape(mp_count, shard_width),
            gain_two_part.reshape(mp_count, shard_width),
            jnp.broadcast_to(scale_part, (mp_count, HD)),
        ],
        axis=1,
    )
    small = lax.psum(lax.psum_scatter(small, "mp", scatter_dimension=0, tiled=True), "dp")
    gain_one_grad = small[0, :shard_width]
    gain_two_grad = small[0, shard_width : 2 * shard_width]
    query_scale_grad = small[0, 2 * shard_width :]
    out_part = jnp.einsum(
        "hie,id->hed", att_heads, branch_grad, preferred_element_type=jnp.float32
    ).reshape(D, D)
    in_part = jnp.einsum("ru,rd->ud", preact_grad, normed_two, preferred_element_type=jnp.float32)
    down_part = jnp.einsum("ru,rd->ud", hidden, feed_grad, preferred_element_type=jnp.float32)
    row_terms = jnp.stack([out_part, in_part, down_part], axis=1)
    shares = lax.psum_scatter(
        row_terms.astype(jnp.bfloat16), "mp", scatter_dimension=0, tiled=True
    )
    totals = lax.psum(
        jnp.concatenate([qkv_part.astype(jnp.bfloat16), shares], axis=1), "dp"
    ).astype(jnp.float32)
    return (
        layer_out,
        tokens_grad,
        cache,
        gain_one_grad,
        gain_two_grad,
        totals[:, 0:3],
        query_scale_grad,
        totals[:, 3],
        totals[:, 4],
        totals[:, 5],
    )


def solution(mesh):
    placed = (
        P(("dp", "mp"), None),
        P(("dp", "mp"), None),
        P(),
        P(),
        P("mp"),
        P("mp"),
        P("mp", None, None),
        P(),
        P("mp", None),
        P("mp", None),
        P("mp", None),
    )
    return jax.shard_map(
        per_device,
        mesh=mesh,
        in_specs=placed,
        out_specs=(
            P(("dp", "mp"), None),
            P(("dp", "mp"), None),
            P(None, "dp", "mp"),
            P("mp"),
            P("mp"),
            P("mp", None, None),
            P(),
            P("mp", None),
            P("mp", None),
            P("mp", None),
        ),
        check_vma=False,
    )
```
